32 devices in a mesh: tile: 2 (over y), dom: 4 (over x, core), view: 4 (over z).
Axes of the slice: x: 2, y: 2, z: 4, core: 2. Of those that a mesh axis runs over, the one named last changes fastest.
Arguments:
- estimate: float32 [128, 32, 256], P(('tile', 'dom')), parts along dimension 0, may hold values from 0.25 to 4
- observed: float32 [4, 128, 32, 256], P('view', ('tile', 'dom')), parts along dimension 1, may hold values from 0.5 to 8
- psf: float32 [4, 4, 3, 9], P('view'), may hold values from 0.02 to 1
- src_map: int32 [4, 16], replicated, may hold values from 0 to 15, as said below
- depth_band: int32 [4, 64], P('view'), may hold values from 0 to 3, as said below
Outputs:
- new_estimate: float32 [128, 32, 256], P(('tile', 'dom')), parts along dimension 0
The draws below stay inside these ranges and needn't reach their ends.
There are 2 independent parts, one for each index of `tile`. The reference program is written for one: setup_inputs(seed, part) draws one part's arguments, and reference() takes and returns one part's arrays. A program takes and returns all parts, laid end to end along the dimension named above; an argument that names none is the same for every part. Nothing has to cross between parts.
Inputs may be any that keep to these rules, and one draw needn't show every extreme that they name: For each view src_map is a permutation of the 16 joined blocks, and the 4 camera blocks f * 4 to f * 4 + 3 show blocks of 4 different depth slabs, one of each. For each view depth_band never falls along depth; it is 0 at the first plane and 3 at the last.
All inputs are finite; a program needn't handle non-finite values.
Results may differ from the reference program's by a relative error of at most 0.0001.
Values sent between devices are 32-bit elements; how exact they have to be, the bound alone decides.
No kernel may reach another device: no remote copies, remote signals or barrier semaphores. Data moves between devices by JAX's collectives and lax.ppermute only.
A program may use at most 64 MiB of HBM per device.

```python
import math
import jax
import jax.numpy as jnp
from jax import lax

X = 256
BY = 8
ZD = 16
RADIUS = 4
NBANDS = 4
TAPS = 9
VIEWS = 4
NB = 4
NBLK = 16
Y = 32
NZ = 64
N_DOM = 4


def draw_src_map(key, part):

    def one_view(view_key):
        keys = jax.random.split(view_key, 3)
        row_shift = jax.random.permutation(keys[0], NB)
        col_shift = jax.random.permutation(keys[1], NB)
        slot_shift = jax.random.randint(keys[2], (NB,), 0, NB)
        dest_pos = jnp.arange(NB, dtype=jnp.int32)[:, None]
        source_dev = (row_shift[:, None] + col_shift[None, :]) % NB
        source_slot = (dest_pos + slot_shift[source_dev]) % NB
        return (source_dev * NB + source_slot).reshape(NBLK).astype(jnp.int32)
    return jax.vmap(one_view)(jax.random.split(jax.random.fold_in(key, 11), VIEWS))


def draw_depth_band(key, part):

    def one_view(view_key):
        bounds = jax.random.randint(view_key, (NBANDS - 1,), 1, NZ)
        planes = jnp.arange(NZ, dtype=jnp.int32)
        return jnp.sum((bounds[:, None] <= planes[None, :]).astype(jnp.int32), axis=0).astype(jnp.int32)
    return jax.vmap(one_view)(jax.random.split(jax.random.fold_in(key, 23), VIEWS))


def level_of(stream_key, shape, cuts, low, largest):
    def one(dim, parts):
        steps = jax.random.uniform(jax.random.fold_in(jax.random.fold_in(stream_key, 6), dim), (parts,), jnp.float32, low / len(cuts), largest / len(cuts))
        return jnp.repeat(jnp.exp(steps), shape[dim] // parts).reshape((-1,) + (1,) * (len(shape) - dim - 1))

    factor_of = one(*cuts[0])
    for cut in cuts[1:]:
        factor_of = factor_of * one(*cut)
    return factor_of


def setup_inputs(seed: int = 0, part: int = 0) -> dict:
    splits = jax.random.split(jax.random.key(seed), 6)
    part_keys = jax.random.split(jax.random.fold_in(splits[5], part), 6)
    estimate = jnp.clip(jnp.exp(math.log(4.0) - 2.7725887 * jax.random.uniform(part_keys[0], (NZ, Y, X), jnp.float32) ** level_of(part_keys[0], (NZ, Y, X), ((0, 4),), -0.2, 0.2)), 0.25, 4.0)
    observed = jnp.clip(jnp.exp(math.log(8.0) - 2.7725887 * jax.random.uniform(part_keys[1], (VIEWS, NZ, Y, X), jnp.float32) ** level_of(part_keys[1], (VIEWS, NZ, Y, X), ((0, 4), (1, 4)), -0.2, 0.2)), 0.5, 8.0)
    psf = jnp.clip(jnp.exp(math.log(1.0) - 3.912023 * jax.random.uniform(splits[2], (VIEWS, NBANDS, 3, TAPS), jnp.float32) ** level_of(splits[2], (VIEWS, NBANDS, 3, TAPS), ((0, 4),), -0.2, 0.2)), 0.02, 1.0)
    src_map = draw_src_map(jax.random.fold_in(splits[5], 71), part)
    depth_band = draw_depth_band(jax.random.fold_in(splits[5], 71), part)
    return dict(estimate=estimate, observed=observed, psf=psf, src_map=src_map, depth_band=depth_band)


precise = lax.Precision.HIGHEST


def band_mats(kernels, length):
    in_pos = jnp.arange(length, dtype=jnp.int32)[:, None]
    out_pos = jnp.arange(length, dtype=jnp.int32)[None, :]
    tap_index = jnp.clip(in_pos - out_pos + RADIUS, 0, 2 * RADIUS)
    inside = (jnp.abs(in_pos - out_pos) <= RADIUS).astype(jnp.float32)
    return kernels[:, tap_index] * inside[None]


def to_blocks(field):
    return field.reshape(N_DOM, ZD, NB, BY, X).transpose(0, 2, 1, 3, 4).reshape(NBLK, ZD, BY, X)


def from_blocks(pieces):
    return pieces.reshape(N_DOM, NB, ZD, BY, X).transpose(0, 2, 1, 3, 4).reshape(NZ, Y, X)


def one_view(estimate, observed_view, kernels, block_map, bands):
    camera = from_blocks(to_blocks(estimate)[block_map])
    x_mats = band_mats(kernels[:, 2], X)
    y_mats = band_mats(kernels[:, 1], Y)

    def lateral_fwd(item):
        plane, band_id = item
        inner = jnp.dot(plane, x_mats[band_id], precision=precise)
        return jnp.dot(y_mats[band_id].T, inner, precision=precise)

    lateral = lax.map(lateral_fwd, (camera, bands))
    g_pos = jnp.arange(NZ, dtype=jnp.int32)[:, None]
    h_pos = jnp.arange(NZ, dtype=jnp.int32)[None, :]
    tap_index = h_pos - g_pos + RADIUS
    valid = (tap_index >= 0) & (tap_index <= 2 * RADIUS)
    depth_taps = jnp.take(kernels[:, 0], bands, axis=0)
    rows_idx = jnp.broadcast_to(g_pos, (NZ, NZ))
    depth_mat = jnp.where(valid, depth_taps[rows_idx, jnp.clip(tap_index, 0, 2 * RADIUS)], 0.0)
    blurred = jnp.einsum('gh,hyx->gyx', depth_mat, lateral, precision=precise)
    ratio_field = observed_view / blurred
    zback = jnp.einsum('gh,gyx->hyx', depth_mat, ratio_field, precision=precise)

    def lateral_back(item):
        plane, band_id = item
        inner = jnp.dot(y_mats[band_id], plane, precision=precise)
        return jnp.dot(inner, x_mats[band_id].T, precision=precise)

    back = lax.map(lateral_back, (zback, bands))
    back_blocks = to_blocks(back)
    joined_blocks = jnp.zeros_like(back_blocks).at[block_map].set(back_blocks)
    return jnp.log(from_blocks(joined_blocks))


def reference(estimate, observed, psf, src_map, depth_band):
    def step(carry, item):
        observed_view, kernels, block_map, bands = item
        return carry + one_view(estimate, observed_view, kernels, block_map, bands), None

    log_total, _ = lax.scan(step, jnp.zeros(estimate.shape, jnp.float32), (observed, psf, src_map, depth_band))
    return estimate * jnp.exp(log_total / VIEWS)
```

```python
import jax
import jax.numpy as jnp
from jax import lax
from jax.sharding import PartitionSpec as P

RADIUS = 4


precise = lax.Precision.HIGHEST


def extended_2(shard, sides, width):
    for axis, dim in sides:
        size, length = (lax.axis_size(axis), shard.shape[dim])
        up = [(i, (i + 1) % size) for i in range(size - 1)]
        down = [(j, i) for i, j in up]
        last = lax.slice_in_dim(shard, length - width, length, axis=dim)
        initial = lax.slice_in_dim(shard, 0, width, axis=dim)
        before = lax.ppermute(last, axis, up)
        after = lax.ppermute(initial, axis, down)
        shard = jnp.concatenate([before, shard, after], axis=dim)
    return shard


def line_sum(value, axis, chunks):
    size = lax.axis_size(axis)
    if size == 1:
        return value
    if size % 2:
        return lax.psum(value, axis)
    me = lax.axis_index(axis)
    half = size // 2
    pieces = jnp.split(value, chunks, axis=0)
    outs = []
    for acc in pieces:
        for r in range(1, half):
            perm = [(r - 1, r), (size - r, size - r - 1)]
            got = lax.ppermute(acc, axis, perm)
            take = (me == r) | (me == size - 1 - r)
            acc = jnp.where(take, got + acc, acc)
        got = lax.ppermute(acc, axis, [(half - 1, half), (half, half - 1)])
        take = (me == half - 1) | (me == half)
        acc = jnp.where(take, acc + got, acc)
        for r in range(1, half):
            perm = [(half - r, half - r - 1), (half - 1 + r, half + r)]
            got = lax.ppermute(acc, axis, perm)
            take = (me == half - r - 1) | (me == half + r)
            acc = jnp.where(take, got, acc)
        outs.append(acc)
    return jnp.concatenate(outs, axis=0)


def taps_along(field, taps, axis, flipped):
    tap_count = taps.shape[1]
    reach = (tap_count - 1) // 2
    length = field.shape[axis]
    widths = [(0, 0), (0, 0), (0, 0)]
    widths[axis] = (reach, reach)
    padded = jnp.pad(field, widths)
    total = jnp.zeros(field.shape, jnp.float32)
    for offset in range(tap_count):
        start = 2 * reach - offset if flipped else offset
        piece = lax.slice_in_dim(padded, start, start + length, axis=axis)
        total = total + taps[:, offset][:, None, None] * piece
    return total


def lateral_fwd(field, x_taps, y_taps):
    inner = taps_along(field, x_taps, 2, False)
    return taps_along(inner, y_taps, 1, False)


def lateral_back(field, x_taps, y_taps):
    inner = taps_along(field, y_taps, 1, True)
    return taps_along(inner, x_taps, 2, True)


def body(estimate, observed, psf, src_map, depth_band):
    plane_count, row_count, lane_count = estimate.shape
    block_count = lax.axis_size("dom")
    block_rows = row_count // block_count
    dom_index = lax.axis_index("dom")
    view_index = lax.axis_index("view")
    view_count = lax.axis_size("view")
    plane_start = dom_index * plane_count
    slot_ids = jnp.arange(block_count, dtype=jnp.int32)
    my_map = lax.dynamic_index_in_dim(src_map, view_index, 0, keepdims=False)
    grid_map = my_map.reshape(block_count, block_count)
    source_dev = grid_map // block_count
    source_slot = grid_map % block_count
    send_slot = jnp.sum(jnp.where(source_dev == dom_index, source_slot, 0), axis=1)
    blocks = estimate.reshape(plane_count, block_count, block_rows, lane_count)
    outgoing = jnp.take(blocks, send_slot, axis=1)
    arrived = lax.all_to_all(outgoing, "dom", split_axis=1, concat_axis=1, tiled=True)
    my_sources = lax.dynamic_index_in_dim(source_dev, dom_index, 0, keepdims=False)
    camera = jnp.take(arrived, my_sources, axis=1).reshape(plane_count, row_count, lane_count)
    kernels = psf[0]
    band_all = depth_band[0]
    total_planes = band_all.shape[0]
    reach = (kernels.shape[2] - 1) // 2
    ext_count = plane_count + 2 * reach
    ext_index = jnp.clip(
        plane_start - reach + jnp.arange(ext_count, dtype=jnp.int32), 0, total_planes - 1
    )
    band_ext = jnp.take(band_all, ext_index)
    band_own = lax.dynamic_slice_in_dim(band_all, plane_start, plane_count)
    x_own = jnp.take(kernels[:, 2], band_own, axis=0)
    y_own = jnp.take(kernels[:, 1], band_own, axis=0)
    lateral = lateral_fwd(camera, x_own, y_own)
    extended = extended_2(lateral, (("dom", 0),), RADIUS)
    z_pos = jnp.arange(plane_count, dtype=jnp.int32)[:, None]
    s_pos = jnp.arange(ext_count, dtype=jnp.int32)[None, :]
    fwd_tap = s_pos - z_pos
    fwd_valid = (fwd_tap >= 0) & (fwd_tap <= 2 * reach)
    taps_own = jnp.take(kernels[:, 0], band_own, axis=0)
    row_sel = jnp.broadcast_to(z_pos, (plane_count, ext_count))
    depth_fwd = jnp.where(fwd_valid, taps_own[row_sel, jnp.clip(fwd_tap, 0, 2 * reach)], 0.0)
    blurred = jnp.einsum("zs,syx->zyx", depth_fwd, extended, precision=precise)
    ratio_field = observed[0] / blurred
    ratio_ext = extended_2(ratio_field, (("dom", 0),), RADIUS)
    back_tap = z_pos - s_pos + 2 * reach
    back_valid = (back_tap >= 0) & (back_tap <= 2 * reach)
    taps_ext = jnp.take(kernels[:, 0], band_ext, axis=0)
    col_sel = jnp.broadcast_to(s_pos, (plane_count, ext_count))
    depth_back = jnp.where(back_valid, taps_ext[col_sel, jnp.clip(back_tap, 0, 2 * reach)], 0.0)
    zback = jnp.einsum("zs,syx->zyx", depth_back, ratio_ext, precision=precise)
    back = lateral_back(zback, x_own, y_own)
    dest_slot = jnp.sum(
        jnp.where(my_sources[None, :] == slot_ids[:, None], slot_ids[None, :], 0), axis=1
    )
    inverse_slot = jnp.sum(
        jnp.where(send_slot[None, :] == slot_ids[:, None], slot_ids[None, :], 0), axis=1
    )
    back_blocks = back.reshape(plane_count, block_count, block_rows, lane_count)
    returning = jnp.take(back_blocks, dest_slot, axis=1)
    returned = lax.all_to_all(returning, "dom", split_axis=1, concat_axis=1, tiled=True)
    log_corr = jnp.log(jnp.take(returned, inverse_slot, axis=1))
    log_total = line_sum(log_corr, "view", 4)
    updated = blocks * jnp.exp(log_total / view_count)
    return updated.reshape(plane_count, row_count, lane_count)


def solution(mesh):
    in_specs = (
        P(("tile", "dom"), None, None),
        P("view", ("tile", "dom"), None, None),
        P("view", None, None, None),
        P(),
        P("view", None),
    )
    out_specs = P(("tile", "dom"), None, None)
    return jax.shard_map(body, mesh=mesh, in_specs=in_specs, out_specs=out_specs, check_vma=False)
```

```python
import jax
import jax.numpy as jnp
from jax import lax
from jax.sharding import PartitionSpec as P

RADIUS = 4


precise = lax.Precision.HIGHEST


def extended_2(shard, sides, width):
    for axis, dim in sides:
        size, length = (lax.axis_size(axis), shard.shape[dim])
        up = [(i, (i + 1) % size) for i in range(size - 1)]
        down = [(j, i) for i, j in up]
        last = lax.slice_in_dim(shard, length - width, length, axis=dim)
        initial = lax.slice_in_dim(shard, 0, width, axis=dim)
        before = lax.ppermute(last, axis, up)
        after = lax.ppermute(initial, axis, down)
        shard = jnp.concatenate([before, shard, after], axis=dim)
    return shard


def line_sum(value, axis, chunks):
    size = lax.axis_size(axis)
    if size == 1:
        return value
    if size % 2:
        return lax.psum(value, axis)
    me = lax.axis_index(axis)
    half = size // 2
    acc = jnp.stack(jnp.split(value, chunks, axis=0))
    rightward = [(i, i + 1) for i in range(size - 1)]
    leftward = [(i + 1, i) for i in range(size - 1)]
    left_side = me < half

    def pick(k):
        return lax.dynamic_index_in_dim(acc, jnp.clip(k, 0, chunks - 1), 0, keepdims=False)

    def put(buf, k, new):
        valid = (k >= 0) & (k < chunks)
        kc = jnp.clip(k, 0, chunks - 1)
        old = lax.dynamic_index_in_dim(buf, kc, 0, keepdims=False)
        return lax.dynamic_update_index_in_dim(buf, jnp.where(valid, new, old), kc, 0)

    for s in range(chunks + size - 2):
        k_right = s - me
        k_left = s - (size - 1 - me)
        from_left = lax.ppermute(pick(k_right), axis, rightward)
        from_right = lax.ppermute(pick(k_left), axis, leftward)
        k_in_left = k_right + 1
        k_in_right = k_left + 1
        old_l = pick(k_in_left)
        new_l = jnp.where(left_side | (me == half), old_l + from_left, from_left)
        new_l = jnp.where(me >= 1, new_l, old_l)
        acc = put(acc, k_in_left, new_l)
        old_r = pick(k_in_right)
        new_r = jnp.where((~left_side) | (me == half - 1), old_r + from_right, from_right)
        new_r = jnp.where(me <= size - 2, new_r, old_r)
        acc = put(acc, k_in_right, new_r)
    return jnp.concatenate(list(acc), axis=0)


def taps_along(field, taps, axis, flipped):
    tap_count = taps.shape[1]
    reach = (tap_count - 1) // 2
    length = field.shape[axis]
    widths = [(0, 0), (0, 0), (0, 0)]
    widths[axis] = (reach, reach)
    padded = jnp.pad(field, widths)
    total = jnp.zeros(field.shape, jnp.float32)
    for offset in range(tap_count):
        start = 2 * reach - offset if flipped else offset
        piece = lax.slice_in_dim(padded, start, start + length, axis=axis)
        total = total + taps[:, offset][:, None, None] * piece
    return total


def lateral_fwd(field, x_taps, y_taps):
    inner = taps_along(field, x_taps, 2, False)
    return taps_along(inner, y_taps, 1, False)


def lateral_back(field, x_taps, y_taps):
    inner = taps_along(field, y_taps, 1, True)
    return taps_along(inner, x_taps, 2, True)


def body(estimate, observed, psf, src_map, depth_band):
    plane_count, row_count, lane_count = estimate.shape
    block_count = lax.axis_size("dom")
    block_rows = row_count // block_count
    dom_index = lax.axis_index("dom")
    view_index = lax.axis_index("view")
    view_count = lax.axis_size("view")
    plane_start = dom_index * plane_count
    slot_ids = jnp.arange(block_count, dtype=jnp.int32)
    my_map = lax.dynamic_index_in_dim(src_map, view_index, 0, keepdims=False)
    grid_map = my_map.reshape(block_count, block_count)
    source_dev = grid_map // block_count
    source_slot = grid_map % block_count
    send_slot = jnp.sum(jnp.where(source_dev == dom_index, source_slot, 0), axis=1)
    blocks = estimate.reshape(plane_count, block_count, block_rows, lane_count)
    outgoing = jnp.take(blocks, send_slot, axis=1)
    arrived = lax.all_to_all(outgoing, "dom", split_axis=1, concat_axis=1, tiled=True)
    my_sources = lax.dynamic_index_in_dim(source_dev, dom_index, 0, keepdims=False)
    camera = jnp.take(arrived, my_sources, axis=1).reshape(plane_count, row_count, lane_count)
    kernels = psf[0]
    band_all = depth_band[0]
    total_planes = band_all.shape[0]
    reach = (kernels.shape[2] - 1) // 2
    ext_count = plane_count + 2 * reach
    ext_index = jnp.clip(
        plane_start - reach + jnp.arange(ext_count, dtype=jnp.int32), 0, total_planes - 1
    )
    band_ext = jnp.take(band_all, ext_index)
    band_own = lax.dynamic_slice_in_dim(band_all, plane_start, plane_count)
    x_own = jnp.take(kernels[:, 2], band_own, axis=0)
    y_own = jnp.take(kernels[:, 1], band_own, axis=0)
    lateral = lateral_fwd(camera, x_own, y_own)
    extended = extended_2(lateral, (("dom", 0),), RADIUS)
    z_pos = jnp.arange(plane_count, dtype=jnp.int32)[:, None]
    s_pos = jnp.arange(ext_count, dtype=jnp.int32)[None, :]
    fwd_tap = s_pos - z_pos
    fwd_valid = (fwd_tap >= 0) & (fwd_tap <= 2 * reach)
    taps_own = jnp.take(kernels[:, 0], band_own, axis=0)
    row_sel = jnp.broadcast_to(z_pos, (plane_count, ext_count))
    depth_fwd = jnp.where(fwd_valid, taps_own[row_sel, jnp.clip(fwd_tap, 0, 2 * reach)], 0.0)
    blurred = jnp.einsum("zs,syx->zyx", depth_fwd, extended, precision=precise)
    ratio_field = observed[0] / blurred
    ratio_ext = extended_2(ratio_field, (("dom", 0),), RADIUS)
    back_tap = z_pos - s_pos + 2 * reach
    back_valid = (back_tap >= 0) & (back_tap <= 2 * reach)
    taps_ext = jnp.take(kernels[:, 0], band_ext, axis=0)
    col_sel = jnp.broadcast_to(s_pos, (plane_count, ext_count))
    depth_back = jnp.where(back_valid, taps_ext[col_sel, jnp.clip(back_tap, 0, 2 * reach)], 0.0)
    zback = jnp.einsum("zs,syx->zyx", depth_back, ratio_ext, precision=precise)
    back = lateral_back(zback, x_own, y_own)
    dest_slot = jnp.sum(
        jnp.where(my_sources[None, :] == slot_ids[:, None], slot_ids[None, :], 0), axis=1
    )
    inverse_slot = jnp.sum(
        jnp.where(send_slot[None, :] == slot_ids[:, None], slot_ids[None, :], 0), axis=1
    )
    back_blocks = back.reshape(plane_count, block_count, block_rows, lane_count)
    returning = jnp.take(back_blocks, dest_slot, axis=1)
    returned = lax.all_to_all(returning, "dom", split_axis=1, concat_axis=1, tiled=True)
    log_corr = jnp.log(jnp.take(returned, inverse_slot, axis=1))
    log_total = line_sum(log_corr, "view", 4)
    updated = blocks * jnp.exp(log_total / view_count)
    return updated.reshape(plane_count, row_count, lane_count)


def solution(mesh):
    in_specs = (
        P(("tile", "dom"), None, None),
        P("view", ("tile", "dom"), None, None),
        P("view", None, None, None),
        P(),
        P("view", None),
    )
    out_specs = P(("tile", "dom"), None, None)
    return jax.shard_map(body, mesh=mesh, in_specs=in_specs, out_specs=out_specs, check_vma=False)
```

```python
import jax
import jax.numpy as jnp
from jax import lax
from jax.sharding import PartitionSpec as P

RADIUS = 4


precise = lax.Precision.HIGHEST


def extended_2(shard, sides, width):
    for axis, dim in sides:
        size, length = (lax.axis_size(axis), shard.shape[dim])
        up = [(i, (i + 1) % size) for i in range(size - 1)]
        down = [(j, i) for i, j in up]
        last = lax.slice_in_dim(shard, length - width, length, axis=dim)
        initial = lax.slice_in_dim(shard, 0, width, axis=dim)
        before = lax.ppermute(last, axis, up)
        after = lax.ppermute(initial, axis, down)
        shard = jnp.concatenate([before, shard, after], axis=dim)
    return shard


def taps_along(field, taps, axis, flipped):
    tap_count = taps.shape[1]
    reach = (tap_count - 1) // 2
    length = field.shape[axis]
    widths = [(0, 0), (0, 0), (0, 0)]
    widths[axis] = (reach, reach)
    padded = jnp.pad(field, widths)
    total = jnp.zeros(field.shape, jnp.float32)
    for offset in range(tap_count):
        start = 2 * reach - offset if flipped else offset
        piece = lax.slice_in_dim(padded, start, start + length, axis=axis)
        total = total + taps[:, offset][:, None, None] * piece
    return total


def lateral_fwd(field, x_taps, y_taps):
    inner = taps_along(field, x_taps, 2, False)
    return taps_along(inner, y_taps, 1, False)


def lateral_back(field, x_taps, y_taps):
    inner = taps_along(field, y_taps, 1, True)
    return taps_along(inner, x_taps, 2, True)


def body(estimate, observed, psf, src_map, depth_band):
    plane_count, row_count, lane_count = estimate.shape
    block_count = lax.axis_size("dom")
    block_rows = row_count // block_count
    dom_index = lax.axis_index("dom")
    view_index = lax.axis_index("view")
    view_count = lax.axis_size("view")
    plane_start = dom_index * plane_count
    slot_ids = jnp.arange(block_count, dtype=jnp.int32)
    my_map = lax.dynamic_index_in_dim(src_map, view_index, 0, keepdims=False)
    grid_map = my_map.reshape(block_count, block_count)
    source_dev = grid_map // block_count
    source_slot = grid_map % block_count
    send_slot = jnp.sum(jnp.where(source_dev == dom_index, source_slot, 0), axis=1)
    blocks = estimate.reshape(plane_count, block_count, block_rows, lane_count)
    outgoing = jnp.take(blocks, send_slot, axis=1)
    arrived = lax.all_to_all(outgoing, "dom", split_axis=1, concat_axis=1, tiled=True)
    my_sources = lax.dynamic_index_in_dim(source_dev, dom_index, 0, keepdims=False)
    camera = jnp.take(arrived, my_sources, axis=1).reshape(plane_count, row_count, lane_count)
    kernels = psf[0]
    band_all = depth_band[0]
    total_planes = band_all.shape[0]
    reach = (kernels.shape[2] - 1) // 2
    ext_count = plane_count + 2 * reach
    ext_index = jnp.clip(
        plane_start - reach + jnp.arange(ext_count, dtype=jnp.int32), 0, total_planes - 1
    )
    band_ext = jnp.take(band_all, ext_index)
    band_own = lax.dynamic_slice_in_dim(band_all, plane_start, plane_count)
    x_own = jnp.take(kernels[:, 2], band_own, axis=0)
    y_own = jnp.take(kernels[:, 1], band_own, axis=0)
    lateral = lateral_fwd(camera, x_own, y_own)
    extended = extended_2(lateral, (("dom", 0),), RADIUS)
    z_pos = jnp.arange(plane_count, dtype=jnp.int32)[:, None]
    s_pos = jnp.arange(ext_count, dtype=jnp.int32)[None, :]
    fwd_tap = s_pos - z_pos
    fwd_valid = (fwd_tap >= 0) & (fwd_tap <= 2 * reach)
    taps_own = jnp.take(kernels[:, 0], band_own, axis=0)
    row_sel = jnp.broadcast_to(z_pos, (plane_count, ext_count))
    depth_fwd = jnp.where(fwd_valid, taps_own[row_sel, jnp.clip(fwd_tap, 0, 2 * reach)], 0.0)
    blurred = jnp.einsum("zs,syx->zyx", depth_fwd, extended, precision=precise)
    ratio_field = observed[0] / blurred
    ratio_ext = extended_2(ratio_field, (("dom", 0),), RADIUS)
    back_tap = z_pos - s_pos + 2 * reach
    back_valid = (back_tap >= 0) & (back_tap <= 2 * reach)
    taps_ext = jnp.take(kernels[:, 0], band_ext, axis=0)
    col_sel = jnp.broadcast_to(s_pos, (plane_count, ext_count))
    depth_back = jnp.where(back_valid, taps_ext[col_sel, jnp.clip(back_tap, 0, 2 * reach)], 0.0)
    zback = jnp.einsum("zs,syx->zyx", depth_back, ratio_ext, precision=precise)
    back = lateral_back(zback, x_own, y_own)
    dest_slot = jnp.sum(
        jnp.where(my_sources[None, :] == slot_ids[:, None], slot_ids[None, :], 0), axis=1
    )
    piece_rows = block_rows // view_count
    logs = jnp.log(back).reshape(plane_count, block_count, view_count, piece_rows, lane_count)
    outgoing = jnp.take(logs, dest_slot, axis=1).transpose(1, 2, 0, 3, 4)
    outgoing = outgoing.reshape(block_count * view_count, plane_count, piece_rows, lane_count)
    arrived_logs = lax.all_to_all(outgoing, ("dom", "view"), 0, 0, tiled=True)
    all_grid = src_map.reshape(view_count, block_count, block_count)
    all_dev = all_grid // block_count
    all_slot = all_grid % block_count
    slot_of = jnp.sum(jnp.where(all_dev == dom_index, all_slot, 0), axis=2)
    cam_of = jnp.sum(
        jnp.where(slot_of[:, :, None] == slot_ids[None, None, :], slot_ids[None, :, None], 0), axis=1
    )
    view_ids = jnp.arange(view_count, dtype=jnp.int32)
    flat_index = (cam_of * view_count + view_ids[:, None]).reshape(-1)
    by_view = jnp.take(arrived_logs, flat_index, axis=0)
    by_view = by_view.reshape(view_count, block_count, plane_count, piece_rows, lane_count)
    log_total = by_view[0]
    for v in range(1, view_count):
        log_total = log_total + by_view[v]
    est_rows = estimate.reshape(plane_count, block_count, view_count, piece_rows, lane_count)
    est_piece = lax.dynamic_index_in_dim(est_rows, view_index, 2, keepdims=False)
    updated = est_piece * jnp.exp(log_total.transpose(1, 0, 2, 3) / view_count)
    joined = lax.all_gather(updated, "view", axis=2, tiled=False)
    return joined.reshape(plane_count, row_count, lane_count)


def solution(mesh):
    in_specs = (
        P(("tile", "dom"), None, None),
        P("view", ("tile", "dom"), None, None),
        P("view", None, None, None),
        P(),
        P("view", None),
    )
    out_specs = P(("tile", "dom"), None, None)
    return jax.shard_map(body, mesh=mesh, in_specs=in_specs, out_specs=out_specs, check_vma=False)
```

```python
import jax
import jax.numpy as jnp
from jax import lax
from jax.sharding import PartitionSpec as P

RADIUS = 4


precise = lax.Precision.HIGHEST


def extended_2(shard, sides, width):
    for axis, dim in sides:
        size, length = (lax.axis_size(axis), shard.shape[dim])
        up = [(i, (i + 1) % size) for i in range(size - 1)]
        down = [(j, i) for i, j in up]
        last = lax.slice_in_dim(shard, length - width, length, axis=dim)
        initial = lax.slice_in_dim(shard, 0, width, axis=dim)
        before = lax.ppermute(last, axis, up)
        after = lax.ppermute(initial, axis, down)
        shard = jnp.concatenate([before, shard, after], axis=dim)
    return shard


def taps_along(field, taps, axis, flipped):
    tap_count = taps.shape[1]
    reach = (tap_count - 1) // 2
    length = field.shape[axis]
    widths = [(0, 0), (0, 0), (0, 0)]
    widths[axis] = (reach, reach)
    padded = jnp.pad(field, widths)
    total = jnp.zeros(field.shape, jnp.float32)
    for offset in range(tap_count):
        start = 2 * reach - offset if flipped else offset
        piece = lax.slice_in_dim(padded, start, start + length, axis=axis)
        total = total + taps[:, offset][:, None, None] * piece
    return total


def lateral_fwd(field, x_taps, y_taps):
    inner = taps_along(field, x_taps, 2, False)
    return taps_along(inner, y_taps, 1, False)


def lateral_back(field, x_taps, y_taps):
    inner = taps_along(field, y_taps, 1, True)
    return taps_along(inner, x_taps, 2, True)


def body(estimate, observed, psf, src_map, depth_band):
    plane_count, row_count, lane_count = estimate.shape
    block_count = lax.axis_size("dom")
    block_rows = row_count // block_count
    dom_index = lax.axis_index("dom")
    view_index = lax.axis_index("view")
    view_count = lax.axis_size("view")
    plane_start = dom_index * plane_count
    slot_ids = jnp.arange(block_count, dtype=jnp.int32)
    my_map = lax.dynamic_index_in_dim(src_map, view_index, 0, keepdims=False)
    grid_map = my_map.reshape(block_count, block_count)
    source_dev = grid_map // block_count
    source_slot = grid_map % block_count
    send_slot = jnp.sum(jnp.where(source_dev == dom_index, source_slot, 0), axis=1)
    blocks = estimate.reshape(plane_count, block_count, block_rows, lane_count)
    outgoing = jnp.take(blocks, send_slot, axis=1)
    arrived = lax.all_to_all(outgoing, "dom", split_axis=1, concat_axis=1, tiled=True)
    my_sources = lax.dynamic_index_in_dim(source_dev, dom_index, 0, keepdims=False)
    camera = jnp.take(arrived, my_sources, axis=1).reshape(plane_count, row_count, lane_count)
    kernels = psf[0]
    band_all = depth_band[0]
    total_planes = band_all.shape[0]
    reach = (kernels.shape[2] - 1) // 2
    ext_count = plane_count + 2 * reach
    ext_index = jnp.clip(
        plane_start - reach + jnp.arange(ext_count, dtype=jnp.int32), 0, total_planes - 1
    )
    band_ext = jnp.take(band_all, ext_index)
    band_own = lax.dynamic_slice_in_dim(band_all, plane_start, plane_count)
    x_own = jnp.take(kernels[:, 2], band_own, axis=0)
    y_own = jnp.take(kernels[:, 1], band_own, axis=0)
    lateral = lateral_fwd(camera, x_own, y_own)
    extended = extended_2(lateral, (("dom", 0),), RADIUS)
    taps_own = jnp.take(kernels[:, 0], band_own, axis=0)
    blurred = jnp.zeros(lateral.shape, jnp.float32)
    for j in range(2 * reach + 1):
        blurred = blurred + taps_own[:, j][:, None, None] * extended[j : j + plane_count]
    ratio_field = observed[0] / blurred
    ratio_ext = extended_2(ratio_field, (("dom", 0),), RADIUS)
    taps_ext = jnp.take(kernels[:, 0], band_ext, axis=0)
    zback = jnp.zeros(ratio_field.shape, jnp.float32)
    for m in range(2 * reach + 1):
        zback = zback + taps_ext[m : m + plane_count, 2 * reach - m][:, None, None] * ratio_ext[m : m + plane_count]
    back = lateral_back(zback, x_own, y_own)
    dest_slot = jnp.sum(
        jnp.where(my_sources[None, :] == slot_ids[:, None], slot_ids[None, :], 0), axis=1
    )
    piece_rows = block_rows // view_count
    logs = jnp.log(back).reshape(plane_count, block_count, view_count, piece_rows, lane_count)
    outgoing = jnp.take(logs, dest_slot, axis=1).transpose(1, 2, 0, 3, 4)
    outgoing = outgoing.reshape(block_count * view_count, plane_count, piece_rows, lane_count)
    arrived_logs = lax.all_to_all(outgoing, ("dom", "view"), 0, 0, tiled=True)
    all_grid = src_map.reshape(view_count, block_count, block_count)
    all_dev = all_grid // block_count
    all_slot = all_grid % block_count
    slot_of = jnp.sum(jnp.where(all_dev == dom_index, all_slot, 0), axis=2)
    cam_of = jnp.sum(
        jnp.where(slot_of[:, :, None] == slot_ids[None, None, :], slot_ids[None, :, None], 0), axis=1
    )
    view_ids = jnp.arange(view_count, dtype=jnp.int32)
    flat_index = (cam_of * view_count + view_ids[:, None]).reshape(-1)
    by_view = jnp.take(arrived_logs, flat_index, axis=0)
    by_view = by_view.reshape(view_count, block_count, plane_count, piece_rows, lane_count)
    log_total = by_view[0]
    for v in range(1, view_count):
        log_total = log_total + by_view[v]
    est_rows = estimate.reshape(plane_count, block_count, view_count, piece_rows, lane_count)
    est_piece = lax.dynamic_index_in_dim(est_rows, view_index, 2, keepdims=False)
    updated = est_piece * jnp.exp(log_total.transpose(1, 0, 2, 3) / view_count)
    joined = lax.all_gather(updated, "view", axis=2, tiled=False)
    return joined.reshape(plane_count, row_count, lane_count)


def solution(mesh):
    in_specs = (
        P(("tile", "dom"), None, None),
        P("view", ("tile", "dom"), None, None),
        P("view", None, None, None),
        P(),
        P("view", None),
    )
    out_specs = P(("tile", "dom"), None, None)
    return jax.shard_map(body, mesh=mesh, in_specs=in_specs, out_specs=out_specs, check_vma=False)
```

```python
import jax
import jax.numpy as jnp
from jax import lax
from jax.sharding import PartitionSpec as P

RADIUS = 4


precise = lax.Precision.HIGHEST


def extended_2(shard, sides, width):
    for axis, dim in sides:
        size, length = (lax.axis_size(axis), shard.shape[dim])
        up = [(i, (i + 1) % size) for i in range(size - 1)]
        down = [(j, i) for i, j in up]
        last = lax.slice_in_dim(shard, length - width, length, axis=dim)
        initial = lax.slice_in_dim(shard, 0, width, axis=dim)
        before = lax.ppermute(last, axis, up)
        after = lax.ppermute(initial, axis, down)
        shard = jnp.concatenate([before, shard, after], axis=dim)
    return shard


def taps_along(field, taps, axis, flipped):
    tap_count = taps.shape[1]
    reach = (tap_count - 1) // 2
    length = field.shape[axis]
    widths = [(0, 0), (0, 0), (0, 0)]
    widths[axis] = (reach, reach)
    padded = jnp.pad(field, widths)
    total = jnp.zeros(field.shape, jnp.float32)
    for offset in range(tap_count):
        start = 2 * reach - offset if flipped else offset
        piece = lax.slice_in_dim(padded, start, start + length, axis=axis)
        total = total + taps[:, offset][:, None, None] * piece
    return total


def lateral_fwd(field, x_taps, y_taps):
    inner = taps_along(field, x_taps, 2, False)
    return taps_along(inner, y_taps, 1, False)


def lateral_back(field, x_taps, y_taps):
    inner = taps_along(field, y_taps, 1, True)
    return taps_along(inner, x_taps, 2, True)


def body(estimate, observed, psf, src_map, depth_band):
    plane_count, row_count, lane_count = estimate.shape
    block_count = lax.axis_size("dom")
    block_rows = row_count // block_count
    dom_index = lax.axis_index("dom")
    view_index = lax.axis_index("view")
    view_count = lax.axis_size("view")
    plane_start = dom_index * plane_count
    slot_ids = jnp.arange(block_count, dtype=jnp.int32)
    my_map = lax.dynamic_index_in_dim(src_map, view_index, 0, keepdims=False)
    grid_map = my_map.reshape(block_count, block_count)
    source_dev = grid_map // block_count
    source_slot = grid_map % block_count
    send_slot = jnp.sum(jnp.where(source_dev == dom_index, source_slot, 0), axis=1)
    blocks = estimate.reshape(plane_count, block_count, block_rows, lane_count)
    outgoing = jnp.take(blocks, send_slot, axis=1)
    arrived = lax.all_to_all(outgoing, "dom", split_axis=1, concat_axis=1, tiled=True)
    my_sources = lax.dynamic_index_in_dim(source_dev, dom_index, 0, keepdims=False)
    camera = jnp.take(arrived, my_sources, axis=1).reshape(plane_count, row_count, lane_count)
    kernels = psf[0]
    band_all = depth_band[0]
    total_planes = band_all.shape[0]
    reach = (kernels.shape[2] - 1) // 2
    ext_count = plane_count + 2 * reach
    ext_index = jnp.clip(
        plane_start - reach + jnp.arange(ext_count, dtype=jnp.int32), 0, total_planes - 1
    )
    band_ext = jnp.take(band_all, ext_index)
    band_own = lax.dynamic_slice_in_dim(band_all, plane_start, plane_count)
    x_own = jnp.take(kernels[:, 2], band_own, axis=0)
    y_own = jnp.take(kernels[:, 1], band_own, axis=0)
    lateral = lateral_fwd(camera, x_own, y_own)
    extended = extended_2(lateral, (("dom", 0),), RADIUS)
    taps_own = jnp.take(kernels[:, 0], band_own, axis=0)
    blurred = jnp.zeros(lateral.shape, jnp.float32)
    for j in range(2 * reach + 1):
        blurred = blurred + taps_own[:, j][:, None, None] * extended[j : j + plane_count]
    ratio_field = observed[0] / blurred
    ratio_ext = extended_2(ratio_field, (("dom", 0),), RADIUS)
    taps_ext = jnp.take(kernels[:, 0], band_ext, axis=0)
    zback = jnp.zeros(ratio_field.shape, jnp.float32)
    for m in range(2 * reach + 1):
        zback = zback + taps_ext[m : m + plane_count, 2 * reach - m][:, None, None] * ratio_ext[m : m + plane_count]
    back = lateral_back(zback, x_own, y_own)
    dest_slot = jnp.sum(
        jnp.where(my_sources[None, :] == slot_ids[:, None], slot_ids[None, :], 0), axis=1
    )
    piece_planes = plane_count // view_count
    logs = jnp.log(back).reshape(view_count, piece_planes, block_count, block_rows, lane_count)
    outgoing = jnp.take(logs, dest_slot, axis=2).transpose(2, 0, 1, 3, 4)
    outgoing = outgoing.reshape(block_count * view_count, piece_planes, block_rows, lane_count)
    arrived_logs = lax.all_to_all(outgoing, ("dom", "view"), 0, 0, tiled=True)
    all_grid = src_map.reshape(view_count, block_count, block_count)
    all_dev = all_grid // block_count
    all_slot = all_grid % block_count
    slot_of = jnp.sum(jnp.where(all_dev == dom_index, all_slot, 0), axis=2)
    cam_of = jnp.sum(
        jnp.where(slot_of[:, :, None] == slot_ids[None, None, :], slot_ids[None, :, None], 0), axis=1
    )
    view_ids = jnp.arange(view_count, dtype=jnp.int32)
    flat_index = (cam_of * view_count + view_ids[:, None]).reshape(-1)
    by_view = jnp.take(arrived_logs, flat_index, axis=0)
    by_view = by_view.reshape(view_count, block_count, piece_planes, block_rows, lane_count)
    log_total = by_view[0]
    for v in range(1, view_count):
        log_total = log_total + by_view[v]
    log_total = log_total.transpose(1, 0, 2, 3).reshape(piece_planes, row_count, lane_count)
    est_piece = lax.dynamic_slice_in_dim(estimate, view_index * piece_planes, piece_planes, 0)
    updated = est_piece * jnp.exp(log_total / view_count)
    return lax.all_gather(updated, "view", axis=0, tiled=True)


def solution(mesh):
    in_specs = (
        P(("tile", "dom"), None, None),
        P("view", ("tile", "dom"), None, None),
        P("view", None, None, None),
        P(),
        P("view", None),
    )
    out_specs = P(("tile", "dom"), None, None)
    return jax.shard_map(body, mesh=mesh, in_specs=in_specs, out_specs=out_specs, check_vma=False)
```

```python
import jax
import jax.numpy as jnp
from jax import lax
from jax.sharding import PartitionSpec as P

RADIUS = 4


precise = lax.Precision.HIGHEST


def extended_2(shard, sides, width):
    for axis, dim in sides:
        size, length = (lax.axis_size(axis), shard.shape[dim])
        up = [(i, (i + 1) % size) for i in range(size - 1)]
        down = [(j, i) for i, j in up]
        last = lax.slice_in_dim(shard, length - width, length, axis=dim)
        initial = lax.slice_in_dim(shard, 0, width, axis=dim)
        before = lax.ppermute(last, axis, up)
        after = lax.ppermute(initial, axis, down)
        shard = jnp.concatenate([before, shard, after], axis=dim)
    return shard


def taps_along(field, taps, axis, flipped):
    tap_count = taps.shape[1]
    reach = (tap_count - 1) // 2
    length = field.shape[axis]
    widths = [(0, 0), (0, 0), (0, 0)]
    widths[axis] = (reach, reach)
    padded = jnp.pad(field, widths)
    total = jnp.zeros(field.shape, jnp.float32)
    for offset in range(tap_count):
        start = 2 * reach - offset if flipped else offset
        piece = lax.slice_in_dim(padded, start, start + length, axis=axis)
        total = total + taps[:, offset][:, None, None] * piece
    return total


def lateral_fwd(field, x_taps, y_taps):
    inner = taps_along(field, x_taps, 2, False)
    return taps_along(inner, y_taps, 1, False)


def lateral_back(field, x_taps, y_taps):
    inner = taps_along(field, y_taps, 1, True)
    return taps_along(inner, x_taps, 2, True)


def body(estimate, observed, psf, src_map, depth_band):
    plane_count, row_count, lane_count = estimate.shape
    block_count = lax.axis_size("dom")
    block_rows = row_count // block_count
    dom_index = lax.axis_index("dom")
    view_index = lax.axis_index("view")
    view_count = lax.axis_size("view")
    plane_start = dom_index * plane_count
    slot_ids = jnp.arange(block_count, dtype=jnp.int32)
    my_map = lax.dynamic_index_in_dim(src_map, view_index, 0, keepdims=False)
    grid_map = my_map.reshape(block_count, block_count)
    source_dev = grid_map // block_count
    source_slot = grid_map % block_count
    send_slot = jnp.sum(jnp.where(source_dev == dom_index, source_slot, 0), axis=1)
    blocks = estimate.reshape(plane_count, block_count, block_rows, lane_count)
    outgoing = jnp.take(blocks, send_slot, axis=1, mode="clip")
    arrived = lax.all_to_all(outgoing, "dom", split_axis=1, concat_axis=1, tiled=True)
    my_sources = lax.dynamic_index_in_dim(source_dev, dom_index, 0, keepdims=False)
    camera = jnp.take(arrived, my_sources, axis=1, mode="clip").reshape(plane_count, row_count, lane_count)
    kernels = psf[0]
    band_all = depth_band[0]
    total_planes = band_all.shape[0]
    reach = (kernels.shape[2] - 1) // 2
    ext_count = plane_count + 2 * reach
    ext_index = jnp.clip(
        plane_start - reach + jnp.arange(ext_count, dtype=jnp.int32), 0, total_planes - 1
    )
    band_ext = jnp.take(band_all, ext_index, mode="clip")
    band_own = lax.dynamic_slice_in_dim(band_all, plane_start, plane_count)
    x_own = jnp.take(kernels[:, 2], band_own, axis=0, mode="clip")
    y_own = jnp.take(kernels[:, 1], band_own, axis=0, mode="clip")
    lateral = lateral_fwd(camera, x_own, y_own)
    extended = extended_2(lateral, (("dom", 0),), RADIUS)
    taps_own = jnp.take(kernels[:, 0], band_own, axis=0, mode="clip")
    blurred = jnp.zeros(lateral.shape, jnp.float32)
    for j in range(2 * reach + 1):
        blurred = blurred + taps_own[:, j][:, None, None] * extended[j : j + plane_count]
    ratio_field = observed[0] / blurred
    ratio_ext = extended_2(ratio_field, (("dom", 0),), RADIUS)
    taps_ext = jnp.take(kernels[:, 0], band_ext, axis=0, mode="clip")
    zback = jnp.zeros(ratio_field.shape, jnp.float32)
    for m in range(2 * reach + 1):
        zback = zback + taps_ext[m : m + plane_count, 2 * reach - m][:, None, None] * ratio_ext[m : m + plane_count]
    back = lateral_back(zback, x_own, y_own)
    dest_slot = jnp.sum(
        jnp.where(my_sources[None, :] == slot_ids[:, None], slot_ids[None, :], 0), axis=1
    )
    piece_planes = plane_count // view_count
    logs = jnp.log(back).reshape(view_count, piece_planes, block_count, block_rows, lane_count)
    outgoing = jnp.take(logs, dest_slot, axis=2, mode="clip").transpose(2, 0, 1, 3, 4)
    outgoing = outgoing.reshape(block_count * view_count, piece_planes, block_rows, lane_count)
    arrived_logs = lax.all_to_all(outgoing, ("dom", "view"), 0, 0, tiled=True)
    all_grid = src_map.reshape(view_count, block_count, block_count)
    all_dev = all_grid // block_count
    all_slot = all_grid % block_count
    slot_of = jnp.sum(jnp.where(all_dev == dom_index, all_slot, 0), axis=2)
    cam_of = jnp.sum(
        jnp.where(slot_of[:, :, None] == slot_ids[None, None, :], slot_ids[None, :, None], 0), axis=1
    )
    view_ids = jnp.arange(view_count, dtype=jnp.int32)
    flat_index = (cam_of * view_count + view_ids[:, None]).reshape(-1)
    by_view = jnp.take(arrived_logs, flat_index, axis=0, mode="clip")
    by_view = by_view.reshape(view_count, block_count, piece_planes, block_rows, lane_count)
    log_total = by_view[0]
    for v in range(1, view_count):
        log_total = log_total + by_view[v]
    log_total = log_total.transpose(1, 0, 2, 3).reshape(piece_planes, row_count, lane_count)
    est_piece = lax.dynamic_slice_in_dim(estimate, view_index * piece_planes, piece_planes, 0)
    updated = est_piece * jnp.exp(log_total / view_count)
    return lax.all_gather(updated, "view", axis=0, tiled=True)


def solution(mesh):
    in_specs = (
        P(("tile", "dom"), None, None),
        P("view", ("tile", "dom"), None, None),
        P("view", None, None, None),
        P(),
        P("view", None),
    )
    out_specs = P(("tile", "dom"), None, None)
    return jax.shard_map(body, mesh=mesh, in_specs=in_specs, out_specs=out_specs, check_vma=False)
```

```python
import jax
import jax.numpy as jnp
from jax import lax
from jax.sharding import PartitionSpec as P

RADIUS = 4


precise = lax.Precision.HIGHEST


def extended_2(shard, sides, width):
    for axis, dim in sides:
        size, length = (lax.axis_size(axis), shard.shape[dim])
        up = [(i, (i + 1) % size) for i in range(size - 1)]
        down = [(j, i) for i, j in up]
        last = lax.slice_in_dim(shard, length - width, length, axis=dim)
        initial = lax.slice_in_dim(shard, 0, width, axis=dim)
        before = lax.ppermute(last, axis, up)
        after = lax.ppermute(initial, axis, down)
        shard = jnp.concatenate([before, shard, after], axis=dim)
    return shard


def taps_along(field, taps, axis, flipped):
    tap_count = taps.shape[1]
    reach = (tap_count - 1) // 2
    length = field.shape[axis]
    widths = [(0, 0), (0, 0), (0, 0)]
    widths[axis] = (reach, reach)
    padded = jnp.pad(field, widths)
    total = jnp.zeros(field.shape, jnp.float32)
    for offset in range(tap_count):
        start = 2 * reach - offset if flipped else offset
        piece = lax.slice_in_dim(padded, start, start + length, axis=axis)
        total = total + taps[:, offset][:, None, None] * piece
    return total


def lateral_fwd(field, x_taps, y_taps):
    inner = taps_along(field, x_taps, 2, False)
    return taps_along(inner, y_taps, 1, False)


def lateral_back(field, x_taps, y_taps):
    inner = taps_along(field, y_taps, 1, True)
    return taps_along(inner, x_taps, 2, True)


def body(estimate, observed, psf, src_map, depth_band):
    plane_count, row_count, lane_count = estimate.shape
    block_count = lax.axis_size("dom")
    block_rows = row_count // block_count
    dom_index = lax.axis_index("dom")
    view_index = lax.axis_index("view")
    view_count = lax.axis_size("view")
    plane_start = dom_index * plane_count
    slot_ids = jnp.arange(block_count, dtype=jnp.int32)
    my_map = lax.dynamic_index_in_dim(src_map, view_index, 0, keepdims=False)
    grid_map = my_map.reshape(block_count, block_count)
    source_dev = grid_map // block_count
    source_slot = grid_map % block_count
    send_slot = jnp.sum(jnp.where(source_dev == dom_index, source_slot, 0), axis=1)
    blocks = estimate.reshape(plane_count, block_count, block_rows, lane_count)
    kernels = psf[0]
    band_all = depth_band[0]
    total_planes = band_all.shape[0]
    reach = (kernels.shape[2] - 1) // 2
    wide = 2 * reach
    last = block_count - 1
    above = jnp.take(send_slot, jnp.clip(slot_ids - 1, 0, last), mode="clip")
    below = jnp.take(send_slot, jnp.clip(slot_ids + 1, 0, last), mode="clip")
    outgoing = jnp.concatenate(
        [
            jnp.take(blocks[plane_count - wide :], above, axis=1, mode="clip"),
            jnp.take(blocks, send_slot, axis=1, mode="clip"),
            jnp.take(blocks[:wide], below, axis=1, mode="clip"),
        ],
        axis=0,
    )
    arrived = lax.all_to_all(outgoing, "dom", split_axis=1, concat_axis=1, tiled=True)
    my_sources = lax.dynamic_index_in_dim(source_dev, dom_index, 0, keepdims=False)
    src_above = lax.dynamic_index_in_dim(source_dev, jnp.maximum(dom_index - 1, 0), 0, keepdims=False)
    src_below = lax.dynamic_index_in_dim(source_dev, jnp.minimum(dom_index + 1, last), 0, keepdims=False)
    camera_ext = jnp.concatenate(
        [
            jnp.take(arrived[:wide], src_above, axis=1, mode="clip"),
            jnp.take(arrived[wide : wide + plane_count], my_sources, axis=1, mode="clip"),
            jnp.take(arrived[wide + plane_count :], src_below, axis=1, mode="clip"),
        ],
        axis=0,
    )
    wide_count = plane_count + 2 * wide
    wide_planes = plane_start - wide + jnp.arange(wide_count, dtype=jnp.int32)
    wide_inside = (wide_planes >= 0) & (wide_planes < total_planes)
    camera_ext = jnp.where(wide_inside[:, None, None, None], camera_ext, 0.0)
    camera_ext = camera_ext.reshape(wide_count, row_count, lane_count)
    band_wide = jnp.take(band_all, jnp.clip(wide_planes, 0, total_planes - 1), mode="clip")
    x_wide = jnp.take(kernels[:, 2], band_wide, axis=0, mode="clip")
    y_wide = jnp.take(kernels[:, 1], band_wide, axis=0, mode="clip")
    lateral_ext = lateral_fwd(camera_ext, x_wide, y_wide)
    ext_count = plane_count + 2 * reach
    ext_planes = plane_start - reach + jnp.arange(ext_count, dtype=jnp.int32)
    ext_inside = (ext_planes >= 0) & (ext_planes < total_planes)
    band_ext = jnp.take(band_all, jnp.clip(ext_planes, 0, total_planes - 1), mode="clip")
    taps_ext = jnp.take(kernels[:, 0], band_ext, axis=0, mode="clip")
    blurred = jnp.zeros((ext_count, row_count, lane_count), jnp.float32)
    for j in range(2 * reach + 1):
        blurred = blurred + taps_ext[:, j][:, None, None] * lateral_ext[j : j + ext_count]
    observed_ext = extended_2(observed[0], (("dom", 0),), reach)
    ratio_ext = jnp.where(ext_inside[:, None, None], observed_ext / blurred, 0.0)
    band_own = lax.dynamic_slice_in_dim(band_all, plane_start, plane_count)
    x_own = jnp.take(kernels[:, 2], band_own, axis=0, mode="clip")
    y_own = jnp.take(kernels[:, 1], band_own, axis=0, mode="clip")
    zback = jnp.zeros((plane_count, row_count, lane_count), jnp.float32)
    for m in range(2 * reach + 1):
        zback = zback + taps_ext[m : m + plane_count, 2 * reach - m][:, None, None] * ratio_ext[m : m + plane_count]
    back = lateral_back(zback, x_own, y_own)
    dest_slot = jnp.sum(
        jnp.where(my_sources[None, :] == slot_ids[:, None], slot_ids[None, :], 0), axis=1
    )
    piece_planes = plane_count // view_count
    logs = jnp.log(back).reshape(view_count, piece_planes, block_count, block_rows, lane_count)
    outgoing = jnp.take(logs, dest_slot, axis=2, mode="clip").transpose(2, 0, 1, 3, 4)
    outgoing = outgoing.reshape(block_count * view_count, piece_planes, block_rows, lane_count)
    arrived_logs = lax.all_to_all(outgoing, ("dom", "view"), 0, 0, tiled=True)
    all_grid = src_map.reshape(view_count, block_count, block_count)
    all_dev = all_grid // block_count
    all_slot = all_grid % block_count
    slot_of = jnp.sum(jnp.where(all_dev == dom_index, all_slot, 0), axis=2)
    cam_of = jnp.sum(
        jnp.where(slot_of[:, :, None] == slot_ids[None, None, :], slot_ids[None, :, None], 0), axis=1
    )
    view_ids = jnp.arange(view_count, dtype=jnp.int32)
    flat_index = (cam_of * view_count + view_ids[:, None]).reshape(-1)
    by_view = jnp.take(arrived_logs, flat_index, axis=0, mode="clip")
    by_view = by_view.reshape(view_count, block_count, piece_planes, block_rows, lane_count)
    log_total = by_view[0]
    for v in range(1, view_count):
        log_total = log_total + by_view[v]
    log_total = log_total.transpose(1, 0, 2, 3).reshape(piece_planes, row_count, lane_count)
    est_piece = lax.dynamic_slice_in_dim(estimate, view_index * piece_planes, piece_planes, 0)
    updated = est_piece * jnp.exp(log_total / view_count)
    return lax.all_gather(updated, "view", axis=0, tiled=True)


def solution(mesh):
    in_specs = (
        P(("tile", "dom"), None, None),
        P("view", ("tile", "dom"), None, None),
        P("view", None, None, None),
        P(),
        P("view", None),
    )
    out_specs = P(("tile", "dom"), None, None)
    return jax.shard_map(body, mesh=mesh, in_specs=in_specs, out_specs=out_specs, check_vma=False)
```

```python
import jax
import jax.numpy as jnp
from jax import lax
from jax.sharding import PartitionSpec as P

RADIUS = 4


precise = lax.Precision.HIGHEST


def extended_2(shard, sides, width):
    for axis, dim in sides:
        size, length = (lax.axis_size(axis), shard.shape[dim])
        up = [(i, (i + 1) % size) for i in range(size - 1)]
        down = [(j, i) for i, j in up]
        last = lax.slice_in_dim(shard, length - width, length, axis=dim)
        initial = lax.slice_in_dim(shard, 0, width, axis=dim)
        before = lax.ppermute(last, axis, up)
        after = lax.ppermute(initial, axis, down)
        shard = jnp.concatenate([before, shard, after], axis=dim)
    return shard


def taps_along(field, taps, axis, flipped):
    tap_count = taps.shape[1]
    reach = (tap_count - 1) // 2
    length = field.shape[axis]
    widths = [(0, 0), (0, 0), (0, 0)]
    widths[axis] = (reach, reach)
    padded = jnp.pad(field, widths)
    total = jnp.zeros(field.shape, jnp.float32)
    for offset in range(tap_count):
        start = 2 * reach - offset if flipped else offset
        piece = lax.slice_in_dim(padded, start, start + length, axis=axis)
        total = total + taps[:, offset][:, None, None] * piece
    return total


def lateral_fwd(field, x_taps, y_taps):
    inner = taps_along(field, x_taps, 2, False)
    return taps_along(inner, y_taps, 1, False)


def lateral_back(field, x_taps, y_taps):
    inner = taps_along(field, y_taps, 1, True)
    return taps_along(inner, x_taps, 2, True)


def body(estimate, observed, psf, src_map, depth_band):
    plane_count, row_count, lane_count = estimate.shape
    block_count = lax.axis_size("dom")
    block_rows = row_count // block_count
    dom_index = lax.axis_index("dom")
    view_index = lax.axis_index("view")
    view_count = lax.axis_size("view")
    plane_start = dom_index * plane_count
    slot_ids = jnp.arange(block_count, dtype=jnp.int32)
    my_map = lax.dynamic_index_in_dim(src_map, view_index, 0, keepdims=False)
    grid_map = my_map.reshape(block_count, block_count)
    source_dev = grid_map // block_count
    source_slot = grid_map % block_count
    send_slot = jnp.sum(jnp.where(source_dev == dom_index, source_slot, 0), axis=1)
    kernels = psf[0]
    band_all = depth_band[0]
    total_planes = band_all.shape[0]
    reach = (kernels.shape[2] - 1) // 2
    wide = 2 * reach
    last = block_count - 1
    above = jnp.take(send_slot, jnp.clip(slot_ids - 1, 0, last), mode="clip")
    below = jnp.take(send_slot, jnp.clip(slot_ids + 1, 0, last), mode="clip")
    wide_count = plane_count + 2 * wide
    chunk_plane = jnp.arange(wide_count, dtype=jnp.int32)
    in_top = chunk_plane < wide
    in_bottom = chunk_plane >= wide + plane_count
    source_plane = jnp.where(
        in_top, chunk_plane + plane_count - wide,
        jnp.where(in_bottom, chunk_plane - wide - plane_count, chunk_plane - wide),
    )
    source_block = jnp.where(
        in_top[:, None], above[None, :], jnp.where(in_bottom[:, None], below[None, :], send_slot[None, :])
    )
    send_index = (source_plane[:, None] * block_count + source_block).reshape(-1)
    flat_blocks = estimate.reshape(plane_count * block_count, block_rows, lane_count)
    outgoing = jnp.take(flat_blocks, send_index, axis=0, mode="clip")
    outgoing = outgoing.reshape(wide_count, block_count, block_rows, lane_count)
    arrived = lax.all_to_all(outgoing, "dom", split_axis=1, concat_axis=1, tiled=True)
    my_sources = lax.dynamic_index_in_dim(source_dev, dom_index, 0, keepdims=False)
    src_above = lax.dynamic_index_in_dim(source_dev, jnp.maximum(dom_index - 1, 0), 0, keepdims=False)
    src_below = lax.dynamic_index_in_dim(source_dev, jnp.minimum(dom_index + 1, last), 0, keepdims=False)
    from_block = jnp.where(
        in_top[:, None], src_above[None, :], jnp.where(in_bottom[:, None], src_below[None, :], my_sources[None, :])
    )
    recv_index = (chunk_plane[:, None] * block_count + from_block).reshape(-1)
    flat_arrived = arrived.reshape(wide_count * block_count, block_rows, lane_count)
    camera_ext = jnp.take(flat_arrived, recv_index, axis=0, mode="clip")
    camera_ext = camera_ext.reshape(wide_count, block_count, block_rows, lane_count)
    wide_planes = plane_start - wide + jnp.arange(wide_count, dtype=jnp.int32)
    wide_inside = (wide_planes >= 0) & (wide_planes < total_planes)
    camera_ext = jnp.where(wide_inside[:, None, None, None], camera_ext, 0.0)
    camera_ext = camera_ext.reshape(wide_count, row_count, lane_count)
    band_wide = jnp.take(band_all, jnp.clip(wide_planes, 0, total_planes - 1), mode="clip")
    x_wide = jnp.take(kernels[:, 2], band_wide, axis=0, mode="clip")
    y_wide = jnp.take(kernels[:, 1], band_wide, axis=0, mode="clip")
    lateral_ext = lateral_fwd(camera_ext, x_wide, y_wide)
    ext_count = plane_count + 2 * reach
    ext_planes = plane_start - reach + jnp.arange(ext_count, dtype=jnp.int32)
    ext_inside = (ext_planes >= 0) & (ext_planes < total_planes)
    band_ext = jnp.take(band_all, jnp.clip(ext_planes, 0, total_planes - 1), mode="clip")
    taps_ext = jnp.take(kernels[:, 0], band_ext, axis=0, mode="clip")
    blurred = jnp.zeros((ext_count, row_count, lane_count), jnp.float32)
    for j in range(2 * reach + 1):
        blurred = blurred + taps_ext[:, j][:, None, None] * lateral_ext[j : j + ext_count]
    observed_ext = extended_2(observed[0], (("dom", 0),), reach)
    ratio_ext = jnp.where(ext_inside[:, None, None], observed_ext / blurred, 0.0)
    band_own = lax.dynamic_slice_in_dim(band_all, plane_start, plane_count)
    x_own = jnp.take(kernels[:, 2], band_own, axis=0, mode="clip")
    y_own = jnp.take(kernels[:, 1], band_own, axis=0, mode="clip")
    zback = jnp.zeros((plane_count, row_count, lane_count), jnp.float32)
    for m in range(2 * reach + 1):
        zback = zback + taps_ext[m : m + plane_count, 2 * reach - m][:, None, None] * ratio_ext[m : m + plane_count]
    back = lateral_back(zback, x_own, y_own)
    dest_slot = jnp.sum(
        jnp.where(my_sources[None, :] == slot_ids[:, None], slot_ids[None, :], 0), axis=1
    )
    piece_planes = plane_count // view_count
    logs = jnp.log(back).reshape(plane_count * block_count, block_rows, lane_count)
    piece_index = jnp.arange(plane_count, dtype=jnp.int32)[None, :] * block_count + dest_slot[:, None]
    outgoing = jnp.take(logs, piece_index.reshape(-1), axis=0, mode="clip")
    outgoing = outgoing.reshape(block_count * view_count, piece_planes, block_rows, lane_count)
    arrived_logs = lax.all_to_all(outgoing, ("dom", "view"), 0, 0, tiled=True)
    all_grid = src_map.reshape(view_count, block_count, block_count)
    all_dev = all_grid // block_count
    all_slot = all_grid % block_count
    slot_of = jnp.sum(jnp.where(all_dev == dom_index, all_slot, 0), axis=2)
    cam_of = jnp.sum(
        jnp.where(slot_of[:, :, None] == slot_ids[None, None, :], slot_ids[None, :, None], 0), axis=1
    )
    view_ids = jnp.arange(view_count, dtype=jnp.int32)
    flat_index = (cam_of * view_count + view_ids[:, None]).reshape(-1)
    by_view = jnp.take(arrived_logs, flat_index, axis=0, mode="clip")
    by_view = by_view.reshape(view_count, block_count, piece_planes, block_rows, lane_count)
    log_total = by_view[0]
    for v in range(1, view_count):
        log_total = log_total + by_view[v]
    log_total = log_total.transpose(1, 0, 2, 3).reshape(piece_planes, row_count, lane_count)
    est_piece = lax.dynamic_slice_in_dim(estimate, view_index * piece_planes, piece_planes, 0)
    updated = est_piece * jnp.exp(log_total / view_count)
    return lax.all_gather(updated, "view", axis=0, tiled=True)


def solution(mesh):
    in_specs = (
        P(("tile", "dom"), None, None),
        P("view", ("tile", "dom"), None, None),
        P("view", None, None, None),
        P(),
        P("view", None),
    )
    out_specs = P(("tile", "dom"), None, None)
    return jax.shard_map(body, mesh=mesh, in_specs=in_specs, out_specs=out_specs, check_vma=False)
```

```python
import jax
import jax.numpy as jnp
from jax import lax
from jax.sharding import PartitionSpec as P

RADIUS = 4


precise = lax.Precision.HIGHEST


def extended_2(shard, sides, width):
    for axis, dim in sides:
        size, length = (lax.axis_size(axis), shard.shape[dim])
        up = [(i, (i + 1) % size) for i in range(size - 1)]
        down = [(j, i) for i, j in up]
        last = lax.slice_in_dim(shard, length - width, length, axis=dim)
        initial = lax.slice_in_dim(shard, 0, width, axis=dim)
        before = lax.ppermute(last, axis, up)
        after = lax.ppermute(initial, axis, down)
        shard = jnp.concatenate([before, shard, after], axis=dim)
    return shard


def taps_along(field, taps, axis, flipped):
    tap_count = taps.shape[0]
    reach = (tap_count - 1) // 2
    length = field.shape[axis]
    widths = [(0, 0), (0, 0), (0, 0)]
    widths[axis] = (reach, reach)
    padded = jnp.pad(field, widths)
    total = jnp.zeros(field.shape, jnp.float32)
    for offset in range(tap_count):
        start = 2 * reach - offset if flipped else offset
        piece = lax.slice_in_dim(padded, start, start + length, axis=axis)
        total = total + taps[offset][:, None, None] * piece
    return total


def lateral_fwd(field, x_taps, y_taps):
    inner = taps_along(field, x_taps, 2, False)
    return taps_along(inner, y_taps, 1, False)


def lateral_back(field, x_taps, y_taps):
    inner = taps_along(field, y_taps, 1, True)
    return taps_along(inner, x_taps, 2, True)


def body(estimate, observed, psf, src_map, depth_band):
    plane_count, row_count, lane_count = estimate.shape
    block_count = lax.axis_size("dom")
    block_rows = row_count // block_count
    dom_index = lax.axis_index("dom")
    view_index = lax.axis_index("view")
    view_count = lax.axis_size("view")
    plane_start = dom_index * plane_count
    slot_ids = jnp.arange(block_count, dtype=jnp.int32)
    my_map = lax.dynamic_index_in_dim(src_map, view_index, 0, keepdims=False)
    grid_map = my_map.reshape(block_count, block_count)
    source_dev = grid_map // block_count
    source_slot = grid_map % block_count
    send_slot = jnp.sum(jnp.where(source_dev == dom_index, source_slot, 0), axis=1)
    kernels = psf[0]
    band_all = depth_band[0]
    total_planes = band_all.shape[0]
    reach = (kernels.shape[2] - 1) // 2
    wide = 2 * reach
    last = block_count - 1
    above = jnp.take(send_slot, jnp.clip(slot_ids - 1, 0, last), mode="clip")
    below = jnp.take(send_slot, jnp.clip(slot_ids + 1, 0, last), mode="clip")
    wide_count = plane_count + 2 * wide
    chunk_plane = jnp.arange(wide_count, dtype=jnp.int32)
    in_top = chunk_plane < wide
    in_bottom = chunk_plane >= wide + plane_count
    source_plane = jnp.where(
        in_top, chunk_plane + plane_count - wide,
        jnp.where(in_bottom, chunk_plane - wide - plane_count, chunk_plane - wide),
    )
    source_block = jnp.where(
        in_top[:, None], above[None, :], jnp.where(in_bottom[:, None], below[None, :], send_slot[None, :])
    )
    send_index = (source_plane[None, :] * block_count + source_block.T).reshape(-1)
    flat_blocks = estimate.reshape(plane_count * block_count, block_rows, lane_count)
    outgoing = jnp.take(flat_blocks, send_index, axis=0, mode="clip")
    outgoing = outgoing.reshape(block_count * wide_count, block_rows, lane_count)
    arrived = lax.all_to_all(outgoing, "dom", split_axis=0, concat_axis=0, tiled=True)
    my_sources = lax.dynamic_index_in_dim(source_dev, dom_index, 0, keepdims=False)
    src_above = lax.dynamic_index_in_dim(source_dev, jnp.maximum(dom_index - 1, 0), 0, keepdims=False)
    src_below = lax.dynamic_index_in_dim(source_dev, jnp.minimum(dom_index + 1, last), 0, keepdims=False)
    from_block = jnp.where(
        in_top[:, None], src_above[None, :], jnp.where(in_bottom[:, None], src_below[None, :], my_sources[None, :])
    )
    recv_index = (from_block * wide_count + chunk_plane[:, None]).reshape(-1)
    camera_ext = jnp.take(arrived, recv_index, axis=0, mode="clip")
    camera_ext = camera_ext.reshape(wide_count, block_count, block_rows, lane_count)
    wide_planes = plane_start - wide + jnp.arange(wide_count, dtype=jnp.int32)
    wide_inside = (wide_planes >= 0) & (wide_planes < total_planes)
    camera_ext = jnp.where(wide_inside[:, None, None, None], camera_ext, 0.0)
    camera_ext = camera_ext.reshape(wide_count, row_count, lane_count)
    band_pad = jnp.pad(band_all, wide, mode="edge")
    band_wide = lax.dynamic_slice_in_dim(band_pad, plane_start, wide_count)
    band_ids = jnp.arange(kernels.shape[0], dtype=jnp.int32)
    in_band = band_wide[None, :] == band_ids[:, None]
    tables = jnp.sum(jnp.where(in_band[:, None, None, :], kernels[:, :, :, None], 0.0), axis=0)
    x_wide = tables[2]
    y_wide = tables[1]
    lateral_ext = lateral_fwd(camera_ext, x_wide, y_wide)
    ext_count = plane_count + 2 * reach
    ext_planes = plane_start - reach + jnp.arange(ext_count, dtype=jnp.int32)
    ext_inside = (ext_planes >= 0) & (ext_planes < total_planes)
    taps_ext = tables[0][:, reach : reach + ext_count]
    blurred = jnp.zeros((ext_count, row_count, lane_count), jnp.float32)
    for j in range(2 * reach + 1):
        blurred = blurred + taps_ext[j][:, None, None] * lateral_ext[j : j + ext_count]
    observed_ext = extended_2(observed[0], (("dom", 0),), reach)
    ratio_ext = jnp.where(ext_inside[:, None, None], observed_ext / blurred, 0.0)
    x_own = tables[2][:, wide : wide + plane_count]
    y_own = tables[1][:, wide : wide + plane_count]
    zback = jnp.zeros((plane_count, row_count, lane_count), jnp.float32)
    for m in range(2 * reach + 1):
        zback = zback + taps_ext[2 * reach - m, m : m + plane_count][:, None, None] * ratio_ext[m : m + plane_count]
    back = lateral_back(zback, x_own, y_own)
    dest_slot = jnp.sum(
        jnp.where(my_sources[None, :] == slot_ids[:, None], slot_ids[None, :], 0), axis=1
    )
    piece_planes = plane_count // view_count
    logs = jnp.log(back).reshape(plane_count * block_count, block_rows, lane_count)
    piece_index = jnp.arange(plane_count, dtype=jnp.int32)[None, :] * block_count + dest_slot[:, None]
    outgoing = jnp.take(logs, piece_index.reshape(-1), axis=0, mode="clip")
    outgoing = outgoing.reshape(block_count * view_count, piece_planes, block_rows, lane_count)
    arrived_logs = lax.all_to_all(outgoing, ("dom", "view"), 0, 0, tiled=True)
    all_grid = src_map.reshape(view_count, block_count, block_count)
    all_dev = all_grid // block_count
    all_slot = all_grid % block_count
    slot_of = jnp.sum(jnp.where(all_dev == dom_index, all_slot, 0), axis=2)
    cam_of = jnp.sum(
        jnp.where(slot_of[:, :, None] == slot_ids[None, None, :], slot_ids[None, :, None], 0), axis=1
    )
    view_ids = jnp.arange(view_count, dtype=jnp.int32)
    flat_index = (cam_of * view_count + view_ids[:, None]).reshape(-1)
    by_view = jnp.take(arrived_logs, flat_index, axis=0, mode="clip")
    by_view = by_view.reshape(view_count, block_count, piece_planes, block_rows, lane_count)
    log_total = by_view[0]
    for v in range(1, view_count):
        log_total = log_total + by_view[v]
    log_total = log_total.transpose(1, 0, 2, 3).reshape(piece_planes, row_count, lane_count)
    est_piece = lax.dynamic_slice_in_dim(estimate, view_index * piece_planes, piece_planes, 0)
    updated = est_piece * jnp.exp(log_total / view_count)
    return lax.all_gather(updated, "view", axis=0, tiled=True)


def solution(mesh):
    in_specs = (
        P(("tile", "dom"), None, None),
        P("view", ("tile", "dom"), None, None),
        P("view", None, None, None),
        P(),
        P("view", None),
    )
    out_specs = P(("tile", "dom"), None, None)
    return jax.shard_map(body, mesh=mesh, in_specs=in_specs, out_specs=out_specs, check_vma=False)
```

```python
import jax
import jax.numpy as jnp
from jax import lax
from jax.sharding import PartitionSpec as P

RADIUS = 4


precise = lax.Precision.HIGHEST


def extended_2(shard, sides, width):
    for axis, dim in sides:
        size, length = (lax.axis_size(axis), shard.shape[dim])
        up = [(i, (i + 1) % size) for i in range(size - 1)]
        down = [(j, i) for i, j in up]
        last = lax.slice_in_dim(shard, length - width, length, axis=dim)
        initial = lax.slice_in_dim(shard, 0, width, axis=dim)
        before = lax.ppermute(last, axis, up)
        after = lax.ppermute(initial, axis, down)
        shard = jnp.concatenate([before, shard, after], axis=dim)
    return shard


def taps_along(field, taps, axis, flipped):
    tap_count = taps.shape[0]
    reach = (tap_count - 1) // 2
    length = field.shape[axis]
    widths = [(0, 0), (0, 0), (0, 0)]
    widths[axis] = (reach, reach)
    padded = jnp.pad(field, widths)
    total = jnp.zeros(field.shape, jnp.float32)
    for offset in range(tap_count):
        start = 2 * reach - offset if flipped else offset
        piece = lax.slice_in_dim(padded, start, start + length, axis=axis)
        total = total + taps[offset][:, None, None] * piece
    return total


def lateral_fwd(field, x_taps, y_taps):
    inner = taps_along(field, x_taps, 2, False)
    return taps_along(inner, y_taps, 1, False)


def lateral_back(field, x_taps, y_taps):
    inner = taps_along(field, y_taps, 1, True)
    return taps_along(inner, x_taps, 2, True)


def body(estimate, observed, psf, src_map, depth_band):
    plane_count, row_count, lane_count = estimate.shape
    block_count = lax.axis_size("dom")
    block_rows = row_count // block_count
    dom_index = lax.axis_index("dom")
    view_index = lax.axis_index("view")
    view_count = lax.axis_size("view")
    plane_start = dom_index * plane_count
    slot_ids = jnp.arange(block_count, dtype=jnp.int32)
    my_map = lax.dynamic_index_in_dim(src_map, view_index, 0, keepdims=False)
    grid_map = my_map.reshape(block_count, block_count)
    source_dev = grid_map // block_count
    source_slot = grid_map % block_count
    near_rows = jnp.stack(
        [
            jnp.concatenate([grid_map[:1], grid_map[:-1]], axis=0),
            grid_map,
            jnp.concatenate([grid_map[1:], grid_map[-1:]], axis=0),
        ]
    )
    near_slots = jnp.sum(
        jnp.where(near_rows // block_count == dom_index, near_rows % block_count, 0), axis=2
    )
    above, send_slot, below = near_slots[0], near_slots[1], near_slots[2]
    kernels = psf[0]
    band_all = depth_band[0]
    total_planes = band_all.shape[0]
    reach = (kernels.shape[2] - 1) // 2
    wide = 2 * reach
    last = block_count - 1
    wide_count = plane_count + 2 * wide
    chunk_plane = jnp.arange(wide_count, dtype=jnp.int32)
    in_top = chunk_plane < wide
    in_bottom = chunk_plane >= wide + plane_count
    source_plane = jnp.where(
        in_top, chunk_plane + plane_count - wide,
        jnp.where(in_bottom, chunk_plane - wide - plane_count, chunk_plane - wide),
    )
    source_block = jnp.where(
        in_top[:, None], above[None, :], jnp.where(in_bottom[:, None], below[None, :], send_slot[None, :])
    )
    send_index = (source_plane[None, :] * block_count + source_block.T).reshape(-1)
    flat_blocks = estimate.reshape(plane_count * block_count, block_rows, lane_count)
    outgoing = jnp.take(flat_blocks, send_index, axis=0, mode="clip")
    outgoing = outgoing.reshape(block_count * wide_count, block_rows, lane_count)
    arrived = lax.all_to_all(outgoing, "dom", split_axis=0, concat_axis=0, tiled=True)
    my_sources = lax.dynamic_index_in_dim(source_dev, dom_index, 0, keepdims=False)
    src_above = lax.dynamic_index_in_dim(source_dev, jnp.maximum(dom_index - 1, 0), 0, keepdims=False)
    src_below = lax.dynamic_index_in_dim(source_dev, jnp.minimum(dom_index + 1, last), 0, keepdims=False)
    from_block = jnp.where(
        in_top[:, None], src_above[None, :], jnp.where(in_bottom[:, None], src_below[None, :], my_sources[None, :])
    )
    recv_index = (from_block * wide_count + chunk_plane[:, None]).reshape(-1)
    camera_ext = jnp.take(arrived, recv_index, axis=0, mode="clip")
    camera_ext = camera_ext.reshape(wide_count, block_count, block_rows, lane_count)
    wide_planes = plane_start - wide + jnp.arange(wide_count, dtype=jnp.int32)
    wide_inside = (wide_planes >= 0) & (wide_planes < total_planes)
    camera_ext = camera_ext.reshape(wide_count, row_count, lane_count)
    band_pad = jnp.pad(band_all, wide, mode="edge")
    band_wide = lax.dynamic_slice_in_dim(band_pad, plane_start, wide_count)
    band_ids = jnp.arange(kernels.shape[0], dtype=jnp.int32)
    in_band = band_wide[None, :] == band_ids[:, None]
    tables = jnp.sum(jnp.where(in_band[:, None, None, :], kernels[:, :, :, None], 0.0), axis=0)
    x_wide = tables[2]
    y_wide = tables[1]
    lateral_ext = lateral_fwd(camera_ext, x_wide, y_wide)
    lateral_ext = jnp.where(wide_inside[:, None, None], lateral_ext, 0.0)
    ext_count = plane_count + 2 * reach
    ext_planes = plane_start - reach + jnp.arange(ext_count, dtype=jnp.int32)
    ext_inside = (ext_planes >= 0) & (ext_planes < total_planes)
    taps_ext = tables[0][:, reach : reach + ext_count]
    blurred = jnp.zeros((ext_count, row_count, lane_count), jnp.float32)
    for j in range(2 * reach + 1):
        blurred = blurred + taps_ext[j][:, None, None] * lateral_ext[j : j + ext_count]
    observed_ext = extended_2(observed[0], (("dom", 0),), reach)
    ratio_ext = jnp.where(ext_inside[:, None, None], observed_ext / blurred, 0.0)
    x_own = tables[2][:, wide : wide + plane_count]
    y_own = tables[1][:, wide : wide + plane_count]
    zback = jnp.zeros((plane_count, row_count, lane_count), jnp.float32)
    for m in range(2 * reach + 1):
        zback = zback + taps_ext[2 * reach - m, m : m + plane_count][:, None, None] * ratio_ext[m : m + plane_count]
    back = lateral_back(zback, x_own, y_own)
    dest_slot = jnp.sum(
        jnp.where(my_sources[None, :] == slot_ids[:, None], slot_ids[None, :], 0), axis=1
    )
    piece_planes = plane_count // view_count
    logs = jnp.log(back).reshape(plane_count * block_count, block_rows, lane_count)
    piece_index = jnp.arange(plane_count, dtype=jnp.int32)[None, :] * block_count + dest_slot[:, None]
    outgoing = jnp.take(logs, piece_index.reshape(-1), axis=0, mode="clip")
    outgoing = outgoing.reshape(block_count * view_count, piece_planes, block_rows, lane_count)
    arrived_logs = lax.all_to_all(outgoing, ("dom", "view"), 0, 0, tiled=True)
    all_grid = src_map.reshape(view_count, block_count, block_count)
    all_dev = all_grid // block_count
    all_slot = all_grid % block_count
    slot_of = jnp.sum(jnp.where(all_dev == dom_index, all_slot, 0), axis=2)
    cam_of = jnp.sum(
        jnp.where(slot_of[:, :, None] == slot_ids[None, None, :], slot_ids[None, :, None], 0), axis=1
    )
    view_ids = jnp.arange(view_count, dtype=jnp.int32)
    flat_index = (cam_of * view_count + view_ids[:, None]).reshape(-1)
    by_view = jnp.take(arrived_logs, flat_index, axis=0, mode="clip")
    by_view = by_view.reshape(view_count, block_count, piece_planes, block_rows, lane_count)
    log_total = by_view[0]
    for v in range(1, view_count):
        log_total = log_total + by_view[v]
    log_total = log_total.transpose(1, 0, 2, 3).reshape(piece_planes, row_count, lane_count)
    est_piece = lax.dynamic_slice_in_dim(estimate, view_index * piece_planes, piece_planes, 0)
    updated = est_piece * jnp.exp(log_total / view_count)
    return lax.all_gather(updated, "view", axis=0, tiled=True)


def solution(mesh):
    in_specs = (
        P(("tile", "dom"), None, None),
        P("view", ("tile", "dom"), None, None),
        P("view", None, None, None),
        P(),
        P("view", None),
    )
    out_specs = P(("tile", "dom"), None, None)
    return jax.shard_map(body, mesh=mesh, in_specs=in_specs, out_specs=out_specs, check_vma=False)
```

```python
import jax
import jax.numpy as jnp
from jax import lax
from jax.sharding import PartitionSpec as P

RADIUS = 4


precise = lax.Precision.HIGHEST


def extended_2(shard, sides, width):
    for axis, dim in sides:
        size, length = (lax.axis_size(axis), shard.shape[dim])
        up = [(i, (i + 1) % size) for i in range(size - 1)]
        down = [(j, i) for i, j in up]
        last = lax.slice_in_dim(shard, length - width, length, axis=dim)
        initial = lax.slice_in_dim(shard, 0, width, axis=dim)
        before = lax.ppermute(last, axis, up)
        after = lax.ppermute(initial, axis, down)
        shard = jnp.concatenate([before, shard, after], axis=dim)
    return shard


def taps_along(field, taps, axis, flipped):
    tap_count = taps.shape[0]
    reach = (tap_count - 1) // 2
    length = field.shape[axis]
    widths = [(0, 0), (0, 0), (0, 0)]
    widths[axis] = (reach, reach)
    padded = jnp.pad(field, widths)
    total = jnp.zeros(field.shape, jnp.float32)
    for offset in range(tap_count):
        start = 2 * reach - offset if flipped else offset
        piece = lax.slice_in_dim(padded, start, start + length, axis=axis)
        total = total + taps[offset][:, None, None] * piece
    return total


def rows_mixed(field, taps, flipped):
    tap_count = taps.shape[0]
    reach = (tap_count - 1) // 2
    length = field.shape[1]
    out_pos = jnp.arange(length, dtype=jnp.int32)[:, None]
    in_pos = jnp.arange(length, dtype=jnp.int32)[None, :]
    offset = out_pos - in_pos if flipped else in_pos - out_pos
    mix = jnp.zeros((taps.shape[1], length, length), jnp.float32)
    for tap in range(tap_count):
        mix = mix + jnp.where((offset == tap - reach)[None], taps[tap][:, None, None], 0.0)
    return jnp.einsum("pri,pix->prx", mix, field, precision=precise)


def lateral_fwd(field, x_taps, y_taps):
    inner = taps_along(field, x_taps, 2, False)
    return rows_mixed(inner, y_taps, False)


def lateral_back(field, x_taps, y_taps):
    inner = rows_mixed(field, y_taps, True)
    return taps_along(inner, x_taps, 2, True)


def body(estimate, observed, psf, src_map, depth_band):
    plane_count, row_count, lane_count = estimate.shape
    block_count = lax.axis_size("dom")
    block_rows = row_count // block_count
    dom_index = lax.axis_index("dom")
    view_index = lax.axis_index("view")
    view_count = lax.axis_size("view")
    plane_start = dom_index * plane_count
    slot_ids = jnp.arange(block_count, dtype=jnp.int32)
    my_map = lax.dynamic_index_in_dim(src_map, view_index, 0, keepdims=False)
    grid_map = my_map.reshape(block_count, block_count)
    source_dev = grid_map // block_count
    source_slot = grid_map % block_count
    near_rows = jnp.stack(
        [
            jnp.concatenate([grid_map[:1], grid_map[:-1]], axis=0),
            grid_map,
            jnp.concatenate([grid_map[1:], grid_map[-1:]], axis=0),
        ]
    )
    near_slots = jnp.sum(
        jnp.where(near_rows // block_count == dom_index, near_rows % block_count, 0), axis=2
    )
    above, send_slot, below = near_slots[0], near_slots[1], near_slots[2]
    kernels = psf[0]
    band_all = depth_band[0]
    total_planes = band_all.shape[0]
    reach = (kernels.shape[2] - 1) // 2
    wide = 2 * reach
    last = block_count - 1
    wide_count = plane_count + 2 * wide
    chunk_plane = jnp.arange(wide_count, dtype=jnp.int32)
    in_top = chunk_plane < wide
    in_bottom = chunk_plane >= wide + plane_count
    source_plane = jnp.where(
        in_top, chunk_plane + plane_count - wide,
        jnp.where(in_bottom, chunk_plane - wide - plane_count, chunk_plane - wide),
    )
    source_block = jnp.where(
        in_top[:, None], above[None, :], jnp.where(in_bottom[:, None], below[None, :], send_slot[None, :])
    )
    send_index = (source_plane[None, :] * block_count + source_block.T).reshape(-1)
    flat_blocks = estimate.reshape(plane_count * block_count, block_rows, lane_count)
    outgoing = jnp.take(flat_blocks, send_index, axis=0, mode="clip")
    outgoing = outgoing.reshape(block_count * wide_count, block_rows, lane_count)
    arrived = lax.all_to_all(outgoing, "dom", split_axis=0, concat_axis=0, tiled=True)
    my_sources = lax.dynamic_index_in_dim(source_dev, dom_index, 0, keepdims=False)
    src_above = lax.dynamic_index_in_dim(source_dev, jnp.maximum(dom_index - 1, 0), 0, keepdims=False)
    src_below = lax.dynamic_index_in_dim(source_dev, jnp.minimum(dom_index + 1, last), 0, keepdims=False)
    from_block = jnp.where(
        in_top[:, None], src_above[None, :], jnp.where(in_bottom[:, None], src_below[None, :], my_sources[None, :])
    )
    recv_index = (from_block * wide_count + chunk_plane[:, None]).reshape(-1)
    camera_ext = jnp.take(arrived, recv_index, axis=0, mode="clip")
    camera_ext = camera_ext.reshape(wide_count, block_count, block_rows, lane_count)
    wide_planes = plane_start - wide + jnp.arange(wide_count, dtype=jnp.int32)
    wide_inside = (wide_planes >= 0) & (wide_planes < total_planes)
    camera_ext = camera_ext.reshape(wide_count, row_count, lane_count)
    band_pad = jnp.pad(band_all, wide, mode="edge")
    band_wide = lax.dynamic_slice_in_dim(band_pad, plane_start, wide_count)
    band_ids = jnp.arange(kernels.shape[0], dtype=jnp.int32)
    in_band = band_wide[None, :] == band_ids[:, None]
    tables = jnp.sum(jnp.where(in_band[:, None, None, :], kernels[:, :, :, None], 0.0), axis=0)
    x_wide = tables[2]
    y_wide = tables[1]
    lateral_ext = lateral_fwd(camera_ext, x_wide, y_wide)
    lateral_ext = jnp.where(wide_inside[:, None, None], lateral_ext, 0.0)
    ext_count = plane_count + 2 * reach
    ext_planes = plane_start - reach + jnp.arange(ext_count, dtype=jnp.int32)
    ext_inside = (ext_planes >= 0) & (ext_planes < total_planes)
    taps_ext = tables[0][:, reach : reach + ext_count]
    blurred = jnp.zeros((ext_count, row_count, lane_count), jnp.float32)
    for j in range(2 * reach + 1):
        blurred = blurred + taps_ext[j][:, None, None] * lateral_ext[j : j + ext_count]
    observed_ext = extended_2(observed[0], (("dom", 0),), reach)
    ratio_ext = jnp.where(ext_inside[:, None, None], observed_ext / blurred, 0.0)
    x_own = tables[2][:, wide : wide + plane_count]
    y_own = tables[1][:, wide : wide + plane_count]
    zback = jnp.zeros((plane_count, row_count, lane_count), jnp.float32)
    for m in range(2 * reach + 1):
        zback = zback + taps_ext[2 * reach - m, m : m + plane_count][:, None, None] * ratio_ext[m : m + plane_count]
    back = lateral_back(zback, x_own, y_own)
    dest_slot = jnp.sum(
        jnp.where(my_sources[None, :] == slot_ids[:, None], slot_ids[None, :], 0), axis=1
    )
    piece_planes = plane_count // view_count
    logs = jnp.log(back).reshape(plane_count * block_count, block_rows, lane_count)
    piece_index = jnp.arange(plane_count, dtype=jnp.int32)[None, :] * block_count + dest_slot[:, None]
    outgoing = jnp.take(logs, piece_index.reshape(-1), axis=0, mode="clip")
    outgoing = outgoing.reshape(block_count * view_count, piece_planes, block_rows, lane_count)
    arrived_logs = lax.all_to_all(outgoing, ("dom", "view"), 0, 0, tiled=True)
    all_grid = src_map.reshape(view_count, block_count, block_count)
    all_dev = all_grid // block_count
    all_slot = all_grid % block_count
    slot_of = jnp.sum(jnp.where(all_dev == dom_index, all_slot, 0), axis=2)
    cam_of = jnp.sum(
        jnp.where(slot_of[:, :, None] == slot_ids[None, None, :], slot_ids[None, :, None], 0), axis=1
    )
    view_ids = jnp.arange(view_count, dtype=jnp.int32)
    flat_index = (cam_of * view_count + view_ids[:, None]).reshape(-1)
    by_view = jnp.take(arrived_logs, flat_index, axis=0, mode="clip")
    by_view = by_view.reshape(view_count, block_count, piece_planes, block_rows, lane_count)
    log_total = by_view[0]
    for v in range(1, view_count):
        log_total = log_total + by_view[v]
    log_total = log_total.transpose(1, 0, 2, 3).reshape(piece_planes, row_count, lane_count)
    est_piece = lax.dynamic_slice_in_dim(estimate, view_index * piece_planes, piece_planes, 0)
    updated = est_piece * jnp.exp(log_total / view_count)
    return lax.all_gather(updated, "view", axis=0, tiled=True)


def solution(mesh):
    in_specs = (
        P(("tile", "dom"), None, None),
        P("view", ("tile", "dom"), None, None),
        P("view", None, None, None),
        P(),
        P("view", None),
    )
    out_specs = P(("tile", "dom"), None, None)
    return jax.shard_map(body, mesh=mesh, in_specs=in_specs, out_specs=out_specs, check_vma=False)
```

```python
import jax
import jax.numpy as jnp
from jax import lax
from jax.sharding import PartitionSpec as P

RADIUS = 4


precise = lax.Precision.HIGHEST


def extended_2(shard, sides, width):
    for axis, dim in sides:
        size, length = (lax.axis_size(axis), shard.shape[dim])
        up = [(i, (i + 1) % size) for i in range(size - 1)]
        down = [(j, i) for i, j in up]
        last = lax.slice_in_dim(shard, length - width, length, axis=dim)
        initial = lax.slice_in_dim(shard, 0, width, axis=dim)
        before = lax.ppermute(last, axis, up)
        after = lax.ppermute(initial, axis, down)
        shard = jnp.concatenate([before, shard, after], axis=dim)
    return shard


def taps_along(field, taps, axis, flipped):
    tap_count = taps.shape[0]
    reach = (tap_count - 1) // 2
    length = field.shape[axis]
    widths = [(0, 0), (0, 0), (0, 0)]
    widths[axis] = (reach, reach)
    padded = jnp.pad(field, widths)
    total = jnp.zeros(field.shape, jnp.float32)
    for offset in range(tap_count):
        start = 2 * reach - offset if flipped else offset
        piece = lax.slice_in_dim(padded, start, start + length, axis=axis)
        total = total + taps[offset][:, None, None] * piece
    return total


def lateral_fwd(field, x_taps, y_taps):
    inner = taps_along(field, x_taps, 2, False)
    return taps_along(inner, y_taps, 1, False)


def lateral_back(field, x_taps, y_taps):
    inner = taps_along(field, y_taps, 1, True)
    return taps_along(inner, x_taps, 2, True)


def body(estimate, observed, psf, src_map, depth_band):
    plane_count, row_count, lane_count = estimate.shape
    block_count = lax.axis_size("dom")
    block_rows = row_count // block_count
    dom_index = lax.axis_index("dom")
    view_index = lax.axis_index("view")
    view_count = lax.axis_size("view")
    plane_start = dom_index * plane_count
    slot_ids = jnp.arange(block_count, dtype=jnp.int32)
    my_map = lax.dynamic_index_in_dim(src_map, view_index, 0, keepdims=False)
    grid_map = my_map.reshape(block_count, block_count)
    source_dev = grid_map // block_count
    source_slot = grid_map % block_count
    near_rows = jnp.stack(
        [
            jnp.concatenate([grid_map[:1], grid_map[:-1]], axis=0),
            grid_map,
            jnp.concatenate([grid_map[1:], grid_map[-1:]], axis=0),
        ]
    )
    near_slots = jnp.sum(
        jnp.where(near_rows // block_count == dom_index, near_rows % block_count, 0), axis=2
    )
    above, send_slot, below = near_slots[0], near_slots[1], near_slots[2]
    kernels = psf[0]
    band_all = depth_band[0]
    total_planes = band_all.shape[0]
    reach = (kernels.shape[2] - 1) // 2
    wide = 2 * reach
    last = block_count - 1
    wide_count = plane_count + 2 * wide
    chunk_plane = jnp.arange(wide_count, dtype=jnp.int32)
    in_top = chunk_plane < wide
    in_bottom = chunk_plane >= wide + plane_count
    source_plane = jnp.where(
        in_top, chunk_plane + plane_count - wide,
        jnp.where(in_bottom, chunk_plane - wide - plane_count, chunk_plane - wide),
    )
    source_block = jnp.where(
        in_top[:, None], above[None, :], jnp.where(in_bottom[:, None], below[None, :], send_slot[None, :])
    )
    send_index = (source_plane[None, :] * block_count + source_block.T).reshape(-1)
    flat_blocks = estimate.reshape(plane_count * block_count, block_rows, lane_count)
    outgoing = jnp.take(flat_blocks, send_index, axis=0, mode="clip")
    outgoing = outgoing.reshape(block_count * wide_count, block_rows, lane_count)
    arrived = lax.all_to_all(outgoing, "dom", split_axis=0, concat_axis=0, tiled=True)
    my_sources = lax.dynamic_index_in_dim(source_dev, dom_index, 0, keepdims=False)
    src_above = lax.dynamic_index_in_dim(source_dev, jnp.maximum(dom_index - 1, 0), 0, keepdims=False)
    src_below = lax.dynamic_index_in_dim(source_dev, jnp.minimum(dom_index + 1, last), 0, keepdims=False)
    from_block = jnp.where(
        in_top[:, None], src_above[None, :], jnp.where(in_bottom[:, None], src_below[None, :], my_sources[None, :])
    )
    recv_index = (from_block * wide_count + chunk_plane[:, None]).reshape(-1)
    camera_ext = jnp.take(arrived, recv_index, axis=0, mode="clip")
    camera_ext = camera_ext.reshape(wide_count, block_count, block_rows, lane_count)
    wide_planes = plane_start - wide + jnp.arange(wide_count, dtype=jnp.int32)
    wide_inside = (wide_planes >= 0) & (wide_planes < total_planes)
    camera_ext = camera_ext.reshape(wide_count, row_count, lane_count)
    band_pad = jnp.pad(band_all, wide, mode="edge")
    band_wide = lax.dynamic_slice_in_dim(band_pad, plane_start, wide_count)
    band_ids = jnp.arange(kernels.shape[0], dtype=jnp.int32)
    in_band = band_wide[None, :] == band_ids[:, None]
    tables = jnp.sum(jnp.where(in_band[:, None, None, :], kernels[:, :, :, None], 0.0), axis=0)
    x_wide = tables[2]
    y_wide = tables[1]
    lateral_ext = lateral_fwd(camera_ext, x_wide, y_wide)
    lateral_ext = jnp.where(wide_inside[:, None, None], lateral_ext, 0.0)
    ext_count = plane_count + 2 * reach
    ext_planes = plane_start - reach + jnp.arange(ext_count, dtype=jnp.int32)
    ext_inside = (ext_planes >= 0) & (ext_planes < total_planes)
    taps_ext = tables[0][:, reach : reach + ext_count]
    blurred = jnp.zeros((ext_count, row_count, lane_count), jnp.float32)
    for j in range(2 * reach + 1):
        blurred = blurred + taps_ext[j][:, None, None] * lateral_ext[j : j + ext_count]
    observed_ext = extended_2(observed[0], (("dom", 0),), reach)
    ratio_ext = jnp.where(ext_inside[:, None, None], observed_ext / blurred, 0.0)
    x_own = tables[2][:, wide : wide + plane_count]
    y_own = tables[1][:, wide : wide + plane_count]
    zback = jnp.zeros((plane_count, row_count, lane_count), jnp.float32)
    for m in range(2 * reach + 1):
        zback = zback + taps_ext[2 * reach - m, m : m + plane_count][:, None, None] * ratio_ext[m : m + plane_count]
    back = lateral_back(zback, x_own, y_own)
    dest_slot = jnp.sum(
        jnp.where(my_sources[None, :] == slot_ids[:, None], slot_ids[None, :], 0), axis=1
    )
    piece_planes = plane_count // view_count
    logs = jnp.log(back).reshape(plane_count * block_count, block_rows, lane_count)
    piece_index = jnp.arange(plane_count, dtype=jnp.int32)[None, :] * block_count + dest_slot[:, None]
    piece_index = piece_index.reshape(block_count, view_count, piece_planes).transpose(1, 0, 2)
    outgoing = jnp.take(logs, piece_index.reshape(-1), axis=0, mode="clip")
    outgoing = outgoing.reshape(block_count * view_count, piece_planes, block_rows, lane_count)
    arrived_logs = lax.all_to_all(outgoing, ("view", "dom"), 0, 0, tiled=True)
    all_grid = src_map.reshape(view_count, block_count, block_count)
    all_dev = all_grid // block_count
    all_slot = all_grid % block_count
    slot_of = jnp.sum(jnp.where(all_dev == dom_index, all_slot, 0), axis=2)
    cam_of = jnp.sum(
        jnp.where(slot_of[:, :, None] == slot_ids[None, None, :], slot_ids[None, :, None], 0), axis=1
    )
    view_ids = jnp.arange(view_count, dtype=jnp.int32)
    flat_index = (view_ids[:, None] * block_count + cam_of).reshape(-1)
    by_view = jnp.take(arrived_logs, flat_index, axis=0, mode="clip")
    by_view = by_view.reshape(view_count, block_count, piece_planes, block_rows, lane_count)
    log_total = by_view[0]
    for v in range(1, view_count):
        log_total = log_total + by_view[v]
    log_total = log_total.transpose(1, 0, 2, 3).reshape(piece_planes, row_count, lane_count)
    est_piece = lax.dynamic_slice_in_dim(estimate, view_index * piece_planes, piece_planes, 0)
    updated = est_piece * jnp.exp(log_total / view_count)
    return lax.all_gather(updated, "view", axis=0, tiled=True)


def solution(mesh):
    in_specs = (
        P(("tile", "dom"), None, None),
        P("view", ("tile", "dom"), None, None),
        P("view", None, None, None),
        P(),
        P("view", None),
    )
    out_specs = P(("tile", "dom"), None, None)
    return jax.shard_map(body, mesh=mesh, in_specs=in_specs, out_specs=out_specs, check_vma=False)
```

```python
import jax
import jax.numpy as jnp
from jax import lax
from jax.sharding import PartitionSpec as P

RADIUS = 4


precise = lax.Precision.HIGHEST


def extended_2(shard, sides, width):
    for axis, dim in sides:
        size, length = (lax.axis_size(axis), shard.shape[dim])
        up = [(i, (i + 1) % size) for i in range(size - 1)]
        down = [(j, i) for i, j in up]
        last = lax.slice_in_dim(shard, length - width, length, axis=dim)
        initial = lax.slice_in_dim(shard, 0, width, axis=dim)
        before = lax.ppermute(last, axis, up)
        after = lax.ppermute(initial, axis, down)
        shard = jnp.concatenate([before, shard, after], axis=dim)
    return shard


def taps_along(field, taps, axis, flipped):
    tap_count = taps.shape[0]
    reach = (tap_count - 1) // 2
    length = field.shape[axis]
    widths = [(0, 0), (0, 0), (0, 0)]
    widths[axis] = (reach, reach)
    padded = jnp.pad(field, widths)
    total = jnp.zeros(field.shape, jnp.float32)
    for offset in range(tap_count):
        start = 2 * reach - offset if flipped else offset
        piece = lax.slice_in_dim(padded, start, start + length, axis=axis)
        total = total + taps[offset][:, None, None] * piece
    return total


def lateral_fwd(field, x_taps, y_taps):
    inner = taps_along(field, x_taps, 2, False)
    return taps_along(inner, y_taps, 1, False)


def body(estimate, observed, psf, src_map, depth_band):
    plane_count, row_count, lane_count = estimate.shape
    block_count = lax.axis_size("dom")
    block_rows = row_count // block_count
    dom_index = lax.axis_index("dom")
    view_index = lax.axis_index("view")
    view_count = lax.axis_size("view")
    plane_start = dom_index * plane_count
    slot_ids = jnp.arange(block_count, dtype=jnp.int32)
    my_map = lax.dynamic_index_in_dim(src_map, view_index, 0, keepdims=False)
    grid_map = my_map.reshape(block_count, block_count)
    source_dev = grid_map // block_count
    source_slot = grid_map % block_count
    near_rows = jnp.stack(
        [
            jnp.concatenate([grid_map[:1], grid_map[:-1]], axis=0),
            grid_map,
            jnp.concatenate([grid_map[1:], grid_map[-1:]], axis=0),
        ]
    )
    near_slots = jnp.sum(
        jnp.where(near_rows // block_count == dom_index, near_rows % block_count, 0), axis=2
    )
    above, send_slot, below = near_slots[0], near_slots[1], near_slots[2]
    kernels = psf[0]
    band_all = depth_band[0]
    total_planes = band_all.shape[0]
    reach = (kernels.shape[2] - 1) // 2
    wide = 2 * reach
    last = block_count - 1
    wide_count = plane_count + 2 * wide
    chunk_plane = jnp.arange(wide_count, dtype=jnp.int32)
    in_top = chunk_plane < wide
    in_bottom = chunk_plane >= wide + plane_count
    source_plane = jnp.where(
        in_top, chunk_plane + plane_count - wide,
        jnp.where(in_bottom, chunk_plane - wide - plane_count, chunk_plane - wide),
    )
    source_block = jnp.where(
        in_top[:, None], above[None, :], jnp.where(in_bottom[:, None], below[None, :], send_slot[None, :])
    )
    send_index = (source_plane[None, :] * block_count + source_block.T).reshape(-1)
    flat_blocks = estimate.reshape(plane_count * block_count, block_rows, lane_count)
    outgoing = jnp.take(flat_blocks, send_index, axis=0, mode="clip")
    outgoing = outgoing.reshape(block_count * wide_count, block_rows, lane_count)
    arrived = lax.all_to_all(outgoing, "dom", split_axis=0, concat_axis=0, tiled=True)
    my_sources = lax.dynamic_index_in_dim(source_dev, dom_index, 0, keepdims=False)
    src_above = lax.dynamic_index_in_dim(source_dev, jnp.maximum(dom_index - 1, 0), 0, keepdims=False)
    src_below = lax.dynamic_index_in_dim(source_dev, jnp.minimum(dom_index + 1, last), 0, keepdims=False)
    from_block = jnp.where(
        in_top[:, None], src_above[None, :], jnp.where(in_bottom[:, None], src_below[None, :], my_sources[None, :])
    )
    recv_index = (from_block * wide_count + chunk_plane[:, None]).reshape(-1)
    camera_ext = jnp.take(arrived, recv_index, axis=0, mode="clip")
    camera_ext = camera_ext.reshape(wide_count, block_count, block_rows, lane_count)
    wide_planes = plane_start - wide + jnp.arange(wide_count, dtype=jnp.int32)
    wide_inside = (wide_planes >= 0) & (wide_planes < total_planes)
    camera_ext = camera_ext.reshape(wide_count, row_count, lane_count)
    band_pad = jnp.pad(band_all, wide, mode="edge")
    band_wide = lax.dynamic_slice_in_dim(band_pad, plane_start, wide_count)
    band_ids = jnp.arange(kernels.shape[0], dtype=jnp.int32)
    in_band = band_wide[None, :] == band_ids[:, None]
    tables = jnp.sum(jnp.where(in_band[:, None, None, :], kernels[:, :, :, None], 0.0), axis=0)
    x_wide = tables[2]
    y_wide = tables[1]
    lateral_ext = lateral_fwd(camera_ext, x_wide, y_wide)
    lateral_ext = jnp.where(wide_inside[:, None, None], lateral_ext, 0.0)
    ext_count = plane_count + 2 * reach
    ext_planes = plane_start - reach + jnp.arange(ext_count, dtype=jnp.int32)
    ext_inside = (ext_planes >= 0) & (ext_planes < total_planes)
    taps_ext = tables[0][:, reach : reach + ext_count]
    blurred = jnp.zeros((ext_count, row_count, lane_count), jnp.float32)
    for j in range(2 * reach + 1):
        blurred = blurred + taps_ext[j][:, None, None] * lateral_ext[j : j + ext_count]
    observed_ext = extended_2(observed[0], (("dom", 0),), reach)
    ratio_ext = jnp.where(ext_inside[:, None, None], observed_ext / blurred, 0.0)
    x_own = tables[2][:, wide : wide + plane_count]
    y_own = tables[1][:, wide : wide + plane_count]
    zback = jnp.zeros((plane_count, row_count, lane_count), jnp.float32)
    for m in range(2 * reach + 1):
        zback = zback + taps_ext[2 * reach - m, m : m + plane_count][:, None, None] * ratio_ext[m : m + plane_count]
    dest_slot = jnp.sum(
        jnp.where(my_sources[None, :] == slot_ids[:, None], slot_ids[None, :], 0), axis=1
    )
    row_ids = jnp.arange(block_rows, dtype=jnp.int32)
    out_rows = (dest_slot[:, None] * block_rows + row_ids[None, :]).reshape(row_count)
    offset = out_rows[:, None] - jnp.arange(row_count, dtype=jnp.int32)[None, :]
    mix = jnp.zeros((plane_count, row_count, row_count), jnp.float32)
    for tap in range(2 * reach + 1):
        mix = mix + jnp.where((offset == tap - reach)[None], y_own[tap][:, None, None], 0.0)
    by_source = jnp.einsum("pri,pix->prx", mix, zback, precision=lax.Precision.HIGHEST)
    back = taps_along(by_source, x_own, 2, True)
    piece_planes = plane_count // view_count
    logs = jnp.log(back).reshape(view_count, piece_planes, block_count, block_rows, lane_count)
    outgoing = logs.transpose(0, 2, 1, 3, 4).reshape(view_count * block_count, piece_planes, block_rows, lane_count)
    arrived_logs = lax.all_to_all(outgoing, ("view", "dom"), 0, 0, tiled=True)
    all_grid = src_map.reshape(view_count, block_count, block_count)
    all_dev = all_grid // block_count
    all_slot = all_grid % block_count
    slot_of = jnp.sum(jnp.where(all_dev == dom_index, all_slot, 0), axis=2)
    cam_of = jnp.sum(
        jnp.where(slot_of[:, :, None] == slot_ids[None, None, :], slot_ids[None, :, None], 0), axis=1
    )
    view_ids = jnp.arange(view_count, dtype=jnp.int32)
    flat_index = (view_ids[:, None] * block_count + cam_of).reshape(-1)
    by_view = jnp.take(arrived_logs, flat_index, axis=0, mode="clip")
    by_view = by_view.reshape(view_count, block_count, piece_planes, block_rows, lane_count)
    log_total = by_view[0]
    for v in range(1, view_count):
        log_total = log_total + by_view[v]
    log_total = log_total.transpose(1, 0, 2, 3).reshape(piece_planes, row_count, lane_count)
    est_piece = lax.dynamic_slice_in_dim(estimate, view_index * piece_planes, piece_planes, 0)
    updated = est_piece * jnp.exp(log_total / view_count)
    return lax.all_gather(updated, "view", axis=0, tiled=True)


def solution(mesh):
    in_specs = (
        P(("tile", "dom"), None, None),
        P("view", ("tile", "dom"), None, None),
        P("view", None, None, None),
        P(),
        P("view", None),
    )
    out_specs = P(("tile", "dom"), None, None)
    return jax.shard_map(body, mesh=mesh, in_specs=in_specs, out_specs=out_specs, check_vma=False)
```

```python
import jax
import jax.numpy as jnp
from jax import lax
from jax.sharding import PartitionSpec as P

RADIUS = 4


precise = lax.Precision.HIGHEST


def extended_2(shard, sides, width):
    for axis, dim in sides:
        size, length = (lax.axis_size(axis), shard.shape[dim])
        up = [(i, (i + 1) % size) for i in range(size - 1)]
        down = [(j, i) for i, j in up]
        last = lax.slice_in_dim(shard, length - width, length, axis=dim)
        initial = lax.slice_in_dim(shard, 0, width, axis=dim)
        before = lax.ppermute(last, axis, up)
        after = lax.ppermute(initial, axis, down)
        shard = jnp.concatenate([before, shard, after], axis=dim)
    return shard


def taps_along(field, taps, axis, flipped):
    tap_count = taps.shape[0]
    reach = (tap_count - 1) // 2
    length = field.shape[axis]
    widths = [(0, 0), (0, 0), (0, 0)]
    widths[axis] = (reach, reach)
    padded = jnp.pad(field, widths)
    total = jnp.zeros(field.shape, jnp.float32)
    for offset in range(tap_count):
        start = 2 * reach - offset if flipped else offset
        piece = lax.slice_in_dim(padded, start, start + length, axis=axis)
        total = total + taps[offset][:, None, None] * piece
    return total


def lateral_fwd(field, x_taps, y_taps):
    inner = taps_along(field, x_taps, 2, False)
    return taps_along(inner, y_taps, 1, False)


def body(estimate, observed, psf, src_map, depth_band):
    plane_count, row_count, lane_count = estimate.shape
    block_count = lax.axis_size("dom")
    block_rows = row_count // block_count
    dom_index = lax.axis_index("dom")
    view_index = lax.axis_index("view")
    view_count = lax.axis_size("view")
    plane_start = dom_index * plane_count
    slot_ids = jnp.arange(block_count, dtype=jnp.int32)
    my_map = lax.dynamic_index_in_dim(src_map, view_index, 0, keepdims=False)
    grid_map = my_map.reshape(block_count, block_count)
    source_dev = grid_map // block_count
    source_slot = grid_map % block_count
    near_rows = jnp.stack(
        [
            jnp.concatenate([grid_map[:1], grid_map[:-1]], axis=0),
            grid_map,
            jnp.concatenate([grid_map[1:], grid_map[-1:]], axis=0),
        ]
    )
    near_slots = jnp.sum(
        jnp.where(near_rows // block_count == dom_index, near_rows % block_count, 0), axis=2
    )
    above, send_slot, below = near_slots[0], near_slots[1], near_slots[2]
    kernels = psf[0]
    band_all = depth_band[0]
    total_planes = band_all.shape[0]
    reach = (kernels.shape[2] - 1) // 2
    wide = 2 * reach
    last = block_count - 1
    wide_count = plane_count + 2 * wide
    chunk_plane = jnp.arange(wide_count, dtype=jnp.int32)
    in_top = chunk_plane < wide
    in_bottom = chunk_plane >= wide + plane_count
    source_plane = jnp.where(
        in_top, chunk_plane + plane_count - wide,
        jnp.where(in_bottom, chunk_plane - wide - plane_count, chunk_plane - wide),
    )
    source_block = jnp.where(
        in_top[:, None], above[None, :], jnp.where(in_bottom[:, None], below[None, :], send_slot[None, :])
    )
    send_index = (source_plane[None, :] * block_count + source_block.T).reshape(-1)
    flat_blocks = estimate.reshape(plane_count * block_count, block_rows, lane_count)
    outgoing = jnp.take(flat_blocks, send_index, axis=0, mode="clip")
    outgoing = outgoing.reshape(block_count * wide_count, block_rows, lane_count)
    arrived = lax.all_to_all(outgoing, "dom", split_axis=0, concat_axis=0, tiled=True)
    my_sources = lax.dynamic_index_in_dim(source_dev, dom_index, 0, keepdims=False)
    src_above = lax.dynamic_index_in_dim(source_dev, jnp.maximum(dom_index - 1, 0), 0, keepdims=False)
    src_below = lax.dynamic_index_in_dim(source_dev, jnp.minimum(dom_index + 1, last), 0, keepdims=False)
    from_block = jnp.where(
        in_top[:, None], src_above[None, :], jnp.where(in_bottom[:, None], src_below[None, :], my_sources[None, :])
    )
    recv_index = (from_block * wide_count + chunk_plane[:, None]).reshape(-1)
    camera_ext = jnp.take(arrived, recv_index, axis=0, mode="clip")
    camera_ext = camera_ext.reshape(wide_count, block_count, block_rows, lane_count)
    wide_planes = plane_start - wide + jnp.arange(wide_count, dtype=jnp.int32)
    wide_inside = (wide_planes >= 0) & (wide_planes < total_planes)
    camera_ext = camera_ext.reshape(wide_count, row_count, lane_count)
    band_pad = jnp.pad(band_all, wide, mode="edge")
    band_wide = lax.dynamic_slice_in_dim(band_pad, plane_start, wide_count)
    band_ids = jnp.arange(kernels.shape[0], dtype=jnp.int32)
    in_band = band_wide[None, :] == band_ids[:, None]
    tables = jnp.sum(jnp.where(in_band[:, None, None, :], kernels[:, :, :, None], 0.0), axis=0)
    x_wide = tables[2]
    y_wide = tables[1]
    lateral_ext = lateral_fwd(camera_ext, x_wide, y_wide)
    lateral_ext = jnp.where(wide_inside[:, None, None], lateral_ext, 0.0)
    ext_count = plane_count + 2 * reach
    ext_planes = plane_start - reach + jnp.arange(ext_count, dtype=jnp.int32)
    ext_inside = (ext_planes >= 0) & (ext_planes < total_planes)
    taps_ext = tables[0][:, reach : reach + ext_count]
    blurred = jnp.zeros((ext_count, row_count, lane_count), jnp.float32)
    for j in range(2 * reach + 1):
        blurred = blurred + taps_ext[j][:, None, None] * lateral_ext[j : j + ext_count]
    observed_ext = extended_2(observed[0], (("dom", 0),), reach)
    ratio_ext = jnp.where(ext_inside[:, None, None], observed_ext / blurred, 0.0)
    x_own = tables[2][:, wide : wide + plane_count]
    y_own = tables[1][:, wide : wide + plane_count]
    zback = jnp.zeros((plane_count, row_count, lane_count), jnp.float32)
    for m in range(2 * reach + 1):
        zback = zback + taps_ext[2 * reach - m, m : m + plane_count][:, None, None] * ratio_ext[m : m + plane_count]
    dest_slot = jnp.sum(
        jnp.where(my_sources[None, :] == slot_ids[:, None], slot_ids[None, :], 0), axis=1
    )
    row_ids = jnp.arange(block_rows, dtype=jnp.int32)
    out_rows = (dest_slot[:, None] * block_rows + row_ids[None, :]).reshape(row_count)
    offset = out_rows[:, None] - jnp.arange(row_count, dtype=jnp.int32)[None, :]
    mix = jnp.zeros((plane_count, row_count, row_count), jnp.float32)
    for tap in range(2 * reach + 1):
        mix = mix + jnp.where((offset == tap - reach)[None], y_own[tap][:, None, None], 0.0)
    by_source = jnp.einsum("pri,pix->prx", mix, zback, precision=lax.Precision.HIGHEST)
    back = taps_along(by_source, x_own, 2, True)
    piece_planes = plane_count // view_count
    logs = jnp.log(back).reshape(view_count, piece_planes, block_count, block_rows, lane_count)
    outgoing = logs.transpose(0, 2, 1, 3, 4).reshape(view_count * block_count, piece_planes, block_rows, lane_count)
    arrived_logs = lax.all_to_all(outgoing, ("view", "dom"), 0, 0, tiled=True)
    all_grid = src_map.reshape(view_count, block_count, block_count)
    all_dev = all_grid // block_count
    all_slot = all_grid % block_count
    slot_of = jnp.sum(jnp.where(all_dev == dom_index, all_slot, 0), axis=2)
    cam_of = jnp.sum(
        jnp.where(slot_of[:, :, None] == slot_ids[None, None, :], slot_ids[None, :, None], 0), axis=1
    )
    view_ids = jnp.arange(view_count, dtype=jnp.int32)
    flat_index = (view_ids[:, None] * block_count + cam_of).reshape(-1)
    by_view = jnp.take(arrived_logs, flat_index, axis=0, mode="clip")
    by_view = by_view.reshape(view_count, block_count, piece_planes, block_rows, lane_count)
    log_total = by_view[0]
    for v in range(1, view_count):
        log_total = log_total + by_view[v]
    log_total = log_total.transpose(1, 0, 2, 3).reshape(piece_planes, row_count, lane_count)
    log_joined = lax.all_gather(log_total, "view", axis=0, tiled=True)
    return estimate * jnp.exp(log_joined / view_count)


def solution(mesh):
    in_specs = (
        P(("tile", "dom"), None, None),
        P("view", ("tile", "dom"), None, None),
        P("view", None, None, None),
        P(),
        P("view", None),
    )
    out_specs = P(("tile", "dom"), None, None)
    return jax.shard_map(body, mesh=mesh, in_specs=in_specs, out_specs=out_specs, check_vma=False)
```

```python
import jax
import jax.numpy as jnp
from jax import lax
from jax.sharding import PartitionSpec as P

RADIUS = 4


precise = lax.Precision.HIGHEST


def extended_2(shard, sides, width):
    for axis, dim in sides:
        size, length = (lax.axis_size(axis), shard.shape[dim])
        up = [(i, (i + 1) % size) for i in range(size - 1)]
        down = [(j, i) for i, j in up]
        last = lax.slice_in_dim(shard, length - width, length, axis=dim)
        initial = lax.slice_in_dim(shard, 0, width, axis=dim)
        before = lax.ppermute(last, axis, up)
        after = lax.ppermute(initial, axis, down)
        shard = jnp.concatenate([before, shard, after], axis=dim)
    return shard


def taps_along(field, taps, axis, flipped):
    tap_count = taps.shape[0]
    reach = (tap_count - 1) // 2
    length = field.shape[axis]
    widths = [(0, 0), (0, 0), (0, 0)]
    widths[axis] = (reach, reach)
    padded = jnp.pad(field, widths)
    total = jnp.zeros(field.shape, jnp.float32)
    for offset in range(tap_count):
        start = 2 * reach - offset if flipped else offset
        piece = lax.slice_in_dim(padded, start, start + length, axis=axis)
        total = total + taps[offset][:, None, None] * piece
    return total


def lateral_fwd(field, x_taps, y_taps):
    inner = taps_along(field, x_taps, 2, False)
    return taps_along(inner, y_taps, 1, False)


def body(estimate, observed, psf, src_map, depth_band):
    plane_count, row_count, lane_count = estimate.shape
    block_count = lax.axis_size("dom")
    block_rows = row_count // block_count
    dom_index = lax.axis_index("dom")
    view_index = lax.axis_index("view")
    view_count = lax.axis_size("view")
    plane_start = dom_index * plane_count
    slot_ids = jnp.arange(block_count, dtype=jnp.int32)
    view_ids = jnp.arange(view_count, dtype=jnp.int32)
    my_map = jnp.sum(jnp.where((view_ids == view_index)[:, None], src_map, 0), axis=0)
    grid_map = my_map.reshape(block_count, block_count)
    source_dev = grid_map // block_count
    source_slot = grid_map % block_count
    near_rows = jnp.stack(
        [
            jnp.concatenate([grid_map[:1], grid_map[:-1]], axis=0),
            grid_map,
            jnp.concatenate([grid_map[1:], grid_map[-1:]], axis=0),
        ]
    )
    near_slots = jnp.sum(
        jnp.where(near_rows // block_count == dom_index, near_rows % block_count, 0), axis=2
    )
    above, send_slot, below = near_slots[0], near_slots[1], near_slots[2]
    kernels = psf[0]
    band_all = depth_band[0]
    total_planes = band_all.shape[0]
    reach = (kernels.shape[2] - 1) // 2
    wide = 2 * reach
    last = block_count - 1
    wide_count = plane_count + 2 * wide
    chunk_plane = jnp.arange(wide_count, dtype=jnp.int32)
    in_top = chunk_plane < wide
    in_bottom = chunk_plane >= wide + plane_count
    source_plane = jnp.where(
        in_top, chunk_plane + plane_count - wide,
        jnp.where(in_bottom, chunk_plane - wide - plane_count, chunk_plane - wide),
    )
    source_block = jnp.where(
        in_top[:, None], above[None, :], jnp.where(in_bottom[:, None], below[None, :], send_slot[None, :])
    )
    send_index = (source_plane[None, :] * block_count + source_block.T).reshape(-1)
    flat_blocks = estimate.reshape(plane_count * block_count, block_rows, lane_count)
    outgoing = jnp.take(flat_blocks, send_index, axis=0, mode="clip")
    outgoing = outgoing.reshape(block_count * wide_count, block_rows, lane_count)
    arrived = lax.all_to_all(outgoing, "dom", split_axis=0, concat_axis=0, tiled=True)
    my_sources = lax.dynamic_index_in_dim(source_dev, dom_index, 0, keepdims=False)
    src_above = lax.dynamic_index_in_dim(source_dev, jnp.maximum(dom_index - 1, 0), 0, keepdims=False)
    src_below = lax.dynamic_index_in_dim(source_dev, jnp.minimum(dom_index + 1, last), 0, keepdims=False)
    from_block = jnp.where(
        in_top[:, None], src_above[None, :], jnp.where(in_bottom[:, None], src_below[None, :], my_sources[None, :])
    )
    recv_index = (from_block * wide_count + chunk_plane[:, None]).reshape(-1)
    camera_ext = jnp.take(arrived, recv_index, axis=0, mode="clip")
    camera_ext = camera_ext.reshape(wide_count, block_count, block_rows, lane_count)
    wide_planes = plane_start - wide + jnp.arange(wide_count, dtype=jnp.int32)
    wide_inside = (wide_planes >= 0) & (wide_planes < total_planes)
    camera_ext = camera_ext.reshape(wide_count, row_count, lane_count)
    band_pad = jnp.pad(band_all, wide, mode="edge")
    band_wide = lax.dynamic_slice_in_dim(band_pad, plane_start, wide_count)
    band_ids = jnp.arange(kernels.shape[0], dtype=jnp.int32)
    in_band = band_wide[None, :] == band_ids[:, None]
    tables = jnp.sum(jnp.where(in_band[:, None, None, :], kernels[:, :, :, None], 0.0), axis=0)
    x_wide = tables[2]
    y_wide = tables[1]
    lateral_ext = lateral_fwd(camera_ext, x_wide, y_wide)
    lateral_ext = jnp.where(wide_inside[:, None, None], lateral_ext, 0.0)
    ext_count = plane_count + 2 * reach
    ext_planes = plane_start - reach + jnp.arange(ext_count, dtype=jnp.int32)
    ext_inside = (ext_planes >= 0) & (ext_planes < total_planes)
    taps_ext = tables[0][:, reach : reach + ext_count]
    blurred = jnp.zeros((ext_count, row_count, lane_count), jnp.float32)
    for j in range(2 * reach + 1):
        blurred = blurred + taps_ext[j][:, None, None] * lateral_ext[j : j + ext_count]
    observed_ext = extended_2(observed[0], (("dom", 0),), reach)
    ratio_ext = jnp.where(ext_inside[:, None, None], observed_ext / blurred, 0.0)
    x_own = tables[2][:, wide : wide + plane_count]
    y_own = tables[1][:, wide : wide + plane_count]
    zback = jnp.zeros((plane_count, row_count, lane_count), jnp.float32)
    for m in range(2 * reach + 1):
        zback = zback + taps_ext[2 * reach - m, m : m + plane_count][:, None, None] * ratio_ext[m : m + plane_count]
    dest_slot = jnp.sum(
        jnp.where(my_sources[None, :] == slot_ids[:, None], slot_ids[None, :], 0), axis=1
    )
    row_ids = jnp.arange(block_rows, dtype=jnp.int32)
    out_rows = (dest_slot[:, None] * block_rows + row_ids[None, :]).reshape(row_count)
    offset = out_rows[:, None] - jnp.arange(row_count, dtype=jnp.int32)[None, :]
    mix = jnp.zeros((plane_count, row_count, row_count), jnp.float32)
    for tap in range(2 * reach + 1):
        mix = mix + jnp.where((offset == tap - reach)[None], y_own[tap][:, None, None], 0.0)
    by_source = jnp.einsum("pri,pix->prx", mix, zback, precision=lax.Precision.HIGHEST)
    back = taps_along(by_source, x_own, 2, True)
    piece_planes = plane_count // view_count
    logs = jnp.log(back).reshape(view_count, piece_planes, block_count, block_rows, lane_count)
    outgoing = logs.transpose(0, 2, 1, 3, 4).reshape(view_count * block_count, piece_planes, block_rows, lane_count)
    arrived_logs = lax.all_to_all(outgoing, ("view", "dom"), 0, 0, tiled=True)
    all_grid = src_map.reshape(view_count, block_count, block_count)
    all_dev = all_grid // block_count
    all_slot = all_grid % block_count
    slot_of = jnp.sum(jnp.where(all_dev == dom_index, all_slot, 0), axis=2)
    cam_of = jnp.sum(
        jnp.where(slot_of[:, :, None] == slot_ids[None, None, :], slot_ids[None, :, None], 0), axis=1
    )
    flat_index = (view_ids[:, None] * block_count + cam_of).reshape(-1)
    by_view = jnp.take(arrived_logs, flat_index, axis=0, mode="clip")
    by_view = by_view.reshape(view_count, block_count, piece_planes, block_rows, lane_count)
    log_total = by_view[0]
    for v in range(1, view_count):
        log_total = log_total + by_view[v]
    log_total = log_total.transpose(1, 0, 2, 3).reshape(piece_planes, row_count, lane_count)
    log_joined = lax.all_gather(log_total, "view", axis=0, tiled=True)
    return estimate * jnp.exp(log_joined / view_count)


def solution(mesh):
    in_specs = (
        P(("tile", "dom"), None, None),
        P("view", ("tile", "dom"), None, None),
        P("view", None, None, None),
        P(),
        P("view", None),
    )
    out_specs = P(("tile", "dom"), None, None)
    return jax.shard_map(body, mesh=mesh, in_specs=in_specs, out_specs=out_specs, check_vma=False)
```

```python
import jax
import jax.numpy as jnp
from jax import lax
from jax.sharding import PartitionSpec as P

RADIUS = 4


precise = lax.Precision.HIGHEST


def extended_2(shard, sides, width):
    for axis, dim in sides:
        size, length = (lax.axis_size(axis), shard.shape[dim])
        up = [(i, (i + 1) % size) for i in range(size - 1)]
        down = [(j, i) for i, j in up]
        last = lax.slice_in_dim(shard, length - width, length, axis=dim)
        initial = lax.slice_in_dim(shard, 0, width, axis=dim)
        before = lax.ppermute(last, axis, up)
        after = lax.ppermute(initial, axis, down)
        shard = jnp.concatenate([before, shard, after], axis=dim)
    return shard


def taps_along(field, taps, axis, flipped):
    tap_count = taps.shape[0]
    reach = (tap_count - 1) // 2
    length = field.shape[axis]
    widths = [(0, 0), (0, 0), (0, 0)]
    widths[axis] = (reach, reach)
    padded = jnp.pad(field, widths)
    total = jnp.zeros(field.shape, jnp.float32)
    for offset in range(tap_count):
        start = 2 * reach - offset if flipped else offset
        piece = lax.slice_in_dim(padded, start, start + length, axis=axis)
        total = total + taps[offset][:, None, None] * piece
    return total


def lateral_fwd(field, x_taps, y_taps):
    inner = taps_along(field, x_taps, 2, False)
    return taps_along(inner, y_taps, 1, False)


def body(estimate, observed, psf, src_map, depth_band):
    plane_count, row_count, lane_count = estimate.shape
    block_count = lax.axis_size("dom")
    block_rows = row_count // block_count
    dom_index = lax.axis_index("dom")
    view_index = lax.axis_index("view")
    view_count = lax.axis_size("view")
    plane_start = dom_index * plane_count
    slot_ids = jnp.arange(block_count, dtype=jnp.int32)
    view_ids = jnp.arange(view_count, dtype=jnp.int32)
    my_map = jnp.sum(jnp.where((view_ids == view_index)[:, None], src_map, 0), axis=0)
    grid_map = my_map.reshape(block_count, block_count)
    source_dev = grid_map // block_count
    source_slot = grid_map % block_count
    near_rows = jnp.stack(
        [
            jnp.concatenate([grid_map[:1], grid_map[:-1]], axis=0),
            grid_map,
            jnp.concatenate([grid_map[1:], grid_map[-1:]], axis=0),
        ]
    )
    near_slots = jnp.sum(
        jnp.where(near_rows // block_count == dom_index, near_rows % block_count, 0), axis=2
    )
    above, send_slot, below = near_slots[0], near_slots[1], near_slots[2]
    kernels = psf[0]
    band_all = depth_band[0]
    total_planes = band_all.shape[0]
    reach = (kernels.shape[2] - 1) // 2
    wide = 2 * reach
    last = block_count - 1
    wide_count = plane_count + 2 * wide
    blocks = estimate.reshape(plane_count, block_count, block_rows, lane_count)
    tops = blocks[plane_count - wide :]
    bottoms = blocks[:wide]

    def column(field, index):
        return lax.dynamic_index_in_dim(field, index, 1, keepdims=False)

    outgoing = jnp.stack(
        [
            jnp.concatenate(
                [column(tops, above[d]), column(blocks, send_slot[d]), column(bottoms, below[d])], axis=0
            )
            for d in range(block_count)
        ]
    )
    outgoing = outgoing.reshape(block_count * wide_count, block_rows, lane_count)
    arrived = lax.all_to_all(outgoing, "dom", split_axis=0, concat_axis=0, tiled=True)
    arrived = arrived.reshape(block_count, wide_count, block_rows, lane_count)
    my_sources = lax.dynamic_index_in_dim(source_dev, dom_index, 0, keepdims=False)
    src_above = lax.dynamic_index_in_dim(source_dev, jnp.maximum(dom_index - 1, 0), 0, keepdims=False)
    src_below = lax.dynamic_index_in_dim(source_dev, jnp.minimum(dom_index + 1, last), 0, keepdims=False)

    def pick(index, start, count):
        chunk = lax.dynamic_index_in_dim(arrived, index, 0, keepdims=False)
        return chunk[start : start + count]

    camera_ext = jnp.concatenate(
        [
            jnp.stack([pick(src_above[t], 0, wide) for t in range(block_count)], axis=1),
            jnp.stack([pick(my_sources[t], wide, plane_count) for t in range(block_count)], axis=1),
            jnp.stack([pick(src_below[t], wide + plane_count, wide) for t in range(block_count)], axis=1),
        ],
        axis=0,
    )
    wide_planes = plane_start - wide + jnp.arange(wide_count, dtype=jnp.int32)
    wide_inside = (wide_planes >= 0) & (wide_planes < total_planes)
    camera_ext = camera_ext.reshape(wide_count, row_count, lane_count)
    band_pad = jnp.pad(band_all, wide, mode="edge")
    band_wide = lax.dynamic_slice_in_dim(band_pad, plane_start, wide_count)
    band_ids = jnp.arange(kernels.shape[0], dtype=jnp.int32)
    in_band = band_wide[None, :] == band_ids[:, None]
    tables = jnp.sum(jnp.where(in_band[:, None, None, :], kernels[:, :, :, None], 0.0), axis=0)
    x_wide = tables[2]
    y_wide = tables[1]
    lateral_ext = lateral_fwd(camera_ext, x_wide, y_wide)
    lateral_ext = jnp.where(wide_inside[:, None, None], lateral_ext, 0.0)
    ext_count = plane_count + 2 * reach
    ext_planes = plane_start - reach + jnp.arange(ext_count, dtype=jnp.int32)
    ext_inside = (ext_planes >= 0) & (ext_planes < total_planes)
    taps_ext = tables[0][:, reach : reach + ext_count]
    blurred = jnp.zeros((ext_count, row_count, lane_count), jnp.float32)
    for j in range(2 * reach + 1):
        blurred = blurred + taps_ext[j][:, None, None] * lateral_ext[j : j + ext_count]
    observed_ext = extended_2(observed[0], (("dom", 0),), reach)
    ratio_ext = jnp.where(ext_inside[:, None, None], observed_ext / blurred, 0.0)
    x_own = tables[2][:, wide : wide + plane_count]
    y_own = tables[1][:, wide : wide + plane_count]
    zback = jnp.zeros((plane_count, row_count, lane_count), jnp.float32)
    for m in range(2 * reach + 1):
        zback = zback + taps_ext[2 * reach - m, m : m + plane_count][:, None, None] * ratio_ext[m : m + plane_count]
    dest_slot = jnp.sum(
        jnp.where(my_sources[None, :] == slot_ids[:, None], slot_ids[None, :], 0), axis=1
    )
    row_ids = jnp.arange(block_rows, dtype=jnp.int32)
    out_rows = (dest_slot[:, None] * block_rows + row_ids[None, :]).reshape(row_count)
    offset = out_rows[:, None] - jnp.arange(row_count, dtype=jnp.int32)[None, :]
    mix = jnp.zeros((plane_count, row_count, row_count), jnp.float32)
    for tap in range(2 * reach + 1):
        mix = mix + jnp.where((offset == tap - reach)[None], y_own[tap][:, None, None], 0.0)
    by_source = jnp.einsum("pri,pix->prx", mix, zback, precision=lax.Precision.HIGHEST)
    back = taps_along(by_source, x_own, 2, True)
    piece_planes = plane_count // view_count
    logs = jnp.log(back).reshape(view_count, piece_planes, block_count, block_rows, lane_count)
    outgoing = logs.transpose(0, 2, 1, 3, 4).reshape(view_count * block_count, piece_planes, block_rows, lane_count)
    arrived_logs = lax.all_to_all(outgoing, ("view", "dom"), 0, 0, tiled=True)
    all_grid = src_map.reshape(view_count, block_count, block_count)
    all_dev = all_grid // block_count
    all_slot = all_grid % block_count
    slot_of = jnp.sum(jnp.where(all_dev == dom_index, all_slot, 0), axis=2)
    cam_of = jnp.sum(
        jnp.where(slot_of[:, :, None] == slot_ids[None, None, :], slot_ids[None, :, None], 0), axis=1
    )
    flat_index = (view_ids[:, None] * block_count + cam_of).reshape(-1)
    by_view = jnp.take(arrived_logs, flat_index, axis=0, mode="clip")
    by_view = by_view.reshape(view_count, block_count, piece_planes, block_rows, lane_count)
    log_total = by_view[0]
    for v in range(1, view_count):
        log_total = log_total + by_view[v]
    log_total = log_total.transpose(1, 0, 2, 3).reshape(piece_planes, row_count, lane_count)
    log_joined = lax.all_gather(log_total, "view", axis=0, tiled=True)
    return estimate * jnp.exp(log_joined / view_count)


def solution(mesh):
    in_specs = (
        P(("tile", "dom"), None, None),
        P("view", ("tile", "dom"), None, None),
        P("view", None, None, None),
        P(),
        P("view", None),
    )
    out_specs = P(("tile", "dom"), None, None)
    return jax.shard_map(body, mesh=mesh, in_specs=in_specs, out_specs=out_specs, check_vma=False)
```

```python
import jax
import jax.numpy as jnp
from jax import lax
from jax.sharding import PartitionSpec as P

RADIUS = 4


precise = lax.Precision.HIGHEST


def extended_2(shard, sides, width):
    for axis, dim in sides:
        size, length = (lax.axis_size(axis), shard.shape[dim])
        up = [(i, (i + 1) % size) for i in range(size - 1)]
        down = [(j, i) for i, j in up]
        last = lax.slice_in_dim(shard, length - width, length, axis=dim)
        initial = lax.slice_in_dim(shard, 0, width, axis=dim)
        before = lax.ppermute(last, axis, up)
        after = lax.ppermute(initial, axis, down)
        shard = jnp.concatenate([before, shard, after], axis=dim)
    return shard


def taps_along(field, taps, axis, flipped):
    tap_count = taps.shape[0]
    reach = (tap_count - 1) // 2
    length = field.shape[axis]
    widths = [(0, 0), (0, 0), (0, 0)]
    widths[axis] = (reach, reach)
    padded = jnp.pad(field, widths)
    total = jnp.zeros(field.shape, jnp.float32)
    for offset in range(tap_count):
        start = 2 * reach - offset if flipped else offset
        piece = lax.slice_in_dim(padded, start, start + length, axis=axis)
        total = total + taps[offset][:, None, None] * piece
    return total


def lateral_fwd(field, x_taps, y_taps):
    inner = taps_along(field, x_taps, 2, False)
    return taps_along(inner, y_taps, 1, False)


def body(estimate, observed, psf, src_map, depth_band):
    plane_count, row_count, lane_count = estimate.shape
    block_count = lax.axis_size("dom")
    block_rows = row_count // block_count
    dom_index = lax.axis_index("dom")
    view_index = lax.axis_index("view")
    view_count = lax.axis_size("view")
    plane_start = dom_index * plane_count
    slot_ids = jnp.arange(block_count, dtype=jnp.int32)
    view_ids = jnp.arange(view_count, dtype=jnp.int32)
    my_map = jnp.sum(jnp.where((view_ids == view_index)[:, None], src_map, 0), axis=0)
    grid_map = my_map.reshape(block_count, block_count)
    source_dev = grid_map // block_count
    source_slot = grid_map % block_count
    near_rows = jnp.stack(
        [
            jnp.concatenate([grid_map[:1], grid_map[:-1]], axis=0),
            grid_map,
            jnp.concatenate([grid_map[1:], grid_map[-1:]], axis=0),
        ]
    )
    near_slots = jnp.sum(
        jnp.where(near_rows // block_count == dom_index, near_rows % block_count, 0), axis=2
    )
    above, send_slot, below = near_slots[0], near_slots[1], near_slots[2]
    kernels = psf[0]
    band_all = depth_band[0]
    total_planes = band_all.shape[0]
    reach = (kernels.shape[2] - 1) // 2
    wide = 2 * reach
    last = block_count - 1
    wide_count = plane_count + 2 * wide
    chunk_plane = jnp.arange(wide_count, dtype=jnp.int32)
    in_top = chunk_plane < wide
    in_bottom = chunk_plane >= wide + plane_count
    source_plane = jnp.where(
        in_top, chunk_plane + plane_count - wide,
        jnp.where(in_bottom, chunk_plane - wide - plane_count, chunk_plane - wide),
    )
    source_block = jnp.where(
        in_top[:, None], above[None, :], jnp.where(in_bottom[:, None], below[None, :], send_slot[None, :])
    )
    send_index = (source_plane[None, :] * block_count + source_block.T).reshape(-1)
    flat_blocks = estimate.reshape(plane_count * block_count, block_rows, lane_count)
    outgoing = jnp.take(flat_blocks, send_index, axis=0, mode="clip")
    outgoing = outgoing.reshape(block_count * wide_count, block_rows, lane_count)
    arrived = lax.all_to_all(outgoing, "dom", split_axis=0, concat_axis=0, tiled=True)
    my_sources = lax.dynamic_index_in_dim(source_dev, dom_index, 0, keepdims=False)
    src_above = lax.dynamic_index_in_dim(source_dev, jnp.maximum(dom_index - 1, 0), 0, keepdims=False)
    src_below = lax.dynamic_index_in_dim(source_dev, jnp.minimum(dom_index + 1, last), 0, keepdims=False)
    from_block = jnp.where(
        in_top[:, None], src_above[None, :], jnp.where(in_bottom[:, None], src_below[None, :], my_sources[None, :])
    )
    recv_index = (from_block * wide_count + chunk_plane[:, None]).reshape(-1)
    camera_ext = jnp.take(arrived, recv_index, axis=0, mode="clip")
    camera_ext = camera_ext.reshape(wide_count, block_count, block_rows, lane_count)
    wide_planes = plane_start - wide + jnp.arange(wide_count, dtype=jnp.int32)
    wide_inside = (wide_planes >= 0) & (wide_planes < total_planes)
    camera_ext = camera_ext.reshape(wide_count, row_count, lane_count)
    band_pad = jnp.pad(band_all, wide, mode="edge")
    band_wide = lax.dynamic_slice_in_dim(band_pad, plane_start, wide_count)
    band_ids = jnp.arange(kernels.shape[0], dtype=jnp.int32)
    in_band = band_wide[None, :] == band_ids[:, None]
    tables = jnp.sum(jnp.where(in_band[:, None, None, :], kernels[:, :, :, None], 0.0), axis=0)
    x_wide = tables[2]
    y_wide = tables[1]
    lateral_ext = lateral_fwd(camera_ext, x_wide, y_wide)
    ext_count = plane_count + 2 * reach
    ext_planes = plane_start - reach + jnp.arange(ext_count, dtype=jnp.int32)
    ext_inside = (ext_planes >= 0) & (ext_planes < total_planes)
    taps_ext = tables[0][:, reach : reach + ext_count]
    blurred = jnp.zeros((ext_count, row_count, lane_count), jnp.float32)
    for j in range(2 * reach + 1):
        weight = jnp.where(wide_inside[j : j + ext_count], taps_ext[j], 0.0)
        blurred = blurred + weight[:, None, None] * lateral_ext[j : j + ext_count]
    observed_ext = extended_2(observed[0], (("dom", 0),), reach)
    ratio_ext = jnp.where(ext_inside[:, None, None], observed_ext / blurred, 0.0)
    x_own = tables[2][:, wide : wide + plane_count]
    y_own = tables[1][:, wide : wide + plane_count]
    zback = jnp.zeros((plane_count, row_count, lane_count), jnp.float32)
    for m in range(2 * reach + 1):
        zback = zback + taps_ext[2 * reach - m, m : m + plane_count][:, None, None] * ratio_ext[m : m + plane_count]
    dest_slot = jnp.sum(
        jnp.where(my_sources[None, :] == slot_ids[:, None], slot_ids[None, :], 0), axis=1
    )
    row_ids = jnp.arange(block_rows, dtype=jnp.int32)
    out_rows = (dest_slot[:, None] * block_rows + row_ids[None, :]).reshape(row_count)
    offset = out_rows[:, None] - jnp.arange(row_count, dtype=jnp.int32)[None, :]
    mix = jnp.zeros((plane_count, row_count, row_count), jnp.float32)
    for tap in range(2 * reach + 1):
        mix = mix + jnp.where((offset == tap - reach)[None], y_own[tap][:, None, None], 0.0)
    by_source = jnp.einsum("pri,pix->prx", mix, zback, precision=lax.Precision.HIGHEST)
    back = taps_along(by_source, x_own, 2, True)
    piece_planes = plane_count // view_count
    logs = jnp.log(back).reshape(view_count, piece_planes, block_count, block_rows, lane_count)
    outgoing = logs.transpose(0, 2, 1, 3, 4).reshape(view_count * block_count, piece_planes, block_rows, lane_count)
    arrived_logs = lax.all_to_all(outgoing, ("view", "dom"), 0, 0, tiled=True)
    all_grid = src_map.reshape(view_count, block_count, block_count)
    all_dev = all_grid // block_count
    all_slot = all_grid % block_count
    slot_of = jnp.sum(jnp.where(all_dev == dom_index, all_slot, 0), axis=2)
    cam_of = jnp.sum(
        jnp.where(slot_of[:, :, None] == slot_ids[None, None, :], slot_ids[None, :, None], 0), axis=1
    )
    flat_index = (view_ids[:, None] * block_count + cam_of).reshape(-1)
    by_view = jnp.take(arrived_logs, flat_index, axis=0, mode="clip")
    by_view = by_view.reshape(view_count, block_count, piece_planes, block_rows, lane_count)
    log_total = by_view[0]
    for v in range(1, view_count):
        log_total = log_total + by_view[v]
    log_total = log_total.transpose(1, 0, 2, 3).reshape(piece_planes, row_count, lane_count)
    log_joined = lax.all_gather(log_total, "view", axis=0, tiled=True)
    return estimate * jnp.exp(log_joined / view_count)


def solution(mesh):
    in_specs = (
        P(("tile", "dom"), None, None),
        P("view", ("tile", "dom"), None, None),
        P("view", None, None, None),
        P(),
        P("view", None),
    )
    out_specs = P(("tile", "dom"), None, None)
    return jax.shard_map(body, mesh=mesh, in_specs=in_specs, out_specs=out_specs, check_vma=False)
```

```python
import jax
import jax.numpy as jnp
from jax import lax
from jax.sharding import PartitionSpec as P

RADIUS = 4


precise = lax.Precision.HIGHEST


def extended_2(shard, sides, width):
    for axis, dim in sides:
        size, length = (lax.axis_size(axis), shard.shape[dim])
        up = [(i, (i + 1) % size) for i in range(size - 1)]
        down = [(j, i) for i, j in up]
        last = lax.slice_in_dim(shard, length - width, length, axis=dim)
        initial = lax.slice_in_dim(shard, 0, width, axis=dim)
        before = lax.ppermute(last, axis, up)
        after = lax.ppermute(initial, axis, down)
        shard = jnp.concatenate([before, shard, after], axis=dim)
    return shard


def taps_along(field, taps, axis, flipped):
    tap_count = taps.shape[0]
    reach = (tap_count - 1) // 2
    length = field.shape[axis]
    widths = [(0, 0), (0, 0), (0, 0)]
    widths[axis] = (reach, reach)
    padded = jnp.pad(field, widths)
    total = jnp.zeros(field.shape, jnp.float32)
    for offset in range(tap_count):
        start = 2 * reach - offset if flipped else offset
        piece = lax.slice_in_dim(padded, start, start + length, axis=axis)
        total = total + taps[offset][:, None, None] * piece
    return total


def lateral_fwd(field, x_taps, y_taps):
    inner = taps_along(field, x_taps, 2, False)
    return taps_along(inner, y_taps, 1, False)


def body(estimate, observed, psf, src_map, depth_band):
    plane_count, row_count, lane_count = estimate.shape
    block_count = lax.axis_size("dom")
    block_rows = row_count // block_count
    dom_index = lax.axis_index("dom")
    view_index = lax.axis_index("view")
    view_count = lax.axis_size("view")
    plane_start = dom_index * plane_count
    slot_ids = jnp.arange(block_count, dtype=jnp.int32)
    view_ids = jnp.arange(view_count, dtype=jnp.int32)
    my_map = jnp.sum(jnp.where((view_ids == view_index)[:, None], src_map, 0), axis=0)
    grid_map = my_map.reshape(block_count, block_count)
    source_dev = grid_map // block_count
    source_slot = grid_map % block_count
    near_rows = jnp.stack(
        [
            jnp.concatenate([grid_map[:1], grid_map[:-1]], axis=0),
            grid_map,
            jnp.concatenate([grid_map[1:], grid_map[-1:]], axis=0),
        ]
    )
    near_slots = jnp.sum(
        jnp.where(near_rows // block_count == dom_index, near_rows % block_count, 0), axis=2
    )
    above, send_slot, below = near_slots[0], near_slots[1], near_slots[2]
    kernels = psf[0]
    band_all = depth_band[0]
    total_planes = band_all.shape[0]
    reach = (kernels.shape[2] - 1) // 2
    wide = 2 * reach
    last = block_count - 1
    wide_count = plane_count + 2 * wide
    chunk_plane = jnp.arange(wide_count, dtype=jnp.int32)
    in_top = chunk_plane < wide
    in_bottom = chunk_plane >= wide + plane_count
    source_plane = jnp.where(
        in_top, chunk_plane + plane_count - wide,
        jnp.where(in_bottom, chunk_plane - wide - plane_count, chunk_plane - wide),
    )
    source_block = jnp.where(
        in_top[:, None], above[None, :], jnp.where(in_bottom[:, None], below[None, :], send_slot[None, :])
    )
    piece_count = wide_count // wide
    piece_first = source_plane[::wide]
    piece_block = source_block[::wide].T
    starts = jnp.stack(
        [jnp.broadcast_to(piece_first[None, :], piece_block.shape), piece_block], axis=-1
    ).reshape(block_count * piece_count, 2)
    numbers = lax.GatherDimensionNumbers(
        offset_dims=(1, 2, 3), collapsed_slice_dims=(1,), start_index_map=(0, 1)
    )
    blocks = estimate.reshape(plane_count, block_count, block_rows, lane_count)
    outgoing = lax.gather(
        blocks, starts, numbers, (wide, 1, block_rows, lane_count), mode=lax.GatherScatterMode.CLIP
    )
    outgoing = outgoing.reshape(block_count * wide_count, block_rows, lane_count)
    arrived = lax.all_to_all(outgoing, "dom", split_axis=0, concat_axis=0, tiled=True)
    my_sources = lax.dynamic_index_in_dim(source_dev, dom_index, 0, keepdims=False)
    src_above = lax.dynamic_index_in_dim(source_dev, jnp.maximum(dom_index - 1, 0), 0, keepdims=False)
    src_below = lax.dynamic_index_in_dim(source_dev, jnp.minimum(dom_index + 1, last), 0, keepdims=False)
    from_block = jnp.where(
        in_top[:, None], src_above[None, :], jnp.where(in_bottom[:, None], src_below[None, :], my_sources[None, :])
    )
    recv_index = (from_block * wide_count + chunk_plane[:, None]).reshape(-1)
    camera_ext = jnp.take(arrived, recv_index, axis=0, mode="clip")
    camera_ext = camera_ext.reshape(wide_count, block_count, block_rows, lane_count)
    wide_planes = plane_start - wide + jnp.arange(wide_count, dtype=jnp.int32)
    wide_inside = (wide_planes >= 0) & (wide_planes < total_planes)
    camera_ext = camera_ext.reshape(wide_count, row_count, lane_count)
    band_pad = jnp.pad(band_all, wide, mode="edge")
    band_wide = lax.dynamic_slice_in_dim(band_pad, plane_start, wide_count)
    band_ids = jnp.arange(kernels.shape[0], dtype=jnp.int32)
    in_band = band_wide[None, :] == band_ids[:, None]
    tables = jnp.sum(jnp.where(in_band[:, None, None, :], kernels[:, :, :, None], 0.0), axis=0)
    x_wide = tables[2]
    y_wide = tables[1]
    lateral_ext = lateral_fwd(camera_ext, x_wide, y_wide)
    ext_count = plane_count + 2 * reach
    ext_planes = plane_start - reach + jnp.arange(ext_count, dtype=jnp.int32)
    ext_inside = (ext_planes >= 0) & (ext_planes < total_planes)
    taps_ext = tables[0][:, reach : reach + ext_count]
    blurred = jnp.zeros((ext_count, row_count, lane_count), jnp.float32)
    for j in range(2 * reach + 1):
        weight = jnp.where(wide_inside[j : j + ext_count], taps_ext[j], 0.0)
        blurred = blurred + weight[:, None, None] * lateral_ext[j : j + ext_count]
    observed_ext = extended_2(observed[0], (("dom", 0),), reach)
    ratio_ext = jnp.where(ext_inside[:, None, None], observed_ext / blurred, 0.0)
    x_own = tables[2][:, wide : wide + plane_count]
    y_own = tables[1][:, wide : wide + plane_count]
    zback = jnp.zeros((plane_count, row_count, lane_count), jnp.float32)
    for m in range(2 * reach + 1):
        zback = zback + taps_ext[2 * reach - m, m : m + plane_count][:, None, None] * ratio_ext[m : m + plane_count]
    dest_slot = jnp.sum(
        jnp.where(my_sources[None, :] == slot_ids[:, None], slot_ids[None, :], 0), axis=1
    )
    row_ids = jnp.arange(block_rows, dtype=jnp.int32)
    out_rows = (dest_slot[:, None] * block_rows + row_ids[None, :]).reshape(row_count)
    offset = out_rows[:, None] - jnp.arange(row_count, dtype=jnp.int32)[None, :]
    mix = jnp.zeros((plane_count, row_count, row_count), jnp.float32)
    for tap in range(2 * reach + 1):
        mix = mix + jnp.where((offset == tap - reach)[None], y_own[tap][:, None, None], 0.0)
    by_source = jnp.einsum("pri,pix->prx", mix, zback, precision=lax.Precision.HIGHEST)
    back = taps_along(by_source, x_own, 2, True)
    piece_planes = plane_count // view_count
    logs = jnp.log(back).reshape(view_count, piece_planes, block_count, block_rows, lane_count)
    outgoing = logs.transpose(0, 2, 1, 3, 4).reshape(view_count * block_count, piece_planes, block_rows, lane_count)
    arrived_logs = lax.all_to_all(outgoing, ("view", "dom"), 0, 0, tiled=True)
    all_grid = src_map.reshape(view_count, block_count, block_count)
    all_dev = all_grid // block_count
    all_slot = all_grid % block_count
    slot_of = jnp.sum(jnp.where(all_dev == dom_index, all_slot, 0), axis=2)
    cam_of = jnp.sum(
        jnp.where(slot_of[:, :, None] == slot_ids[None, None, :], slot_ids[None, :, None], 0), axis=1
    )
    flat_index = (view_ids[:, None] * block_count + cam_of).reshape(-1)
    by_view = jnp.take(arrived_logs, flat_index, axis=0, mode="clip")
    by_view = by_view.reshape(view_count, block_count, piece_planes, block_rows, lane_count)
    log_total = by_view[0]
    for v in range(1, view_count):
        log_total = log_total + by_view[v]
    log_total = log_total.transpose(1, 0, 2, 3).reshape(piece_planes, row_count, lane_count)
    log_joined = lax.all_gather(log_total, "view", axis=0, tiled=True)
    return estimate * jnp.exp(log_joined / view_count)


def solution(mesh):
    in_specs = (
        P(("tile", "dom"), None, None),
        P("view", ("tile", "dom"), None, None),
        P("view", None, None, None),
        P(),
        P("view", None),
    )
    out_specs = P(("tile", "dom"), None, None)
    return jax.shard_map(body, mesh=mesh, in_specs=in_specs, out_specs=out_specs, check_vma=False)
```

```python
import jax
import jax.numpy as jnp
from jax import lax
from jax.sharding import PartitionSpec as P

RADIUS = 4


precise = lax.Precision.HIGHEST


def extended_2(shard, sides, width):
    for axis, dim in sides:
        size, length = (lax.axis_size(axis), shard.shape[dim])
        up = [(i, (i + 1) % size) for i in range(size - 1)]
        down = [(j, i) for i, j in up]
        last = lax.slice_in_dim(shard, length - width, length, axis=dim)
        initial = lax.slice_in_dim(shard, 0, width, axis=dim)
        before = lax.ppermute(last, axis, up)
        after = lax.ppermute(initial, axis, down)
        shard = jnp.concatenate([before, shard, after], axis=dim)
    return shard


def taps_along(field, taps, axis, flipped):
    tap_count = taps.shape[0]
    reach = (tap_count - 1) // 2
    length = field.shape[axis]
    widths = [(0, 0), (0, 0), (0, 0)]
    widths[axis] = (reach, reach)
    padded = jnp.pad(field, widths)
    total = jnp.zeros(field.shape, jnp.float32)
    for offset in range(tap_count):
        start = 2 * reach - offset if flipped else offset
        piece = lax.slice_in_dim(padded, start, start + length, axis=axis)
        total = total + taps[offset][:, None, None] * piece
    return total


def lateral_fwd(field, x_taps, y_taps):
    inner = taps_along(field, x_taps, 2, False)
    return taps_along(inner, y_taps, 1, False)


def body(estimate, observed, psf, src_map, depth_band):
    plane_count, row_count, lane_count = estimate.shape
    block_count = lax.axis_size("dom")
    block_rows = row_count // block_count
    dom_index = lax.axis_index("dom")
    view_index = lax.axis_index("view")
    view_count = lax.axis_size("view")
    plane_start = dom_index * plane_count
    slot_ids = jnp.arange(block_count, dtype=jnp.int32)
    view_ids = jnp.arange(view_count, dtype=jnp.int32)
    my_map = jnp.sum(jnp.where((view_ids == view_index)[:, None], src_map, 0), axis=0)
    grid_map = my_map.reshape(block_count, block_count)
    source_dev = grid_map // block_count
    source_slot = grid_map % block_count
    near_rows = jnp.stack(
        [
            jnp.concatenate([grid_map[:1], grid_map[:-1]], axis=0),
            grid_map,
            jnp.concatenate([grid_map[1:], grid_map[-1:]], axis=0),
        ]
    )
    near_slots = jnp.sum(
        jnp.where(near_rows // block_count == dom_index, near_rows % block_count, 0), axis=2
    )
    above, send_slot, below = near_slots[0], near_slots[1], near_slots[2]
    kernels = psf[0]
    band_all = depth_band[0]
    total_planes = band_all.shape[0]
    reach = (kernels.shape[2] - 1) // 2
    wide = reach
    last = block_count - 1
    wide_count = plane_count + 2 * wide
    chunk_plane = jnp.arange(wide_count, dtype=jnp.int32)
    in_top = chunk_plane < wide
    in_bottom = chunk_plane >= wide + plane_count
    source_plane = jnp.where(
        in_top, chunk_plane + plane_count - wide,
        jnp.where(in_bottom, chunk_plane - wide - plane_count, chunk_plane - wide),
    )
    source_block = jnp.where(
        in_top[:, None], above[None, :], jnp.where(in_bottom[:, None], below[None, :], send_slot[None, :])
    )
    send_index = (source_plane[None, :] * block_count + source_block.T).reshape(-1)
    flat_blocks = estimate.reshape(plane_count * block_count, block_rows, lane_count)
    outgoing = jnp.take(flat_blocks, send_index, axis=0, mode="clip")
    outgoing = outgoing.reshape(block_count * wide_count, block_rows, lane_count)
    arrived = lax.all_to_all(outgoing, "dom", split_axis=0, concat_axis=0, tiled=True)
    my_sources = lax.dynamic_index_in_dim(source_dev, dom_index, 0, keepdims=False)
    src_above = lax.dynamic_index_in_dim(source_dev, jnp.maximum(dom_index - 1, 0), 0, keepdims=False)
    src_below = lax.dynamic_index_in_dim(source_dev, jnp.minimum(dom_index + 1, last), 0, keepdims=False)
    from_block = jnp.where(
        in_top[:, None], src_above[None, :], jnp.where(in_bottom[:, None], src_below[None, :], my_sources[None, :])
    )
    recv_index = (from_block * wide_count + chunk_plane[:, None]).reshape(-1)
    camera_ext = jnp.take(arrived, recv_index, axis=0, mode="clip")
    camera_ext = camera_ext.reshape(wide_count, block_count, block_rows, lane_count)
    wide_planes = plane_start - wide + jnp.arange(wide_count, dtype=jnp.int32)
    wide_inside = (wide_planes >= 0) & (wide_planes < total_planes)
    camera_ext = camera_ext.reshape(wide_count, row_count, lane_count)
    band_pad = jnp.pad(band_all, wide, mode="edge")
    band_wide = lax.dynamic_slice_in_dim(band_pad, plane_start, wide_count)
    band_ids = jnp.arange(kernels.shape[0], dtype=jnp.int32)
    in_band = band_wide[None, :] == band_ids[:, None]
    tables = jnp.sum(jnp.where(in_band[:, None, None, :], kernels[:, :, :, None], 0.0), axis=0)
    x_wide = tables[2]
    y_wide = tables[1]
    lateral_ext = lateral_fwd(camera_ext, x_wide, y_wide)
    taps_own = tables[0][:, wide : wide + plane_count]
    blurred = jnp.zeros((plane_count, row_count, lane_count), jnp.float32)
    for j in range(2 * reach + 1):
        weight = jnp.where(wide_inside[j : j + plane_count], taps_own[j], 0.0)
        blurred = blurred + weight[:, None, None] * lateral_ext[j : j + plane_count]
    ratio_field = observed[0] / blurred
    ratio_ext = extended_2(ratio_field, (("dom", 0),), reach)
    taps_ext = tables[0]
    x_own = tables[2][:, wide : wide + plane_count]
    y_own = tables[1][:, wide : wide + plane_count]
    zback = jnp.zeros((plane_count, row_count, lane_count), jnp.float32)
    for m in range(2 * reach + 1):
        zback = zback + taps_ext[2 * reach - m, m : m + plane_count][:, None, None] * ratio_ext[m : m + plane_count]
    dest_slot = jnp.sum(
        jnp.where(my_sources[None, :] == slot_ids[:, None], slot_ids[None, :], 0), axis=1
    )
    row_ids = jnp.arange(block_rows, dtype=jnp.int32)
    out_rows = (dest_slot[:, None] * block_rows + row_ids[None, :]).reshape(row_count)
    offset = out_rows[:, None] - jnp.arange(row_count, dtype=jnp.int32)[None, :]
    mix = jnp.zeros((plane_count, row_count, row_count), jnp.float32)
    for tap in range(2 * reach + 1):
        mix = mix + jnp.where((offset == tap - reach)[None], y_own[tap][:, None, None], 0.0)
    by_source = jnp.einsum("pri,pix->prx", mix, zback, precision=lax.Precision.HIGHEST)
    back = taps_along(by_source, x_own, 2, True)
    piece_planes = plane_count // view_count
    logs = jnp.log(back).reshape(view_count, piece_planes, block_count, block_rows, lane_count)
    outgoing = logs.transpose(0, 2, 1, 3, 4).reshape(view_count * block_count, piece_planes, block_rows, lane_count)
    arrived_logs = lax.all_to_all(outgoing, ("view", "dom"), 0, 0, tiled=True)
    all_grid = src_map.reshape(view_count, block_count, block_count)
    all_dev = all_grid // block_count
    all_slot = all_grid % block_count
    slot_of = jnp.sum(jnp.where(all_dev == dom_index, all_slot, 0), axis=2)
    cam_of = jnp.sum(
        jnp.where(slot_of[:, :, None] == slot_ids[None, None, :], slot_ids[None, :, None], 0), axis=1
    )
    flat_index = (view_ids[:, None] * block_count + cam_of).reshape(-1)
    by_view = jnp.take(arrived_logs, flat_index, axis=0, mode="clip")
    by_view = by_view.reshape(view_count, block_count, piece_planes, block_rows, lane_count)
    log_total = by_view[0]
    for v in range(1, view_count):
        log_total = log_total + by_view[v]
    log_total = log_total.transpose(1, 0, 2, 3).reshape(piece_planes, row_count, lane_count)
    log_joined = lax.all_gather(log_total, "view", axis=0, tiled=True)
    return estimate * jnp.exp(log_joined / view_count)


def solution(mesh):
    in_specs = (
        P(("tile", "dom"), None, None),
        P("view", ("tile", "dom"), None, None),
        P("view", None, None, None),
        P(),
        P("view", None),
    )
    out_specs = P(("tile", "dom"), None, None)
    return jax.shard_map(body, mesh=mesh, in_specs=in_specs, out_specs=out_specs, check_vma=False)
```

```python
import jax
import jax.numpy as jnp
from jax import lax
from jax.sharding import PartitionSpec as P

RADIUS = 4


precise = lax.Precision.HIGHEST


def extended_2(shard, sides, width):
    for axis, dim in sides:
        size, length = (lax.axis_size(axis), shard.shape[dim])
        up = [(i, (i + 1) % size) for i in range(size - 1)]
        down = [(j, i) for i, j in up]
        last = lax.slice_in_dim(shard, length - width, length, axis=dim)
        initial = lax.slice_in_dim(shard, 0, width, axis=dim)
        before = lax.ppermute(last, axis, up)
        after = lax.ppermute(initial, axis, down)
        shard = jnp.concatenate([before, shard, after], axis=dim)
    return shard


def taps_along(field, taps, axis, flipped):
    tap_count = taps.shape[0]
    reach = (tap_count - 1) // 2
    length = field.shape[axis]
    widths = [(0, 0), (0, 0), (0, 0)]
    widths[axis] = (reach, reach)
    padded = jnp.pad(field, widths)
    total = jnp.zeros(field.shape, jnp.float32)
    for offset in range(tap_count):
        start = 2 * reach - offset if flipped else offset
        piece = lax.slice_in_dim(padded, start, start + length, axis=axis)
        total = total + taps[offset][:, None, None] * piece
    return total


def lateral_fwd(field, x_taps, y_taps):
    inner = taps_along(field, x_taps, 2, False)
    return taps_along(inner, y_taps, 1, False)


def body(estimate, observed, psf, src_map, depth_band):
    plane_count, row_count, lane_count = estimate.shape
    block_count = lax.axis_size("dom")
    block_rows = row_count // block_count
    dom_index = lax.axis_index("dom")
    view_index = lax.axis_index("view")
    view_count = lax.axis_size("view")
    plane_start = dom_index * plane_count
    slot_ids = jnp.arange(block_count, dtype=jnp.int32)
    view_ids = jnp.arange(view_count, dtype=jnp.int32)
    my_map = jnp.sum(jnp.where((view_ids == view_index)[:, None], src_map, 0), axis=0)
    grid_map = my_map.reshape(block_count, block_count)
    source_dev = grid_map // block_count
    source_slot = grid_map % block_count
    near_rows = jnp.stack(
        [
            jnp.concatenate([grid_map[:1], grid_map[:-1]], axis=0),
            grid_map,
            jnp.concatenate([grid_map[1:], grid_map[-1:]], axis=0),
        ]
    )
    near_slots = jnp.sum(
        jnp.where(near_rows // block_count == dom_index, near_rows % block_count, 0), axis=2
    )
    above, send_slot, below = near_slots[0], near_slots[1], near_slots[2]
    kernels = psf[0]
    band_all = depth_band[0]
    total_planes = band_all.shape[0]
    reach = (kernels.shape[2] - 1) // 2
    wide = 2 * reach
    last = block_count - 1
    wide_count = plane_count + 2 * wide
    chunk_plane = jnp.arange(wide_count, dtype=jnp.int32)
    in_top = chunk_plane < wide
    in_bottom = chunk_plane >= wide + plane_count
    source_plane = jnp.where(
        in_top, chunk_plane + plane_count - wide,
        jnp.where(in_bottom, chunk_plane - wide - plane_count, chunk_plane - wide),
    )
    source_block = jnp.where(
        in_top[:, None], above[None, :], jnp.where(in_bottom[:, None], below[None, :], send_slot[None, :])
    )
    send_index = (source_plane[None, :] * block_count + source_block.T).reshape(-1)
    flat_blocks = estimate.reshape(plane_count * block_count, block_rows, lane_count)
    outgoing = jnp.take(flat_blocks, send_index, axis=0, mode="clip")
    outgoing = outgoing.reshape(block_count * wide_count, block_rows, lane_count)
    arrived = lax.all_to_all(outgoing, "dom", split_axis=0, concat_axis=0, tiled=True)
    my_sources = lax.dynamic_index_in_dim(source_dev, dom_index, 0, keepdims=False)
    src_above = lax.dynamic_index_in_dim(source_dev, jnp.maximum(dom_index - 1, 0), 0, keepdims=False)
    src_below = lax.dynamic_index_in_dim(source_dev, jnp.minimum(dom_index + 1, last), 0, keepdims=False)
    from_block = jnp.where(
        in_top[:, None], src_above[None, :], jnp.where(in_bottom[:, None], src_below[None, :], my_sources[None, :])
    )
    inverse = jnp.sum(
        jnp.where(from_block[:, :, None] == slot_ids[None, None, :], slot_ids[None, :, None], 0), axis=1
    )
    arrived = arrived.reshape(block_count, wide_count, block_rows, lane_count)
    wide_planes = plane_start - wide + jnp.arange(wide_count, dtype=jnp.int32)
    wide_inside = (wide_planes >= 0) & (wide_planes < total_planes)
    band_pad = jnp.pad(band_all, wide, mode="edge")
    band_wide = lax.dynamic_slice_in_dim(band_pad, plane_start, wide_count)
    band_ids = jnp.arange(kernels.shape[0], dtype=jnp.int32)
    in_band = band_wide[None, :] == band_ids[:, None]
    tables = jnp.sum(jnp.where(in_band[:, None, None, :], kernels[:, :, :, None], 0.0), axis=0)
    x_wide = tables[2]
    y_wide = tables[1]
    padded = jnp.pad(arrived, [(0, 0), (0, 0), (0, 0), (reach, reach)])
    lanes_done = jnp.zeros(arrived.shape, jnp.float32)
    for tap in range(2 * reach + 1):
        lanes_done = lanes_done + x_wide[tap][None, :, None, None] * padded[..., tap : tap + lane_count]
    row_ids = jnp.arange(block_rows, dtype=jnp.int32)
    in_rows = inverse[:, :, None] * block_rows + row_ids[None, None, :]
    offset = in_rows[:, None, :, :] - jnp.arange(row_count, dtype=jnp.int32)[None, :, None, None]
    mix = jnp.zeros((wide_count, row_count, block_count, block_rows), jnp.float32)
    for tap in range(2 * reach + 1):
        mix = mix + jnp.where(offset == tap - reach, y_wide[tap][:, None, None, None], 0.0)
    lateral_ext = jnp.einsum("prsk,spkx->prx", mix, lanes_done, precision=lax.Precision.HIGHEST)
    ext_count = plane_count + 2 * reach
    ext_planes = plane_start - reach + jnp.arange(ext_count, dtype=jnp.int32)
    ext_inside = (ext_planes >= 0) & (ext_planes < total_planes)
    taps_ext = tables[0][:, reach : reach + ext_count]
    blurred = jnp.zeros((ext_count, row_count, lane_count), jnp.float32)
    for j in range(2 * reach + 1):
        weight = jnp.where(wide_inside[j : j + ext_count], taps_ext[j], 0.0)
        blurred = blurred + weight[:, None, None] * lateral_ext[j : j + ext_count]
    observed_ext = extended_2(observed[0], (("dom", 0),), reach)
    ratio_ext = jnp.where(ext_inside[:, None, None], observed_ext / blurred, 0.0)
    x_own = tables[2][:, wide : wide + plane_count]
    y_own = tables[1][:, wide : wide + plane_count]
    zback = jnp.zeros((plane_count, row_count, lane_count), jnp.float32)
    for m in range(2 * reach + 1):
        zback = zback + taps_ext[2 * reach - m, m : m + plane_count][:, None, None] * ratio_ext[m : m + plane_count]
    dest_slot = jnp.sum(
        jnp.where(my_sources[None, :] == slot_ids[:, None], slot_ids[None, :], 0), axis=1
    )
    row_ids = jnp.arange(block_rows, dtype=jnp.int32)
    out_rows = (dest_slot[:, None] * block_rows + row_ids[None, :]).reshape(row_count)
    offset = out_rows[:, None] - jnp.arange(row_count, dtype=jnp.int32)[None, :]
    mix = jnp.zeros((plane_count, row_count, row_count), jnp.float32)
    for tap in range(2 * reach + 1):
        mix = mix + jnp.where((offset == tap - reach)[None], y_own[tap][:, None, None], 0.0)
    by_source = jnp.einsum("pri,pix->prx", mix, zback, precision=lax.Precision.HIGHEST)
    back = taps_along(by_source, x_own, 2, True)
    piece_planes = plane_count // view_count
    logs = jnp.log(back).reshape(view_count, piece_planes, block_count, block_rows, lane_count)
    outgoing = logs.transpose(0, 2, 1, 3, 4).reshape(view_count * block_count, piece_planes, block_rows, lane_count)
    arrived_logs = lax.all_to_all(outgoing, ("view", "dom"), 0, 0, tiled=True)
    all_grid = src_map.reshape(view_count, block_count, block_count)
    all_dev = all_grid // block_count
    all_slot = all_grid % block_count
    slot_of = jnp.sum(jnp.where(all_dev == dom_index, all_slot, 0), axis=2)
    cam_of = jnp.sum(
        jnp.where(slot_of[:, :, None] == slot_ids[None, None, :], slot_ids[None, :, None], 0), axis=1
    )
    flat_index = (view_ids[:, None] * block_count + cam_of).reshape(-1)
    by_view = jnp.take(arrived_logs, flat_index, axis=0, mode="clip")
    by_view = by_view.reshape(view_count, block_count, piece_planes, block_rows, lane_count)
    log_total = by_view[0]
    for v in range(1, view_count):
        log_total = log_total + by_view[v]
    log_total = log_total.transpose(1, 0, 2, 3).reshape(piece_planes, row_count, lane_count)
    log_joined = lax.all_gather(log_total, "view", axis=0, tiled=True)
    return estimate * jnp.exp(log_joined / view_count)


def solution(mesh):
    in_specs = (
        P(("tile", "dom"), None, None),
        P("view", ("tile", "dom"), None, None),
        P("view", None, None, None),
        P(),
        P("view", None),
    )
    out_specs = P(("tile", "dom"), None, None)
    return jax.shard_map(body, mesh=mesh, in_specs=in_specs, out_specs=out_specs, check_vma=False)
```

```python
import jax
import jax.numpy as jnp
from jax import lax
from jax.sharding import PartitionSpec as P

RADIUS = 4


precise = lax.Precision.HIGHEST


def extended_2(shard, sides, width):
    for axis, dim in sides:
        size, length = (lax.axis_size(axis), shard.shape[dim])
        up = [(i, (i + 1) % size) for i in range(size - 1)]
        down = [(j, i) for i, j in up]
        last = lax.slice_in_dim(shard, length - width, length, axis=dim)
        initial = lax.slice_in_dim(shard, 0, width, axis=dim)
        before = lax.ppermute(last, axis, up)
        after = lax.ppermute(initial, axis, down)
        shard = jnp.concatenate([before, shard, after], axis=dim)
    return shard


def taps_along(field, taps, axis, flipped):
    tap_count = taps.shape[0]
    reach = (tap_count - 1) // 2
    length = field.shape[axis]
    widths = [(0, 0), (0, 0), (0, 0)]
    widths[axis] = (reach, reach)
    padded = jnp.pad(field, widths)
    total = jnp.zeros(field.shape, jnp.float32)
    for offset in range(tap_count):
        start = 2 * reach - offset if flipped else offset
        piece = lax.slice_in_dim(padded, start, start + length, axis=axis)
        total = total + taps[offset][:, None, None] * piece
    return total


def lateral_fwd(field, x_taps, y_taps):
    inner = taps_along(field, x_taps, 2, False)
    return taps_along(inner, y_taps, 1, False)


def body(estimate, observed, psf, src_map, depth_band):
    plane_count, row_count, lane_count = estimate.shape
    block_count = lax.axis_size("dom")
    block_rows = row_count // block_count
    dom_index = lax.axis_index("dom")
    view_index = lax.axis_index("view")
    view_count = lax.axis_size("view")
    plane_start = dom_index * plane_count
    slot_ids = jnp.arange(block_count, dtype=jnp.int32)
    view_ids = jnp.arange(view_count, dtype=jnp.int32)
    my_map = jnp.sum(jnp.where((view_ids == view_index)[:, None], src_map, 0), axis=0)
    grid_map = my_map.reshape(block_count, block_count)
    source_dev = grid_map // block_count
    source_slot = grid_map % block_count
    near_rows = jnp.stack(
        [
            jnp.concatenate([grid_map[:1], grid_map[:-1]], axis=0),
            grid_map,
            jnp.concatenate([grid_map[1:], grid_map[-1:]], axis=0),
        ]
    )
    near_slots = jnp.sum(
        jnp.where(near_rows // block_count == dom_index, near_rows % block_count, 0), axis=2
    )
    above, send_slot, below = near_slots[0], near_slots[1], near_slots[2]
    kernels = psf[0]
    band_all = depth_band[0]
    total_planes = band_all.shape[0]
    reach = (kernels.shape[2] - 1) // 2
    wide = 2 * reach
    last = block_count - 1
    wide_count = plane_count + 2 * wide
    chunk_plane = jnp.arange(wide_count, dtype=jnp.int32)
    in_top = chunk_plane < wide
    in_bottom = chunk_plane >= wide + plane_count
    source_plane = jnp.where(
        in_top, chunk_plane + plane_count - wide,
        jnp.where(in_bottom, chunk_plane - wide - plane_count, chunk_plane - wide),
    )
    source_block = jnp.where(
        in_top[:, None], above[None, :], jnp.where(in_bottom[:, None], below[None, :], send_slot[None, :])
    )
    send_index = (source_plane[None, :] * block_count + source_block.T).reshape(-1)
    flat_blocks = estimate.reshape(plane_count * block_count, block_rows, lane_count)
    outgoing = jnp.take(flat_blocks, send_index, axis=0, mode="clip")
    outgoing = outgoing.reshape(block_count * wide_count, block_rows, lane_count)
    arrived = lax.all_to_all(outgoing, "dom", split_axis=0, concat_axis=0, tiled=True)
    my_sources = lax.dynamic_index_in_dim(source_dev, dom_index, 0, keepdims=False)
    src_above = lax.dynamic_index_in_dim(source_dev, jnp.maximum(dom_index - 1, 0), 0, keepdims=False)
    src_below = lax.dynamic_index_in_dim(source_dev, jnp.minimum(dom_index + 1, last), 0, keepdims=False)
    from_block = jnp.where(
        in_top[:, None], src_above[None, :], jnp.where(in_bottom[:, None], src_below[None, :], my_sources[None, :])
    )
    recv_index = (from_block * wide_count + chunk_plane[:, None]).reshape(-1)
    camera_ext = jnp.take(arrived, recv_index, axis=0, mode="clip")
    camera_ext = camera_ext.reshape(wide_count, block_count, block_rows, lane_count)
    wide_planes = plane_start - wide + jnp.arange(wide_count, dtype=jnp.int32)
    wide_inside = (wide_planes >= 0) & (wide_planes < total_planes)
    camera_ext = camera_ext.reshape(wide_count, row_count, lane_count)
    band_pad = jnp.pad(band_all, wide, mode="edge")
    band_wide = lax.dynamic_slice_in_dim(band_pad, plane_start, wide_count)
    band_ids = jnp.arange(kernels.shape[0], dtype=jnp.int32)
    in_band = band_wide[None, :] == band_ids[:, None]
    tables = jnp.sum(jnp.where(in_band[:, None, None, :], kernels[:, :, :, None], 0.0), axis=0)
    x_wide = tables[2]
    y_wide = tables[1]
    lateral_ext = lateral_fwd(camera_ext, x_wide, y_wide)
    ext_count = plane_count + 2 * reach
    ext_planes = plane_start - reach + jnp.arange(ext_count, dtype=jnp.int32)
    ext_inside = (ext_planes >= 0) & (ext_planes < total_planes)
    taps_ext = tables[0][:, reach : reach + ext_count]
    blurred = jnp.zeros((ext_count, row_count, lane_count), jnp.float32)
    for j in range(2 * reach + 1):
        weight = jnp.where(wide_inside[j : j + ext_count], taps_ext[j], 0.0)
        blurred = blurred + weight[:, None, None] * lateral_ext[j : j + ext_count]
    observed_ext = extended_2(observed[0], (("dom", 0),), reach)
    ratio_ext = jnp.where(ext_inside[:, None, None], observed_ext / blurred, 0.0)
    x_own = tables[2][:, wide : wide + plane_count]
    y_own = tables[1][:, wide : wide + plane_count]
    zback = jnp.zeros((plane_count, row_count, lane_count), jnp.float32)
    for m in range(2 * reach + 1):
        zback = zback + taps_ext[2 * reach - m, m : m + plane_count][:, None, None] * ratio_ext[m : m + plane_count]
    dest_slot = jnp.sum(
        jnp.where(my_sources[None, :] == slot_ids[:, None], slot_ids[None, :], 0), axis=1
    )
    row_ids = jnp.arange(block_rows, dtype=jnp.int32)
    out_rows = (dest_slot[:, None] * block_rows + row_ids[None, :]).reshape(row_count)
    offset = out_rows[:, None] - jnp.arange(row_count, dtype=jnp.int32)[None, :]
    mix = jnp.zeros((plane_count, row_count, row_count), jnp.float32)
    for tap in range(2 * reach + 1):
        mix = mix + jnp.where((offset == tap - reach)[None], y_own[tap][:, None, None], 0.0)
    by_source = jnp.einsum("pri,pix->prx", mix, zback, precision=lax.Precision.HIGHEST)
    piece_planes = plane_count // view_count
    by_source = by_source.reshape(view_count, piece_planes, block_count, block_rows, lane_count)
    by_source = by_source.transpose(0, 2, 1, 3, 4)
    padded = jnp.pad(by_source, [(0, 0)] * 4 + [(reach, reach)])
    back = jnp.zeros(by_source.shape, jnp.float32)
    for tap in range(2 * reach + 1):
        weight = x_own[tap].reshape(view_count, 1, piece_planes, 1, 1)
        back = back + weight * padded[..., 2 * reach - tap : 2 * reach - tap + lane_count]
    outgoing = jnp.log(back).reshape(view_count * block_count, piece_planes, block_rows, lane_count)
    arrived_logs = lax.all_to_all(outgoing, ("view", "dom"), 0, 0, tiled=True)
    all_grid = src_map.reshape(view_count, block_count, block_count)
    all_dev = all_grid // block_count
    all_slot = all_grid % block_count
    slot_of = jnp.sum(jnp.where(all_dev == dom_index, all_slot, 0), axis=2)
    cam_of = jnp.sum(
        jnp.where(slot_of[:, :, None] == slot_ids[None, None, :], slot_ids[None, :, None], 0), axis=1
    )
    flat_index = (view_ids[:, None] * block_count + cam_of).reshape(-1)
    by_view = jnp.take(arrived_logs, flat_index, axis=0, mode="clip")
    by_view = by_view.reshape(view_count, block_count, piece_planes, block_rows, lane_count)
    log_total = by_view[0]
    for v in range(1, view_count):
        log_total = log_total + by_view[v]
    log_total = log_total.transpose(1, 0, 2, 3).reshape(piece_planes, row_count, lane_count)
    log_joined = lax.all_gather(log_total, "view", axis=0, tiled=True)
    return estimate * jnp.exp(log_joined / view_count)


def solution(mesh):
    in_specs = (
        P(("tile", "dom"), None, None),
        P("view", ("tile", "dom"), None, None),
        P("view", None, None, None),
        P(),
        P("view", None),
    )
    out_specs = P(("tile", "dom"), None, None)
    return jax.shard_map(body, mesh=mesh, in_specs=in_specs, out_specs=out_specs, check_vma=False)
```

```python
import jax
import jax.numpy as jnp
from jax import lax
from jax.sharding import PartitionSpec as P

RADIUS = 4


precise = lax.Precision.HIGHEST


def extended_2(shard, sides, width):
    for axis, dim in sides:
        size, length = (lax.axis_size(axis), shard.shape[dim])
        up = [(i, (i + 1) % size) for i in range(size - 1)]
        down = [(j, i) for i, j in up]
        last = lax.slice_in_dim(shard, length - width, length, axis=dim)
        initial = lax.slice_in_dim(shard, 0, width, axis=dim)
        before = lax.ppermute(last, axis, up)
        after = lax.ppermute(initial, axis, down)
        shard = jnp.concatenate([before, shard, after], axis=dim)
    return shard


def taps_along(field, taps, axis, flipped):
    tap_count = taps.shape[0]
    reach = (tap_count - 1) // 2
    length = field.shape[axis]
    widths = [(0, 0), (0, 0), (0, 0)]
    widths[axis] = (reach, reach)
    padded = jnp.pad(field, widths)
    total = jnp.zeros(field.shape, jnp.float32)
    for offset in range(tap_count):
        start = 2 * reach - offset if flipped else offset
        piece = lax.slice_in_dim(padded, start, start + length, axis=axis)
        total = total + taps[offset][:, None, None] * piece
    return total


def lateral_fwd(field, x_taps, y_taps):
    inner = taps_along(field, x_taps, 2, False)
    return taps_along(inner, y_taps, 1, False)


def body(estimate, observed, psf, src_map, depth_band):
    plane_count, row_count, lane_count = estimate.shape
    block_count = lax.axis_size("dom")
    block_rows = row_count // block_count
    dom_index = lax.axis_index("dom")
    view_index = lax.axis_index("view")
    view_count = lax.axis_size("view")
    plane_start = dom_index * plane_count
    slot_ids = jnp.arange(block_count, dtype=jnp.int32)
    view_ids = jnp.arange(view_count, dtype=jnp.int32)
    my_map = jnp.sum(jnp.where((view_ids == view_index)[:, None], src_map, 0), axis=0)
    grid_map = my_map.reshape(block_count, block_count)
    source_dev = grid_map // block_count
    source_slot = grid_map % block_count
    near_rows = jnp.stack(
        [
            jnp.concatenate([grid_map[:1], grid_map[:-1]], axis=0),
            grid_map,
            jnp.concatenate([grid_map[1:], grid_map[-1:]], axis=0),
        ]
    )
    near_slots = jnp.sum(
        jnp.where(near_rows // block_count == dom_index, near_rows % block_count, 0), axis=2
    )
    above, send_slot, below = near_slots[0], near_slots[1], near_slots[2]
    kernels = psf[0]
    band_all = depth_band[0]
    total_planes = band_all.shape[0]
    reach = (kernels.shape[2] - 1) // 2
    wide = 2 * reach
    last = block_count - 1
    wide_count = plane_count + 2 * wide
    chunk_plane = jnp.arange(wide_count, dtype=jnp.int32)
    in_top = chunk_plane < wide
    in_bottom = chunk_plane >= wide + plane_count
    source_plane = jnp.where(
        in_top, chunk_plane + plane_count - wide,
        jnp.where(in_bottom, chunk_plane - wide - plane_count, chunk_plane - wide),
    )
    source_block = jnp.where(
        in_top[:, None], above[None, :], jnp.where(in_bottom[:, None], below[None, :], send_slot[None, :])
    )
    send_index = (source_plane[None, :] * block_count + source_block.T).reshape(-1)
    flat_blocks = estimate.reshape(plane_count * block_count, block_rows, lane_count)
    outgoing = jnp.take(flat_blocks, send_index, axis=0, mode="clip")
    outgoing = outgoing.reshape(block_count * wide_count, block_rows, lane_count)
    arrived = lax.all_to_all(outgoing, "dom", split_axis=0, concat_axis=0, tiled=True)
    my_sources = lax.dynamic_index_in_dim(source_dev, dom_index, 0, keepdims=False)
    src_above = lax.dynamic_index_in_dim(source_dev, jnp.maximum(dom_index - 1, 0), 0, keepdims=False)
    src_below = lax.dynamic_index_in_dim(source_dev, jnp.minimum(dom_index + 1, last), 0, keepdims=False)
    from_block = jnp.where(
        in_top[:, None], src_above[None, :], jnp.where(in_bottom[:, None], src_below[None, :], my_sources[None, :])
    )
    recv_index = (from_block * wide_count + chunk_plane[:, None]).reshape(-1)
    camera_ext = jnp.take(arrived, recv_index, axis=0, mode="clip")
    camera_ext = camera_ext.reshape(wide_count, block_count, block_rows, lane_count)
    wide_planes = plane_start - wide + jnp.arange(wide_count, dtype=jnp.int32)
    wide_inside = (wide_planes >= 0) & (wide_planes < total_planes)
    camera_ext = camera_ext.reshape(wide_count, row_count, lane_count)
    band_pad = jnp.pad(band_all, wide, mode="edge")
    band_wide = lax.dynamic_slice_in_dim(band_pad, plane_start, wide_count)
    band_ids = jnp.arange(kernels.shape[0], dtype=jnp.int32)
    in_band = band_wide[None, :] == band_ids[:, None]
    tables = jnp.sum(jnp.where(in_band[:, None, None, :], kernels[:, :, :, None], 0.0), axis=0)
    x_wide = tables[2]
    y_wide = tables[1]
    lateral_ext = lateral_fwd(camera_ext, x_wide, y_wide)
    ext_count = plane_count + 2 * reach
    ext_planes = plane_start - reach + jnp.arange(ext_count, dtype=jnp.int32)
    ext_inside = (ext_planes >= 0) & (ext_planes < total_planes)
    taps_ext = tables[0][:, reach : reach + ext_count]
    blurred = jnp.zeros((ext_count, row_count, lane_count), jnp.float32)
    for j in range(2 * reach + 1):
        weight = jnp.where(wide_inside[j : j + ext_count], taps_ext[j], 0.0)
        blurred = blurred + weight[:, None, None] * lateral_ext[j : j + ext_count]
    observed_ext = extended_2(observed[0], (("dom", 0),), reach)
    ratio_ext = jnp.where(ext_inside[:, None, None], observed_ext / blurred, 0.0)
    x_own = tables[2][:, wide : wide + plane_count]
    y_own = tables[1][:, wide : wide + plane_count]
    zback = jnp.zeros((plane_count, row_count, lane_count), jnp.float32)
    for m in range(2 * reach + 1):
        zback = zback + taps_ext[2 * reach - m, m : m + plane_count][:, None, None] * ratio_ext[m : m + plane_count]
    dest_slot = jnp.sum(
        jnp.where(my_sources[None, :] == slot_ids[:, None], slot_ids[None, :], 0), axis=1
    )
    row_ids = jnp.arange(block_rows, dtype=jnp.int32)
    out_rows = (dest_slot[:, None] * block_rows + row_ids[None, :]).reshape(row_count)
    offset = out_rows[:, None] - jnp.arange(row_count, dtype=jnp.int32)[None, :]
    mix = jnp.zeros((plane_count, row_count, row_count), jnp.float32)
    for tap in range(2 * reach + 1):
        mix = mix + jnp.where((offset == tap - reach)[None], y_own[tap][:, None, None], 0.0)
    by_source = jnp.einsum("pri,pix->prx", mix, zback, precision=lax.Precision.HIGHEST)
    back = taps_along(by_source, x_own, 2, True)
    piece_planes = plane_count // view_count
    logs = jnp.log(back).reshape(view_count, piece_planes, block_count, block_rows, lane_count)
    outgoing = logs.transpose(0, 2, 1, 3, 4).reshape(view_count * block_count, piece_planes, block_rows, lane_count)
    arrived_logs = lax.all_to_all(outgoing, ("view", "dom"), 0, 0, tiled=True)
    all_grid = src_map.reshape(view_count, block_count, block_count)
    all_dev = all_grid // block_count
    all_slot = all_grid % block_count
    slot_of = jnp.sum(jnp.where(all_dev == dom_index, all_slot, 0), axis=2)
    cam_of = jnp.sum(
        jnp.where(slot_of[:, :, None] == slot_ids[None, None, :], slot_ids[None, :, None], 0), axis=1
    )
    flat_index = (view_ids[:, None] * block_count + cam_of).reshape(-1)
    by_view = jnp.take(arrived_logs, flat_index, axis=0, mode="clip")
    by_view = by_view.reshape(view_count, block_count, piece_planes, block_rows, lane_count)
    log_total = by_view[0]
    for v in range(1, view_count):
        log_total = log_total + by_view[v]
    log_total = log_total.transpose(1, 0, 2, 3).reshape(piece_planes, row_count, lane_count)
    scale_joined = lax.all_gather(jnp.exp(log_total / view_count), "view", axis=0, tiled=True)
    return estimate * scale_joined


def solution(mesh):
    in_specs = (
        P(("tile", "dom"), None, None),
        P("view", ("tile", "dom"), None, None),
        P("view", None, None, None),
        P(),
        P("view", None),
    )
    out_specs = P(("tile", "dom"), None, None)
    return jax.shard_map(body, mesh=mesh, in_specs=in_specs, out_specs=out_specs, check_vma=False)
```

```python
import jax
import jax.numpy as jnp
from jax import lax
from jax.sharding import PartitionSpec as P

RADIUS = 4


precise = lax.Precision.HIGHEST


def extended_2(shard, sides, width):
    for axis, dim in sides:
        size, length = (lax.axis_size(axis), shard.shape[dim])
        up = [(i, (i + 1) % size) for i in range(size - 1)]
        down = [(j, i) for i, j in up]
        last = lax.slice_in_dim(shard, length - width, length, axis=dim)
        initial = lax.slice_in_dim(shard, 0, width, axis=dim)
        before = lax.ppermute(last, axis, up)
        after = lax.ppermute(initial, axis, down)
        shard = jnp.concatenate([before, shard, after], axis=dim)
    return shard


def taps_along(field, taps, axis, flipped):
    tap_count = taps.shape[0]
    reach = (tap_count - 1) // 2
    length = field.shape[axis]
    widths = [(0, 0), (0, 0), (0, 0)]
    widths[axis] = (reach, reach)
    padded = jnp.pad(field, widths)
    total = jnp.zeros(field.shape, jnp.float32)
    for offset in range(tap_count):
        start = 2 * reach - offset if flipped else offset
        piece = lax.slice_in_dim(padded, start, start + length, axis=axis)
        total = total + taps[offset][:, None, None] * piece
    return total


def lateral_fwd(field, x_taps, y_taps):
    inner = taps_along(field, x_taps, 2, False)
    return taps_along(inner, y_taps, 1, False)


def body(estimate, observed, psf, src_map, depth_band):
    plane_count, row_count, lane_count = estimate.shape
    block_count = lax.axis_size("dom")
    block_rows = row_count // block_count
    dom_index = lax.axis_index("dom")
    view_index = lax.axis_index("view")
    view_count = lax.axis_size("view")
    plane_start = dom_index * plane_count
    slot_ids = jnp.arange(block_count, dtype=jnp.int32)
    view_ids = jnp.arange(view_count, dtype=jnp.int32)
    my_map = jnp.sum(jnp.where((view_ids == view_index)[:, None], src_map, 0), axis=0)
    grid_map = my_map.reshape(block_count, block_count)
    source_dev = grid_map // block_count
    source_slot = grid_map % block_count
    near_rows = jnp.stack(
        [
            jnp.concatenate([grid_map[:1], grid_map[:-1]], axis=0),
            grid_map,
            jnp.concatenate([grid_map[1:], grid_map[-1:]], axis=0),
        ]
    )
    near_slots = jnp.sum(
        jnp.where(near_rows // block_count == dom_index, near_rows % block_count, 0), axis=2
    )
    above, send_slot, below = near_slots[0], near_slots[1], near_slots[2]
    kernels = psf[0]
    band_all = depth_band[0]
    total_planes = band_all.shape[0]
    reach = (kernels.shape[2] - 1) // 2
    wide = 2 * reach
    last = block_count - 1
    wide_count = plane_count + 2 * wide
    chunk_plane = jnp.arange(wide_count, dtype=jnp.int32)
    in_top = chunk_plane < wide
    in_bottom = chunk_plane >= wide + plane_count
    source_plane = jnp.where(
        in_top, chunk_plane + plane_count - wide,
        jnp.where(in_bottom, chunk_plane - wide - plane_count, chunk_plane - wide),
    )
    source_block = jnp.where(
        in_top[:, None], above[None, :], jnp.where(in_bottom[:, None], below[None, :], send_slot[None, :])
    )
    main_index = (jnp.arange(plane_count, dtype=jnp.int32)[None, :] * block_count + send_slot[:, None]).reshape(-1)
    flat_blocks = estimate.reshape(plane_count * block_count, block_rows, lane_count)
    main = jnp.take(flat_blocks, main_index, axis=0, mode="clip")
    main = main.reshape(block_count, plane_count, block_rows, lane_count)
    prev_main = jnp.concatenate([main[:1], main[:-1]], axis=0)
    next_main = jnp.concatenate([main[1:], main[-1:]], axis=0)
    outgoing = jnp.concatenate([prev_main[:, plane_count - wide :], main, next_main[:, :wide]], axis=1)
    outgoing = outgoing.reshape(block_count * wide_count, block_rows, lane_count)
    arrived = lax.all_to_all(outgoing, "dom", split_axis=0, concat_axis=0, tiled=True)
    my_sources = lax.dynamic_index_in_dim(source_dev, dom_index, 0, keepdims=False)
    src_above = lax.dynamic_index_in_dim(source_dev, jnp.maximum(dom_index - 1, 0), 0, keepdims=False)
    src_below = lax.dynamic_index_in_dim(source_dev, jnp.minimum(dom_index + 1, last), 0, keepdims=False)
    from_block = jnp.where(
        in_top[:, None], src_above[None, :], jnp.where(in_bottom[:, None], src_below[None, :], my_sources[None, :])
    )
    recv_index = (from_block * wide_count + chunk_plane[:, None]).reshape(-1)
    camera_ext = jnp.take(arrived, recv_index, axis=0, mode="clip")
    camera_ext = camera_ext.reshape(wide_count, block_count, block_rows, lane_count)
    wide_planes = plane_start - wide + jnp.arange(wide_count, dtype=jnp.int32)
    wide_inside = (wide_planes >= 0) & (wide_planes < total_planes)
    camera_ext = camera_ext.reshape(wide_count, row_count, lane_count)
    band_pad = jnp.pad(band_all, wide, mode="edge")
    band_wide = lax.dynamic_slice_in_dim(band_pad, plane_start, wide_count)
    band_ids = jnp.arange(kernels.shape[0], dtype=jnp.int32)
    in_band = band_wide[None, :] == band_ids[:, None]
    tables = jnp.sum(jnp.where(in_band[:, None, None, :], kernels[:, :, :, None], 0.0), axis=0)
    x_wide = tables[2]
    y_wide = tables[1]
    lateral_ext = lateral_fwd(camera_ext, x_wide, y_wide)
    ext_count = plane_count + 2 * reach
    ext_planes = plane_start - reach + jnp.arange(ext_count, dtype=jnp.int32)
    ext_inside = (ext_planes >= 0) & (ext_planes < total_planes)
    taps_ext = tables[0][:, reach : reach + ext_count]
    blurred = jnp.zeros((ext_count, row_count, lane_count), jnp.float32)
    for j in range(2 * reach + 1):
        weight = jnp.where(wide_inside[j : j + ext_count], taps_ext[j], 0.0)
        blurred = blurred + weight[:, None, None] * lateral_ext[j : j + ext_count]
    observed_ext = extended_2(observed[0], (("dom", 0),), reach)
    ratio_ext = jnp.where(ext_inside[:, None, None], observed_ext / blurred, 0.0)
    x_own = tables[2][:, wide : wide + plane_count]
    y_own = tables[1][:, wide : wide + plane_count]
    zback = jnp.zeros((plane_count, row_count, lane_count), jnp.float32)
    for m in range(2 * reach + 1):
        zback = zback + taps_ext[2 * reach - m, m : m + plane_count][:, None, None] * ratio_ext[m : m + plane_count]
    dest_slot = jnp.sum(
        jnp.where(my_sources[None, :] == slot_ids[:, None], slot_ids[None, :], 0), axis=1
    )
    row_ids = jnp.arange(block_rows, dtype=jnp.int32)
    out_rows = (dest_slot[:, None] * block_rows + row_ids[None, :]).reshape(row_count)
    offset = out_rows[:, None] - jnp.arange(row_count, dtype=jnp.int32)[None, :]
    mix = jnp.zeros((plane_count, row_count, row_count), jnp.float32)
    for tap in range(2 * reach + 1):
        mix = mix + jnp.where((offset == tap - reach)[None], y_own[tap][:, None, None], 0.0)
    by_source = jnp.einsum("pri,pix->prx", mix, zback, precision=lax.Precision.HIGHEST)
    back = taps_along(by_source, x_own, 2, True)
    piece_planes = plane_count // view_count
    logs = jnp.log(back).reshape(view_count, piece_planes, block_count, block_rows, lane_count)
    outgoing = logs.transpose(0, 2, 1, 3, 4).reshape(view_count * block_count, piece_planes, block_rows, lane_count)
    arrived_logs = lax.all_to_all(outgoing, ("view", "dom"), 0, 0, tiled=True)
    all_grid = src_map.reshape(view_count, block_count, block_count)
    all_dev = all_grid // block_count
    all_slot = all_grid % block_count
    slot_of = jnp.sum(jnp.where(all_dev == dom_index, all_slot, 0), axis=2)
    cam_of = jnp.sum(
        jnp.where(slot_of[:, :, None] == slot_ids[None, None, :], slot_ids[None, :, None], 0), axis=1
    )
    flat_index = (view_ids[:, None] * block_count + cam_of).reshape(-1)
    by_view = jnp.take(arrived_logs, flat_index, axis=0, mode="clip")
    by_view = by_view.reshape(view_count, block_count, piece_planes, block_rows, lane_count)
    log_total = by_view[0]
    for v in range(1, view_count):
        log_total = log_total + by_view[v]
    log_total = log_total.transpose(1, 0, 2, 3).reshape(piece_planes, row_count, lane_count)
    log_joined = lax.all_gather(log_total, "view", axis=0, tiled=True)
    return estimate * jnp.exp(log_joined / view_count)


def solution(mesh):
    in_specs = (
        P(("tile", "dom"), None, None),
        P("view", ("tile", "dom"), None, None),
        P("view", None, None, None),
        P(),
        P("view", None),
    )
    out_specs = P(("tile", "dom"), None, None)
    return jax.shard_map(body, mesh=mesh, in_specs=in_specs, out_specs=out_specs, check_vma=False)
```

```python
import jax
import jax.numpy as jnp
from jax import lax
from jax.sharding import PartitionSpec as P

RADIUS = 4


precise = lax.Precision.HIGHEST


def extended_2(shard, sides, width):
    for axis, dim in sides:
        size, length = (lax.axis_size(axis), shard.shape[dim])
        up = [(i, (i + 1) % size) for i in range(size - 1)]
        down = [(j, i) for i, j in up]
        last = lax.slice_in_dim(shard, length - width, length, axis=dim)
        initial = lax.slice_in_dim(shard, 0, width, axis=dim)
        before = lax.ppermute(last, axis, up)
        after = lax.ppermute(initial, axis, down)
        shard = jnp.concatenate([before, shard, after], axis=dim)
    return shard


def taps_along(field, taps, axis, flipped):
    tap_count = taps.shape[0]
    reach = (tap_count - 1) // 2
    length = field.shape[axis]
    widths = [(0, 0), (0, 0), (0, 0)]
    widths[axis] = (reach, reach)
    padded = jnp.pad(field, widths)
    total = jnp.zeros(field.shape, jnp.float32)
    for offset in range(tap_count):
        start = 2 * reach - offset if flipped else offset
        piece = lax.slice_in_dim(padded, start, start + length, axis=axis)
        total = total + taps[offset][:, None, None] * piece
    return total


def lateral_fwd(field, x_taps, y_taps):
    inner = taps_along(field, x_taps, 2, False)
    return taps_along(inner, y_taps, 1, False)


def body(estimate, observed, psf, src_map, depth_band):
    plane_count, row_count, lane_count = estimate.shape
    block_count = lax.axis_size("dom")
    block_rows = row_count // block_count
    dom_index = lax.axis_index("dom")
    view_index = lax.axis_index("view")
    view_count = lax.axis_size("view")
    plane_start = dom_index * plane_count
    slot_ids = jnp.arange(block_count, dtype=jnp.int32)
    view_ids = jnp.arange(view_count, dtype=jnp.int32)
    my_map = jnp.sum(jnp.where((view_ids == view_index)[:, None], src_map, 0), axis=0)
    grid_map = my_map.reshape(block_count, block_count)
    source_dev = grid_map // block_count
    source_slot = grid_map % block_count
    near_rows = jnp.stack(
        [
            jnp.concatenate([grid_map[:1], grid_map[:-1]], axis=0),
            grid_map,
            jnp.concatenate([grid_map[1:], grid_map[-1:]], axis=0),
        ]
    )
    near_slots = jnp.sum(
        jnp.where(near_rows // block_count == dom_index, near_rows % block_count, 0), axis=2
    )
    above, send_slot, below = near_slots[0], near_slots[1], near_slots[2]
    kernels = psf[0]
    band_all = depth_band[0]
    total_planes = band_all.shape[0]
    reach = (kernels.shape[2] - 1) // 2
    wide = 2 * reach
    last = block_count - 1
    wide_count = plane_count + 2 * wide
    chunk_plane = jnp.arange(wide_count, dtype=jnp.int32)
    in_top = chunk_plane < wide
    in_bottom = chunk_plane >= wide + plane_count
    source_plane = jnp.where(
        in_top, chunk_plane + plane_count - wide,
        jnp.where(in_bottom, chunk_plane - wide - plane_count, chunk_plane - wide),
    )
    source_block = jnp.where(
        in_top[:, None], above[None, :], jnp.where(in_bottom[:, None], below[None, :], send_slot[None, :])
    )
    main_index = (jnp.arange(plane_count, dtype=jnp.int32)[None, :] * block_count + send_slot[:, None]).reshape(-1)
    flat_blocks = estimate.reshape(plane_count * block_count, block_rows, lane_count)
    main = jnp.take(flat_blocks, main_index, axis=0, mode="clip")
    main = main.reshape(block_count, plane_count, block_rows, lane_count)
    prev_main = jnp.concatenate([main[:1], main[:-1]], axis=0)
    next_main = jnp.concatenate([main[1:], main[-1:]], axis=0)
    outgoing = jnp.concatenate([prev_main[:, plane_count - wide :], main, next_main[:, :wide]], axis=1)
    send_planes = (jnp.arange(block_count, dtype=jnp.int32)[:, None] * plane_count
                   + jnp.arange(plane_count + 2 * wide, dtype=jnp.int32)[None, :])
    send_band = jnp.take(jnp.pad(band_all, wide, mode="edge"), send_planes, mode="clip")
    send_in_band = send_band[None] == jnp.arange(kernels.shape[0], dtype=jnp.int32)[:, None, None]
    send_x = jnp.sum(jnp.where(send_in_band[:, None], kernels[:, 2, :, None, None], 0.0), axis=0)
    lane_pad = jnp.pad(outgoing, [(0, 0), (0, 0), (0, 0), (reach, reach)])
    outgoing = jnp.zeros(outgoing.shape, jnp.float32)
    for tap in range(2 * reach + 1):
        outgoing = outgoing + send_x[tap][:, :, None, None] * lane_pad[..., tap : tap + lane_count]
    outgoing = outgoing.reshape(block_count * wide_count, block_rows, lane_count)
    arrived = lax.all_to_all(outgoing, "dom", split_axis=0, concat_axis=0, tiled=True)
    my_sources = lax.dynamic_index_in_dim(source_dev, dom_index, 0, keepdims=False)
    src_above = lax.dynamic_index_in_dim(source_dev, jnp.maximum(dom_index - 1, 0), 0, keepdims=False)
    src_below = lax.dynamic_index_in_dim(source_dev, jnp.minimum(dom_index + 1, last), 0, keepdims=False)
    from_block = jnp.where(
        in_top[:, None], src_above[None, :], jnp.where(in_bottom[:, None], src_below[None, :], my_sources[None, :])
    )
    recv_index = (from_block * wide_count + chunk_plane[:, None]).reshape(-1)
    camera_ext = jnp.take(arrived, recv_index, axis=0, mode="clip")
    camera_ext = camera_ext.reshape(wide_count, block_count, block_rows, lane_count)
    wide_planes = plane_start - wide + jnp.arange(wide_count, dtype=jnp.int32)
    wide_inside = (wide_planes >= 0) & (wide_planes < total_planes)
    camera_ext = camera_ext.reshape(wide_count, row_count, lane_count)
    band_pad = jnp.pad(band_all, wide, mode="edge")
    band_wide = lax.dynamic_slice_in_dim(band_pad, plane_start, wide_count)
    band_ids = jnp.arange(kernels.shape[0], dtype=jnp.int32)
    in_band = band_wide[None, :] == band_ids[:, None]
    tables = jnp.sum(jnp.where(in_band[:, None, None, :], kernels[:, :, :, None], 0.0), axis=0)
    x_wide = tables[2]
    y_wide = tables[1]
    lateral_ext = taps_along(camera_ext, y_wide, 1, False)
    ext_count = plane_count + 2 * reach
    ext_planes = plane_start - reach + jnp.arange(ext_count, dtype=jnp.int32)
    ext_inside = (ext_planes >= 0) & (ext_planes < total_planes)
    taps_ext = tables[0][:, reach : reach + ext_count]
    blurred = jnp.zeros((ext_count, row_count, lane_count), jnp.float32)
    for j in range(2 * reach + 1):
        weight = jnp.where(wide_inside[j : j + ext_count], taps_ext[j], 0.0)
        blurred = blurred + weight[:, None, None] * lateral_ext[j : j + ext_count]
    observed_ext = extended_2(observed[0], (("dom", 0),), reach)
    ratio_ext = jnp.where(ext_inside[:, None, None], observed_ext / blurred, 0.0)
    x_own = tables[2][:, wide : wide + plane_count]
    y_own = tables[1][:, wide : wide + plane_count]
    zback = jnp.zeros((plane_count, row_count, lane_count), jnp.float32)
    for m in range(2 * reach + 1):
        zback = zback + taps_ext[2 * reach - m, m : m + plane_count][:, None, None] * ratio_ext[m : m + plane_count]
    dest_slot = jnp.sum(
        jnp.where(my_sources[None, :] == slot_ids[:, None], slot_ids[None, :], 0), axis=1
    )
    row_ids = jnp.arange(block_rows, dtype=jnp.int32)
    out_rows = (dest_slot[:, None] * block_rows + row_ids[None, :]).reshape(row_count)
    offset = out_rows[:, None] - jnp.arange(row_count, dtype=jnp.int32)[None, :]
    mix = jnp.zeros((plane_count, row_count, row_count), jnp.float32)
    for tap in range(2 * reach + 1):
        mix = mix + jnp.where((offset == tap - reach)[None], y_own[tap][:, None, None], 0.0)
    by_source = jnp.einsum("pri,pix->prx", mix, zback, precision=lax.Precision.HIGHEST)
    back = taps_along(by_source, x_own, 2, True)
    piece_planes = plane_count // view_count
    logs = jnp.log(back).reshape(view_count, piece_planes, block_count, block_rows, lane_count)
    outgoing = logs.transpose(0, 2, 1, 3, 4).reshape(view_count * block_count, piece_planes, block_rows, lane_count)
    arrived_logs = lax.all_to_all(outgoing, ("view", "dom"), 0, 0, tiled=True)
    all_grid = src_map.reshape(view_count, block_count, block_count)
    all_dev = all_grid // block_count
    all_slot = all_grid % block_count
    slot_of = jnp.sum(jnp.where(all_dev == dom_index, all_slot, 0), axis=2)
    cam_of = jnp.sum(
        jnp.where(slot_of[:, :, None] == slot_ids[None, None, :], slot_ids[None, :, None], 0), axis=1
    )
    flat_index = (view_ids[:, None] * block_count + cam_of).reshape(-1)
    by_view = jnp.take(arrived_logs, flat_index, axis=0, mode="clip")
    by_view = by_view.reshape(view_count, block_count, piece_planes, block_rows, lane_count)
    log_total = by_view[0]
    for v in range(1, view_count):
        log_total = log_total + by_view[v]
    log_total = log_total.transpose(1, 0, 2, 3).reshape(piece_planes, row_count, lane_count)
    log_joined = lax.all_gather(log_total, "view", axis=0, tiled=True)
    return estimate * jnp.exp(log_joined / view_count)


def solution(mesh):
    in_specs = (
        P(("tile", "dom"), None, None),
        P("view", ("tile", "dom"), None, None),
        P("view", None, None, None),
        P(),
        P("view", None),
    )
    out_specs = P(("tile", "dom"), None, None)
    return jax.shard_map(body, mesh=mesh, in_specs=in_specs, out_specs=out_specs, check_vma=False)
```
